32 devices in a mesh: section: 2 (over core), fsdp: 2 (over y), expert: 8 (over z, x).
Axes of the slice: x: 2, y: 2, z: 4, core: 2. Of those that a mesh axis runs over, the one named last changes fastest.
Arguments:
- tokens: bfloat16 [2048, 2048], P(('fsdp', 'expert')), may hold values from -40 to 40
- norm_gain: float32 [2, 2048], P('section'), may hold values from 0.5 to 1.5
- router: bfloat16 [2, 2048, 32], P('section'), may hold values from -0.3125 to 0.3125
- w_gate: bfloat16 [2, 32, 2048, 768], P('section', 'expert', 'fsdp'), may hold values from -0.125 to 0.125
- w_up: bfloat16 [2, 32, 2048, 768], P('section', 'expert', 'fsdp'), may hold values from -0.125 to 0.125
- w_down: bfloat16 [2, 32, 768, 2048], P('section', 'expert', None, 'fsdp'), may hold values from -0.21875 to 0.21875
- routes: int32 [2, 2048, 6], P('section', ('fsdp', 'expert')), may hold values from 0 to 31, all different within a row; in each aligned block of 64 rows (0 to 63, 64 to 127, ..., all dimensions but the last counted through in order) at most 14 rows name the same one
Outputs:
- final_out: bfloat16 [2048, 2048], P(('fsdp', 'expert'), 'section')
- layer_stats: float32 [2], P('section')
The draws below stay inside these ranges and needn't reach their ends.
Inputs may be any that keep to these rules, and one draw needn't show every extreme that they name: `routes`: each row names 6 different experts; in every aligned block of 64 rows of one layer no expert is named by more than 14 rows, a bound that some block reaches.
All inputs are finite; a program needn't handle non-finite values.
Results may differ from the reference program's by a relative error of at most 0.0065.
Values may be sent and summed in bfloat16 or wider, within the bound.
No kernel may reach another device: no remote copies, remote signals or barrier semaphores. Data moves between devices by JAX's collectives and lax.ppermute only.
A program may use at most 192 MiB of HBM per device.

```python
import math
from functools import partial
import jax
import jax.numpy as jnp
import numpy as np
from jax import lax

D = 2048
H = 768
TOP = 6
EXPERTS = 32
MB_TOK = 64
CAP = 14
TOKENS = 2048
LAYERS = 2


def draw_tokens(key, part):
    key_base, key_rows, key_cols = jax.random.split(key, 3)
    position = jnp.arange(TOKENS, dtype=jnp.float32) / max(TOKENS - 1, 1)
    base_draw = jnp.clip(jax.random.normal(key_base, (TOKENS, D), jnp.float32), -4.0, 4.0)
    rising = 3.0 ** position
    row_scale = 0.05 * rising * 10.0 ** jax.random.uniform(key_rows, (TOKENS,), jnp.float32, 0.0, 1.0)
    col_scale = 10.0 ** jax.random.uniform(key_cols, (1, D), jnp.float32, -0.5, 0.5)
    return (base_draw * row_scale[:, None] * col_scale).astype(jnp.bfloat16)


def levels(rng, extent, shards, low, top_value):
    def one(axis_at, shards_of):
        draws = jax.random.uniform(jax.random.fold_in(jax.random.fold_in(rng, 6), axis_at), (shards_of,), jnp.float32, low / len(shards), top_value / len(shards))
        return jnp.repeat(jnp.exp(draws), extent[axis_at] // shards_of).reshape((-1,) + (1,) * (len(extent) - axis_at - 1))

    factor_of = one(*shards[0])
    for cut in shards[1:]:
        factor_of = factor_of * one(*cut)
    return factor_of


def assign_block(stream_key, own, number, rows, amount, top, most, lean):
    ranking = jax.random.permutation(stream_key, amount)
    packed, ordinary = portions_of(amount, rows * top, most, lean, True), portions_of(amount, rows * top, most, lean, False)
    places = jnp.arange(amount)

    def named(tallies, offset_by):
        used = int((tallies > 0).sum())
        fixed = max(1, used // 4)
        moved = fixed + (places - fixed + offset_by * (used - fixed)) % max(1, amount - fixed)
        return jnp.zeros((amount,), jnp.int32).at[ranking[jnp.where(places < fixed, places, moved)]].set(jnp.asarray(tallies, jnp.int32))

    tallies = jnp.where(number % 4 == 0, named(packed, number // 4), named(ordinary, number - number // 4 - 1))
    mixed = jax.random.permutation(jax.random.fold_in(own, 3), amount)
    source_of, sink = mixed[0:amount // 2 * 2:2], mixed[1:amount // 2 * 2:2]
    room = jnp.minimum(tallies[source_of] - 1, most - tallies[sink]) // 2
    room = jnp.where((source_of == ranking[0]) | (sink == ranking[0]) | (tallies[sink] == 0), 0, jnp.maximum(room, 0))
    moved = jax.random.randint(jax.random.fold_in(own, 4), (amount // 2,), 0, 1 << 20) % (room + 1)
    tallies = tallies.at[source_of].add(-moved).at[sink].add(moved)
    members = jnp.searchsorted(jnp.cumsum(tallies), jnp.arange(rows * top), side="right").astype(jnp.int32)
    listing = members.reshape(top, rows).T
    listing = listing[jax.random.permutation(jax.random.fold_in(own, 1), rows)]
    offset_by = jax.random.randint(jax.random.fold_in(own, 2), (rows, 1), 0, top)
    return jnp.take_along_axis(listing, (jnp.arange(top)[None, :] + offset_by) % top, axis=1)


def portions_of(amount, total, limit, lean, full):
    weights = [(1 << 20) // math.isqrt(rank ** lean) + 1 for rank in range(1, amount + 1)]
    largest = limit if full else min(limit, max(-(-total // amount), total * weights[0] // sum(weights)))
    least = 1 if total - largest >= amount - 1 else 0
    counts, rest = [largest] + [least] * (amount - 1), total - largest - least * (amount - 1)
    while rest > 0:
        free = [i for i in range(1, amount) if counts[i] < largest] or [i for i in range(1, amount) if counts[i] < limit]
        pool, left = sum([weights[i] for i in free]), rest
        for i in free:
            extra = min(limit - counts[i], max(1, left * weights[i] // pool), rest)
            counts[i] = counts[i] + extra
            rest = rest - extra
    return np.array(counts)


def centred(own_key, dims, scale, bound, shards=(), kind=jnp.bfloat16):
    drawn = jax.random.normal(own_key, dims, jnp.float32) * scale
    if len(shards) > 0:
        drawn = levels(own_key, dims, shards, -0.22, 0.18) * drawn
    return jnp.clip(drawn, min=-bound, max=bound).astype(kind)


def setup_inputs(seed: int = 0) -> dict:
    key_of = jax.random.split(jax.random.key(seed), 8)
    tokens = draw_tokens(jax.random.fold_in(key_of[7], 71), 0)
    norm_gain = jnp.clip(0.5 + 1.0 * jax.random.uniform(key_of[1], (LAYERS, D), jnp.float32) ** levels(key_of[1], (LAYERS, D), ((0, 2),), -0.2, 0.2), 0.5, 1.5)
    router = centred(key_of[2], (LAYERS, D, EXPERTS), (2.2 / D ** 0.5), 0.3125, ((0, 2),))
    w_gate = centred(key_of[3], (LAYERS, EXPERTS, D, H), D ** -0.5, 0.125, ((0, 2), (1, 8), (2, 2)))
    w_up = centred(key_of[4], (LAYERS, EXPERTS, D, H), D ** -0.5, 0.125, ((0, 2), (1, 8), (2, 2)))
    w_down = centred(key_of[5], (LAYERS, EXPERTS, H, D), H ** -0.5, 0.21875, ((0, 2), (1, 8), (3, 2)))
    routes_keys = jax.random.split(jax.random.fold_in(key_of[6], 1), LAYERS * TOKENS // MB_TOK)
    routes_turns = jax.random.permutation(jax.random.fold_in(key_of[6], 3), LAYERS * TOKENS // MB_TOK)
    routes = jax.vmap(lambda own, number: assign_block(jax.random.fold_in(key_of[6], 2), own, number, MB_TOK, EXPERTS, TOP, CAP, 0))(routes_keys, routes_turns).reshape((LAYERS, TOKENS, TOP))
    return {"tokens": tokens, "norm_gain": norm_gain, "router": router, "w_gate": w_gate, "w_up": w_up, "w_down": w_down, "routes": routes}


def rms_scaled(hidden_rows, gain_row):
    values = hidden_rows.astype(jnp.float32)
    scale = lax.rsqrt(lax.optimization_barrier(jnp.mean(values * values, axis=-1, keepdims=True)) + 1e-06)
    return (values * scale * gain_row.astype(jnp.float32)).astype(jnp.bfloat16)

def gate_weights(normed, router_weight, route_rows):
    logits = jnp.dot(normed, router_weight, preferred_element_type=jnp.float32)
    scores = jax.nn.sigmoid(logits)
    expert_ids = jnp.arange(router_weight.shape[1], dtype=jnp.int32)
    chosen_mask = (route_rows[:, :, None] == expert_ids[None, None, :]).astype(jnp.float32)
    chosen = lax.optimization_barrier(jnp.sum(scores[:, None, :] * chosen_mask, axis=2))
    return chosen / lax.optimization_barrier(jnp.sum(chosen, axis=1, keepdims=True))

def slot_positions(route_rows, experts_count, capacity):
    flat_routes = route_rows.reshape(-1)
    onehot = (flat_routes[:, None] == jnp.arange(experts_count, dtype=jnp.int32)[None, :]).astype(jnp.int32)
    before = jnp.cumsum(onehot, axis=0) - onehot
    slot_index = lax.optimization_barrier(jnp.sum(before * onehot, axis=1))
    return (flat_routes * capacity + slot_index).reshape(route_rows.shape).astype(jnp.int32)

def reference(tokens, norm_gain, router, w_gate, w_up, w_down, routes):
    block_count = TOKENS // MB_TOK
    group_size = math.gcd(block_count, 16)
    round_count = block_count // group_size
    slots_total = EXPERTS * CAP
    hidden = tokens
    layer_stats = []
    for layer_index in range(LAYERS):
        gate_wide = w_gate[layer_index].astype(jnp.float32)
        up_wide = w_up[layer_index].astype(jnp.float32)
        down_wide = w_down[layer_index].astype(jnp.float32)
        gain_row = norm_gain[layer_index]
        router_weight = router[layer_index]

        def run_group(pieces):
            row_block, route_rows = pieces
            normed = rms_scaled(row_block, gain_row)
            mix_weights = gate_weights(normed, router_weight, route_rows)
            route_blocks = route_rows.reshape(group_size, MB_TOK, TOP)
            positions = jax.vmap(partial(slot_positions, experts_count=EXPERTS, capacity=CAP))(route_blocks)
            block_ids = jnp.broadcast_to(jnp.arange(group_size, dtype=jnp.int32)[:, None, None], positions.shape)
            spread = jnp.broadcast_to(normed.reshape(group_size, MB_TOK, 1, D), (group_size, MB_TOK, TOP, D))
            buffer = jnp.zeros((group_size, slots_total, D), jnp.bfloat16).at[block_ids, positions].set(spread)
            slot_rows = buffer.reshape(group_size, EXPERTS, CAP, D).astype(jnp.float32)
            gate_part = jnp.einsum('gecd,edh->gech', slot_rows, gate_wide)
            up_part = jnp.einsum('gecd,edh->gech', slot_rows, up_wide)
            inner_act = (jax.nn.silu(gate_part) * up_part).astype(jnp.bfloat16)
            inner_act = lax.optimization_barrier(inner_act).astype(jnp.float32)
            produced = jnp.einsum('gech,ehd->gecd', inner_act, down_wide).astype(jnp.bfloat16)
            flat_out = produced.reshape(group_size, slots_total, D)
            picked = flat_out[block_ids, positions].reshape(group_size * MB_TOK, TOP, D)
            branch_sum = lax.optimization_barrier(jnp.sum(mix_weights[:, :, None] * picked.astype(jnp.float32), axis=1))
            return (row_block.astype(jnp.float32) + branch_sum).astype(jnp.bfloat16)
        hidden = lax.map(run_group, (hidden.reshape(round_count, group_size * MB_TOK, D), routes[layer_index].reshape(round_count, group_size * MB_TOK, TOP)))
        hidden = hidden.reshape(TOKENS, D)
        values = hidden.astype(jnp.float32)
        layer_stats.append(jnp.sqrt(jnp.sum(values * values) / (TOKENS * D)))
    return (hidden, jnp.stack(layer_stats))
```

```python
import jax
import jax.numpy as jnp
from jax import lax
from jax.sharding import PartitionSpec as P

TOP = 6
BLOCK = 64


epsilon = 1e-06


def other_section(value):
    return lax.ppermute(value, "section", [(0, 1), (1, 0)])


def rms_scaled(hidden_rows, gain_row):
    values = hidden_rows.astype(jnp.float32)
    scale = lax.rsqrt(jnp.mean(values * values, axis=-1, keepdims=True) + epsilon)
    return (values * scale * gain_row).astype(jnp.bfloat16)


def gate_weights(normed, router_weight, route_rows):
    logits = jnp.dot(normed, router_weight, preferred_element_type=jnp.float32)
    scores = jax.nn.sigmoid(logits)
    expert_ids = jnp.arange(router_weight.shape[1], dtype=jnp.int32)
    chosen_mask = (route_rows[:, :, None] == expert_ids[None, None, :]).astype(jnp.float32)
    chosen = jnp.sum(scores[:, None, :] * chosen_mask, axis=2)
    return chosen / jnp.sum(chosen, axis=1, keepdims=True)


def slot_positions(route_rows, experts_count, capacity):
    flat_routes = route_rows.reshape(-1)
    onehot = (flat_routes[:, None] == jnp.arange(experts_count, dtype=jnp.int32)[None, :]).astype(
        jnp.int32
    )
    before = jnp.cumsum(onehot, axis=0) - onehot
    slot_index = jnp.sum(before * onehot, axis=1)
    return (flat_routes * capacity + slot_index).reshape(route_rows.shape)


def expert_layer(entering, route_rows, gain_row, router_weight, weights, capacity):
    gate_w, up_w, down_w = weights
    width = entering.shape[1]
    experts_count = router_weight.shape[1]
    local_experts, chunk, hidden_units = gate_w.shape
    fsdp_count = lax.axis_size("fsdp")
    expert_devices = lax.axis_size("expert")
    peers = fsdp_count * expert_devices
    normed = rms_scaled(entering, gain_row)
    mix_weights = gate_weights(normed, router_weight, route_rows)
    positions = slot_positions(route_rows, experts_count, capacity)
    slot_ids = jnp.arange(experts_count * capacity, dtype=jnp.int32)
    placing = jnp.any(positions[None, :, :] == slot_ids[:, None, None], axis=2).astype(jnp.bfloat16)
    buffer = jnp.dot(placing, normed, preferred_element_type=jnp.float32).astype(jnp.bfloat16)
    outgoing = (
        buffer.reshape(expert_devices, local_experts * capacity, fsdp_count, chunk)
        .transpose(2, 0, 1, 3)
        .reshape(peers, local_experts * capacity, chunk)
    )
    arrived = lax.all_to_all(outgoing, ("fsdp", "expert"), 0, 0, tiled=True)
    arrived = arrived.reshape(peers, local_experts, capacity, chunk)
    gate_part = jnp.einsum("sjcd,jdh->sjch", arrived, gate_w, preferred_element_type=jnp.float32)
    up_part = jnp.einsum("sjcd,jdh->sjch", arrived, up_w, preferred_element_type=jnp.float32)
    both = jnp.concatenate([gate_part, up_part], axis=-1)
    summed = lax.psum_scatter(both, "fsdp", scatter_dimension=0, tiled=True)
    gate_sum = summed[..., :hidden_units]
    up_sum = summed[..., hidden_units:]
    inner_act = (jax.nn.silu(gate_sum) * up_sum).astype(jnp.bfloat16)
    inner_all = lax.all_gather(inner_act, "fsdp", axis=0, tiled=True)
    produced = jnp.einsum(
        "sjch,jhd->sjcd", inner_all, down_w, preferred_element_type=jnp.float32
    ).astype(jnp.bfloat16)
    returned = lax.all_to_all(
        produced.reshape(peers, local_experts * capacity, chunk),
        ("fsdp", "expert"),
        0,
        0,
        tiled=True,
    )
    flat_out = (
        returned.reshape(fsdp_count, expert_devices, local_experts * capacity, chunk)
        .transpose(1, 2, 0, 3)
        .reshape(experts_count * capacity, width)
    )
    picked = jnp.take(flat_out, positions, axis=0)
    branch_sum = jnp.sum(mix_weights[:, :, None] * picked.astype(jnp.float32), axis=1)
    return (entering.astype(jnp.float32) + branch_sum).astype(jnp.bfloat16)


def body(tokens, norm_gain, router, w_gate, w_up, w_down, routes):
    section_index = lax.axis_index("section")
    sections = lax.axis_size("section")
    token_rows, width = tokens.shape
    piece = token_rows // sections
    experts_count = router.shape[2]
    block_capacity = (7 * BLOCK * TOP + 6 * experts_count - 1) // (6 * experts_count)
    capacity = block_capacity * (piece // BLOCK)
    own_weights = (w_gate[0], w_up[0], w_down[0])
    other_weights = tuple(other_section(w) for w in own_weights)
    own_small = (norm_gain[0], router[0], routes[0])
    other_small = tuple(other_section(v) for v in own_small)
    hidden = lax.dynamic_slice_in_dim(tokens, section_index * piece, piece, 0)
    squares = []
    for layer in range(sections):
        mine = section_index == layer
        gain_row, router_weight, route_all = [
            jnp.where(mine, a, b) for a, b in zip(own_small, other_small)
        ]
        weights = tuple(jnp.where(mine, a, b) for a, b in zip(own_weights, other_weights))
        route_rows = lax.dynamic_slice_in_dim(route_all, section_index * piece, piece, 0)
        hidden = expert_layer(hidden, route_rows, gain_row, router_weight, weights, capacity)
        values = hidden.astype(jnp.float32)
        squares.append(jnp.sum(values * values))
    totals = lax.psum(jnp.stack(squares), ("section", "fsdp", "expert"))
    token_total = token_rows * lax.axis_size("fsdp") * lax.axis_size("expert")
    stats = jnp.sqrt(totals / (token_total * width))
    layer_stats = lax.dynamic_slice_in_dim(stats, section_index, 1, 0)
    half_width = width // 2
    keep = lax.dynamic_slice_in_dim(hidden, section_index * half_width, half_width, 1)
    send = lax.dynamic_slice_in_dim(hidden, (1 - section_index) * half_width, half_width, 1)
    arrived = other_section(send)
    final_out = jnp.where(
        section_index == 0,
        jnp.concatenate([keep, arrived], axis=0),
        jnp.concatenate([arrived, keep], axis=0),
    )
    return (final_out, layer_stats)


def solution(mesh):
    in_specs = (
        P(("fsdp", "expert"), None),
        P("section", None),
        P("section", None, None),
        P("section", "expert", "fsdp", None),
        P("section", "expert", "fsdp", None),
        P("section", "expert", None, "fsdp"),
        P("section", ("fsdp", "expert"), None),
    )
    out_specs = (P(("fsdp", "expert"), "section"), P("section"))
    return jax.shard_map(body, mesh=mesh, in_specs=in_specs, out_specs=out_specs, check_vma=False)
```

```python
import jax
import jax.numpy as jnp
from jax import lax
from jax.sharding import PartitionSpec as P

TOP = 6
BLOCK = 64


epsilon = 1e-06


def other_section(value):
    return lax.ppermute(value, "section", [(0, 1), (1, 0)])


def ring_pairs(count, shift):
    return [(source, (source + shift) % count) for source in range(count)]


def rms_scaled(hidden_rows, gain_row):
    values = hidden_rows.astype(jnp.float32)
    scale = lax.rsqrt(jnp.mean(values * values, axis=-1, keepdims=True) + epsilon)
    return (values * scale * gain_row).astype(jnp.bfloat16)


def gate_weights(normed, router_weight, route_rows):
    logits = jnp.dot(normed, router_weight, preferred_element_type=jnp.float32)
    scores = jax.nn.sigmoid(logits)
    expert_ids = jnp.arange(router_weight.shape[1], dtype=jnp.int32)
    chosen_mask = (route_rows[:, :, None] == expert_ids[None, None, :]).astype(jnp.float32)
    chosen = jnp.sum(scores[:, None, :] * chosen_mask, axis=2)
    return chosen / jnp.sum(chosen, axis=1, keepdims=True)


def slot_positions(route_rows, experts_count, capacity):
    flat_routes = route_rows.reshape(-1)
    onehot = (flat_routes[:, None] == jnp.arange(experts_count, dtype=jnp.int32)[None, :]).astype(
        jnp.int32
    )
    before = jnp.cumsum(onehot, axis=0) - onehot
    slot_index = jnp.sum(before * onehot, axis=1)
    return (flat_routes * capacity + slot_index).reshape(route_rows.shape)


def expert_layer(entering, route_rows, gain_row, router_weight, weights, capacity):
    gate_w, up_w, down_w = weights
    width = entering.shape[1]
    experts_count = router_weight.shape[1]
    local_experts, chunk, hidden_units = gate_w.shape
    fsdp_count = lax.axis_size("fsdp")
    expert_devices = lax.axis_size("expert")
    peers = fsdp_count * expert_devices
    normed = rms_scaled(entering, gain_row)
    mix_weights = gate_weights(normed, router_weight, route_rows)
    positions = slot_positions(route_rows, experts_count, capacity)
    slot_ids = jnp.arange(experts_count * capacity, dtype=jnp.int32)
    placing = jnp.any(positions[None, :, :] == slot_ids[:, None, None], axis=2).astype(jnp.bfloat16)
    buffer = jnp.dot(placing, normed, preferred_element_type=jnp.float32).astype(jnp.bfloat16)
    outgoing = (
        buffer.reshape(expert_devices, local_experts * capacity, fsdp_count, chunk)
        .transpose(2, 0, 1, 3)
        .reshape(peers, local_experts * capacity, chunk)
    )
    arrived = lax.all_to_all(outgoing, ("fsdp", "expert"), 0, 0, tiled=True)
    arrived = arrived.reshape(peers, local_experts, capacity, chunk)
    fsdp_index = lax.axis_index("fsdp")
    gate_part = jnp.einsum("sjcd,jdh->sjch", arrived, gate_w, preferred_element_type=jnp.float32)
    up_part = jnp.einsum("sjcd,jdh->sjch", arrived, up_w, preferred_element_type=jnp.float32)
    block_shape = (fsdp_count, expert_devices, local_experts, capacity, hidden_units)
    gate_blocks = gate_part.reshape(block_shape)
    up_blocks = up_part.reshape(block_shape)
    gate_sum = lax.dynamic_index_in_dim(gate_blocks, fsdp_index, 0, keepdims=False)
    up_sum = lax.dynamic_index_in_dim(up_blocks, fsdp_index, 0, keepdims=False)
    for shift in range(1, fsdp_count):
        target = (fsdp_index + shift) % fsdp_count
        outgoing_pair = jnp.stack(
            [
                lax.dynamic_index_in_dim(gate_blocks, target, 0, keepdims=False),
                lax.dynamic_index_in_dim(up_blocks, target, 0, keepdims=False),
            ]
        ).astype(jnp.bfloat16)
        got = lax.ppermute(outgoing_pair, "fsdp", ring_pairs(fsdp_count, shift))
        gate_sum = gate_sum + got[0].astype(jnp.float32)
        up_sum = up_sum + got[1].astype(jnp.float32)
    inner_act = (jax.nn.silu(gate_sum) * up_sum).astype(jnp.bfloat16)
    inner_pieces = [inner_act]
    for shift in range(1, fsdp_count):
        inner_pieces.append(lax.ppermute(inner_act, "fsdp", ring_pairs(fsdp_count, shift)))
    order = (fsdp_index - jnp.arange(fsdp_count, dtype=jnp.int32)) % fsdp_count
    inner_all = jnp.take(jnp.stack(inner_pieces), order, axis=0).reshape(
        peers, local_experts, capacity, hidden_units
    )
    produced = jnp.einsum(
        "sjch,jhd->sjcd", inner_all, down_w, preferred_element_type=jnp.float32
    ).astype(jnp.bfloat16)
    returned = lax.all_to_all(
        produced.reshape(peers, local_experts * capacity, chunk),
        ("fsdp", "expert"),
        0,
        0,
        tiled=True,
    )
    flat_out = (
        returned.reshape(fsdp_count, expert_devices, local_experts * capacity, chunk)
        .transpose(1, 2, 0, 3)
        .reshape(experts_count * capacity, width)
    )
    picked = jnp.take(flat_out, positions, axis=0)
    branch_sum = jnp.sum(mix_weights[:, :, None] * picked.astype(jnp.float32), axis=1)
    return (entering.astype(jnp.float32) + branch_sum).astype(jnp.bfloat16)


def body(tokens, norm_gain, router, w_gate, w_up, w_down, routes):
    section_index = lax.axis_index("section")
    sections = lax.axis_size("section")
    token_rows, width = tokens.shape
    piece = token_rows // sections
    experts_count = router.shape[2]
    block_capacity = (7 * BLOCK * TOP + 6 * experts_count - 1) // (6 * experts_count)
    capacity = block_capacity * (piece // BLOCK)
    own_weights = (w_gate[0], w_up[0], w_down[0])
    other_weights = tuple(other_section(w) for w in own_weights)
    own_small = (norm_gain[0], router[0], routes[0])
    other_small = tuple(other_section(v) for v in own_small)
    hidden = lax.dynamic_slice_in_dim(tokens, section_index * piece, piece, 0)
    squares = []
    for layer in range(sections):
        mine = section_index == layer
        gain_row, router_weight, route_all = [
            jnp.where(mine, a, b) for a, b in zip(own_small, other_small)
        ]
        weights = tuple(jnp.where(mine, a, b) for a, b in zip(own_weights, other_weights))
        route_rows = lax.dynamic_slice_in_dim(route_all, section_index * piece, piece, 0)
        hidden = expert_layer(hidden, route_rows, gain_row, router_weight, weights, capacity)
        values = hidden.astype(jnp.float32)
        squares.append(jnp.sum(values * values))
    everyone = ("section", "fsdp", "expert")
    device_count = sections * lax.axis_size("fsdp") * lax.axis_size("expert")
    square_rows = jnp.broadcast_to(jnp.stack(squares)[None, :], (device_count, sections))
    totals = jnp.sum(lax.all_to_all(square_rows, everyone, 0, 0, tiled=True), axis=0)
    token_total = token_rows * lax.axis_size("fsdp") * lax.axis_size("expert")
    stats = jnp.sqrt(totals / (token_total * width))
    layer_stats = lax.dynamic_slice_in_dim(stats, section_index, 1, 0)
    half_width = width // 2
    keep = lax.dynamic_slice_in_dim(hidden, section_index * half_width, half_width, 1)
    send = lax.dynamic_slice_in_dim(hidden, (1 - section_index) * half_width, half_width, 1)
    arrived = other_section(send)
    final_out = jnp.where(
        section_index == 0,
        jnp.concatenate([keep, arrived], axis=0),
        jnp.concatenate([arrived, keep], axis=0),
    )
    return (final_out, layer_stats)


def solution(mesh):
    in_specs = (
        P(("fsdp", "expert"), None),
        P("section", None),
        P("section", None, None),
        P("section", "expert", "fsdp", None),
        P("section", "expert", "fsdp", None),
        P("section", "expert", None, "fsdp"),
        P("section", ("fsdp", "expert"), None),
    )
    out_specs = (P(("fsdp", "expert"), "section"), P("section"))
    return jax.shard_map(body, mesh=mesh, in_specs=in_specs, out_specs=out_specs, check_vma=False)
```

```python
import jax
import jax.numpy as jnp
from jax import lax
from jax.sharding import PartitionSpec as P

TOP = 6
BLOCK = 64


epsilon = 1e-06


def other_section(value):
    return lax.ppermute(value, "section", [(0, 1), (1, 0)])


def ring_pairs(count, shift):
    return [(source, (source + shift) % count) for source in range(count)]


def rms_scaled(hidden_rows, gain_row):
    values = hidden_rows.astype(jnp.float32)
    scale = lax.rsqrt(jnp.mean(values * values, axis=-1, keepdims=True) + epsilon)
    return (values * scale * gain_row).astype(jnp.bfloat16)


def gate_weights(normed, router_weight, route_rows):
    logits = jnp.dot(normed, router_weight, preferred_element_type=jnp.float32)
    scores = jax.nn.sigmoid(logits)
    expert_ids = jnp.arange(router_weight.shape[1], dtype=jnp.int32)
    chosen_mask = (route_rows[:, :, None] == expert_ids[None, None, :]).astype(jnp.float32)
    chosen = jnp.sum(scores[:, None, :] * chosen_mask, axis=2)
    return chosen / jnp.sum(chosen, axis=1, keepdims=True)


def slot_positions(route_rows, experts_count, capacity):
    flat_routes = route_rows.reshape(-1)
    onehot = (flat_routes[:, None] == jnp.arange(experts_count, dtype=jnp.int32)[None, :]).astype(
        jnp.int32
    )
    before = jnp.cumsum(onehot, axis=0) - onehot
    slot_index = jnp.sum(before * onehot, axis=1)
    return (flat_routes * capacity + slot_index).reshape(route_rows.shape)


def expert_layer(entering, route_rows, gain_row, router_weight, weights, capacity):
    gate_w, up_w, down_w = weights
    width = entering.shape[1]
    experts_count = router_weight.shape[1]
    local_experts, chunk, hidden_units = gate_w.shape
    fsdp_count = lax.axis_size("fsdp")
    expert_devices = lax.axis_size("expert")
    peers = fsdp_count * expert_devices
    normed = rms_scaled(entering, gain_row)
    mix_weights = gate_weights(normed, router_weight, route_rows)
    positions = slot_positions(route_rows, experts_count, capacity)
    slot_ids = jnp.arange(experts_count * capacity, dtype=jnp.int32)
    hits = positions[:, :, None] == slot_ids[None, None, :]
    placing = jnp.any(hits, axis=1).astype(jnp.bfloat16)
    buffer = jnp.einsum(
        "rs,rfd->fsd",
        placing,
        normed.reshape(normed.shape[0], fsdp_count, chunk),
        preferred_element_type=jnp.float32,
    ).astype(jnp.bfloat16)
    outgoing = buffer.reshape(peers, local_experts * capacity, chunk)
    arrived = lax.all_to_all(outgoing, ("fsdp", "expert"), 0, 0, tiled=True)
    arrived = arrived.reshape(peers, local_experts, capacity, chunk)
    fsdp_index = lax.axis_index("fsdp")
    gate_part = jnp.einsum("sjcd,jdh->sjch", arrived, gate_w, preferred_element_type=jnp.float32)
    up_part = jnp.einsum("sjcd,jdh->sjch", arrived, up_w, preferred_element_type=jnp.float32)
    block_shape = (fsdp_count, expert_devices, local_experts, capacity, hidden_units)
    gate_blocks = gate_part.reshape(block_shape)
    up_blocks = up_part.reshape(block_shape)
    gate_sum = lax.dynamic_index_in_dim(gate_blocks, fsdp_index, 0, keepdims=False)
    up_sum = lax.dynamic_index_in_dim(up_blocks, fsdp_index, 0, keepdims=False)
    for shift in range(1, fsdp_count):
        target = (fsdp_index + shift) % fsdp_count
        outgoing_pair = jnp.stack(
            [
                lax.dynamic_index_in_dim(gate_blocks, target, 0, keepdims=False),
                lax.dynamic_index_in_dim(up_blocks, target, 0, keepdims=False),
            ]
        ).astype(jnp.bfloat16)
        got = lax.ppermute(outgoing_pair, "fsdp", ring_pairs(fsdp_count, shift))
        gate_sum = gate_sum + got[0].astype(jnp.float32)
        up_sum = up_sum + got[1].astype(jnp.float32)
    inner_act = (jax.nn.silu(gate_sum) * up_sum).astype(jnp.bfloat16)
    inner_pieces = [inner_act]
    for shift in range(1, fsdp_count):
        inner_pieces.append(lax.ppermute(inner_act, "fsdp", ring_pairs(fsdp_count, shift)))
    order = (fsdp_index - jnp.arange(fsdp_count, dtype=jnp.int32)) % fsdp_count
    inner_all = jnp.take(jnp.stack(inner_pieces), order, axis=0).reshape(
        peers, local_experts, capacity, hidden_units
    )
    produced = jnp.einsum(
        "sjch,jhd->sjcd", inner_all, down_w, preferred_element_type=jnp.float32
    ).astype(jnp.bfloat16)
    returned = lax.all_to_all(
        produced.reshape(peers, local_experts * capacity, chunk),
        ("fsdp", "expert"),
        0,
        0,
        tiled=True,
    )
    combining = jnp.sum(jnp.where(hits, mix_weights[:, :, None], 0.0), axis=1)
    branch_sum = jnp.einsum(
        "rs,fsd->rfd",
        combining,
        returned.reshape(fsdp_count, experts_count * capacity, chunk).astype(jnp.float32),
        precision=lax.Precision.HIGHEST,
        preferred_element_type=jnp.float32,
    ).reshape(normed.shape[0], width)
    return (entering.astype(jnp.float32) + branch_sum).astype(jnp.bfloat16)


def body(tokens, norm_gain, router, w_gate, w_up, w_down, routes):
    section_index = lax.axis_index("section")
    sections = lax.axis_size("section")
    token_rows, width = tokens.shape
    piece = token_rows // sections
    experts_count = router.shape[2]
    block_capacity = (7 * BLOCK * TOP + 6 * experts_count - 1) // (6 * experts_count)
    capacity = block_capacity * (piece // BLOCK)
    own_weights = (w_gate[0], w_up[0], w_down[0])
    other_weights = tuple(other_section(w) for w in own_weights)
    own_small = (norm_gain[0], router[0], routes[0])
    other_small = tuple(other_section(v) for v in own_small)
    hidden = lax.dynamic_slice_in_dim(tokens, section_index * piece, piece, 0)
    squares = []
    for layer in range(sections):
        mine = section_index == layer
        gain_row, router_weight, route_all = [
            jnp.where(mine, a, b) for a, b in zip(own_small, other_small)
        ]
        weights = tuple(jnp.where(mine, a, b) for a, b in zip(own_weights, other_weights))
        route_rows = lax.dynamic_slice_in_dim(route_all, section_index * piece, piece, 0)
        hidden = expert_layer(hidden, route_rows, gain_row, router_weight, weights, capacity)
        values = hidden.astype(jnp.float32)
        squares.append(jnp.sum(values * values))
    everyone = ("section", "fsdp", "expert")
    device_count = sections * lax.axis_size("fsdp") * lax.axis_size("expert")
    square_rows = jnp.broadcast_to(jnp.stack(squares)[None, :], (device_count, sections))
    totals = jnp.sum(lax.all_to_all(square_rows, everyone, 0, 0, tiled=True), axis=0)
    token_total = token_rows * lax.axis_size("fsdp") * lax.axis_size("expert")
    stats = jnp.sqrt(totals / (token_total * width))
    layer_stats = lax.dynamic_slice_in_dim(stats, section_index, 1, 0)
    half_width = width // 2
    keep = lax.dynamic_slice_in_dim(hidden, section_index * half_width, half_width, 1)
    send = lax.dynamic_slice_in_dim(hidden, (1 - section_index) * half_width, half_width, 1)
    arrived = other_section(send)
    final_out = jnp.where(
        section_index == 0,
        jnp.concatenate([keep, arrived], axis=0),
        jnp.concatenate([arrived, keep], axis=0),
    )
    return (final_out, layer_stats)


def solution(mesh):
    in_specs = (
        P(("fsdp", "expert"), None),
        P("section", None),
        P("section", None, None),
        P("section", "expert", "fsdp", None),
        P("section", "expert", "fsdp", None),
        P("section", "expert", None, "fsdp"),
        P("section", ("fsdp", "expert"), None),
    )
    out_specs = (P(("fsdp", "expert"), "section"), P("section"))
    return jax.shard_map(body, mesh=mesh, in_specs=in_specs, out_specs=out_specs, check_vma=False)
```

```python
import jax
import jax.numpy as jnp
from jax import lax
from jax.sharding import PartitionSpec as P

TOP = 6
BLOCK = 64
GROUPS = 2


epsilon = 1e-06


def other_section(value):
    return lax.ppermute(value, "section", [(0, 1), (1, 0)])


def ring_pairs(count, shift):
    return [(source, (source + shift) % count) for source in range(count)]


def rms_scaled(hidden_rows, gain_row):
    values = hidden_rows.astype(jnp.float32)
    scale = lax.rsqrt(jnp.mean(values * values, axis=-1, keepdims=True) + epsilon)
    return (values * scale * gain_row).astype(jnp.bfloat16)


def gate_weights(normed, router_weight, route_rows):
    logits = jnp.dot(normed, router_weight, preferred_element_type=jnp.float32)
    scores = jax.nn.sigmoid(logits)
    expert_ids = jnp.arange(router_weight.shape[1], dtype=jnp.int32)
    chosen_mask = (route_rows[:, :, None] == expert_ids[None, None, :]).astype(jnp.float32)
    chosen = jnp.sum(scores[:, None, :] * chosen_mask, axis=2)
    return chosen / jnp.sum(chosen, axis=1, keepdims=True)


def slot_positions(route_rows, experts_count, capacity):
    flat_routes = route_rows.reshape(-1)
    onehot = (flat_routes[:, None] == jnp.arange(experts_count, dtype=jnp.int32)[None, :]).astype(
        jnp.int32
    )
    before = jnp.cumsum(onehot, axis=0) - onehot
    slot_index = jnp.sum(before * onehot, axis=1)
    return (flat_routes * capacity + slot_index).reshape(route_rows.shape)


def expert_layer(entering, route_rows, gain_row, router_weight, weights, capacity):
    gate_w, up_w, down_w = weights
    width = entering.shape[1]
    experts_count = router_weight.shape[1]
    local_experts, chunk, hidden_units = gate_w.shape
    fsdp_count = lax.axis_size("fsdp")
    expert_devices = lax.axis_size("expert")
    peers = fsdp_count * expert_devices
    normed = rms_scaled(entering, gain_row)
    mix_weights = gate_weights(normed, router_weight, route_rows)
    positions = slot_positions(route_rows, experts_count, capacity)
    slot_ids = jnp.arange(experts_count * capacity, dtype=jnp.int32)
    hits = positions[:, :, None] == slot_ids[None, None, :]
    placing = jnp.any(hits, axis=1).astype(jnp.bfloat16)
    buffer = jnp.einsum(
        "rs,rfd->fsd",
        placing,
        normed.reshape(normed.shape[0], fsdp_count, chunk),
        preferred_element_type=jnp.float32,
    ).astype(jnp.bfloat16)
    fsdp_index = lax.axis_index("fsdp")
    order = (fsdp_index - jnp.arange(fsdp_count, dtype=jnp.int32)) % fsdp_count
    combining = jnp.sum(jnp.where(hits, mix_weights[:, :, None], 0.0), axis=1).reshape(
        -1, expert_devices, local_experts, capacity
    )
    slots_in = buffer.reshape(peers, local_experts, capacity, chunk)
    group_size = local_experts // GROUPS
    group_slices = [slice(g * group_size, (g + 1) * group_size) for g in range(GROUPS)]

    def dispatch(outgoing):
        arrived = lax.all_to_all(outgoing, ("fsdp", "expert"), 0, 0, tiled=True)
        return arrived.reshape(peers, group_size, capacity, chunk)

    def partials(arrived, group_experts):
        gate_part = jnp.einsum(
            "sjcd,jdh->sjch", arrived, gate_w[group_experts], preferred_element_type=jnp.float32
        )
        up_part = jnp.einsum(
            "sjcd,jdh->sjch", arrived, up_w[group_experts], preferred_element_type=jnp.float32
        )
        block_shape = (fsdp_count, expert_devices, group_size, capacity, hidden_units)
        return gate_part.reshape(block_shape), up_part.reshape(block_shape)

    def exchange(gate_blocks, up_blocks):
        gate_sum = lax.dynamic_index_in_dim(gate_blocks, fsdp_index, 0, keepdims=False)
        up_sum = lax.dynamic_index_in_dim(up_blocks, fsdp_index, 0, keepdims=False)
        for shift in range(1, fsdp_count):
            target = (fsdp_index + shift) % fsdp_count
            outgoing_pair = jnp.stack(
                [
                    lax.dynamic_index_in_dim(gate_blocks, target, 0, keepdims=False),
                    lax.dynamic_index_in_dim(up_blocks, target, 0, keepdims=False),
                ]
            ).astype(jnp.bfloat16)
            got = lax.ppermute(outgoing_pair, "fsdp", ring_pairs(fsdp_count, shift))
            gate_sum = gate_sum + got[0].astype(jnp.float32)
            up_sum = up_sum + got[1].astype(jnp.float32)
        inner_act = (jax.nn.silu(gate_sum) * up_sum).astype(jnp.bfloat16)
        inner_pieces = [inner_act]
        for shift in range(1, fsdp_count):
            inner_pieces.append(lax.ppermute(inner_act, "fsdp", ring_pairs(fsdp_count, shift)))
        return jnp.take(jnp.stack(inner_pieces), order, axis=0).reshape(
            peers, group_size, capacity, hidden_units
        )

    def finish(inner_all, group_experts):
        produced = jnp.einsum(
            "sjch,jhd->sjcd", inner_all, down_w[group_experts], preferred_element_type=jnp.float32
        ).astype(jnp.bfloat16)
        returned = lax.all_to_all(
            produced.reshape(peers, group_size * capacity, chunk),
            ("fsdp", "expert"),
            0,
            0,
            tiled=True,
        )
        return jnp.einsum(
            "rejc,fejcd->rfd",
            combining[:, :, group_experts],
            returned.reshape(fsdp_count, expert_devices, group_size, capacity, chunk).astype(
                jnp.float32
            ),
            precision=lax.Precision.HIGHEST,
            preferred_element_type=jnp.float32,
        )

    outgoing = [slots_in[:, g].reshape(peers, group_size * capacity, chunk) for g in group_slices]
    first_arrived = dispatch(outgoing[0])
    first_blocks = partials(first_arrived, group_slices[0])
    second_out, first_blocks = lax.optimization_barrier((outgoing[1], first_blocks))
    second_arrived = dispatch(second_out)
    first_inner = exchange(*first_blocks)
    second_blocks = partials(second_arrived, group_slices[1])
    first_inner, second_blocks = lax.optimization_barrier((first_inner, second_blocks))
    branch_sum = finish(first_inner, group_slices[0])
    second_inner = exchange(*second_blocks)
    branch_sum = branch_sum + finish(second_inner, group_slices[1])
    branch_sum = branch_sum.reshape(entering.shape[0], width)
    return (entering.astype(jnp.float32) + branch_sum).astype(jnp.bfloat16)


def body(tokens, norm_gain, router, w_gate, w_up, w_down, routes):
    section_index = lax.axis_index("section")
    sections = lax.axis_size("section")
    token_rows, width = tokens.shape
    piece = token_rows // sections
    experts_count = router.shape[2]
    block_capacity = (7 * BLOCK * TOP + 6 * experts_count - 1) // (6 * experts_count)
    capacity = block_capacity * (piece // BLOCK)
    own_weights = (w_gate[0], w_up[0], w_down[0])
    other_weights = tuple(other_section(w) for w in own_weights)
    own_small = (norm_gain[0], router[0], routes[0])
    other_small = tuple(other_section(v) for v in own_small)
    hidden = lax.dynamic_slice_in_dim(tokens, section_index * piece, piece, 0)
    squares = []
    for layer in range(sections):
        mine = section_index == layer
        gain_row, router_weight, route_all = [
            jnp.where(mine, a, b) for a, b in zip(own_small, other_small)
        ]
        weights = tuple(jnp.where(mine, a, b) for a, b in zip(own_weights, other_weights))
        route_rows = lax.dynamic_slice_in_dim(route_all, section_index * piece, piece, 0)
        hidden = expert_layer(hidden, route_rows, gain_row, router_weight, weights, capacity)
        values = hidden.astype(jnp.float32)
        squares.append(jnp.sum(values * values))
    everyone = ("section", "fsdp", "expert")
    device_count = sections * lax.axis_size("fsdp") * lax.axis_size("expert")
    square_rows = jnp.broadcast_to(jnp.stack(squares)[None, :], (device_count, sections))
    totals = jnp.sum(lax.all_to_all(square_rows, everyone, 0, 0, tiled=True), axis=0)
    token_total = token_rows * lax.axis_size("fsdp") * lax.axis_size("expert")
    stats = jnp.sqrt(totals / (token_total * width))
    layer_stats = lax.dynamic_slice_in_dim(stats, section_index, 1, 0)
    half_width = width // 2
    keep = lax.dynamic_slice_in_dim(hidden, section_index * half_width, half_width, 1)
    send = lax.dynamic_slice_in_dim(hidden, (1 - section_index) * half_width, half_width, 1)
    arrived = other_section(send)
    final_out = jnp.where(
        section_index == 0,
        jnp.concatenate([keep, arrived], axis=0),
        jnp.concatenate([arrived, keep], axis=0),
    )
    return (final_out, layer_stats)


def solution(mesh):
    in_specs = (
        P(("fsdp", "expert"), None),
        P("section", None),
        P("section", None, None),
        P("section", "expert", "fsdp", None),
        P("section", "expert", "fsdp", None),
        P("section", "expert", None, "fsdp"),
        P("section", ("fsdp", "expert"), None),
    )
    out_specs = (P(("fsdp", "expert"), "section"), P("section"))
    return jax.shard_map(body, mesh=mesh, in_specs=in_specs, out_specs=out_specs, check_vma=False)
```

```python
import jax
import jax.numpy as jnp
from jax import lax
from jax.sharding import PartitionSpec as P

TOP = 6
BLOCK = 64
GROUPS = 4


epsilon = 1e-06


def other_section(value):
    return lax.ppermute(value, "section", [(0, 1), (1, 0)])


def ring_pairs(count, shift):
    return [(source, (source + shift) % count) for source in range(count)]


def rms_scaled(hidden_rows, gain_row):
    values = hidden_rows.astype(jnp.float32)
    scale = lax.rsqrt(jnp.mean(values * values, axis=-1, keepdims=True) + epsilon)
    return (values * scale * gain_row).astype(jnp.bfloat16)


def gate_weights(normed, router_weight, route_rows):
    logits = jnp.dot(normed, router_weight, preferred_element_type=jnp.float32)
    scores = jax.nn.sigmoid(logits)
    expert_ids = jnp.arange(router_weight.shape[1], dtype=jnp.int32)
    chosen_mask = (route_rows[:, :, None] == expert_ids[None, None, :]).astype(jnp.float32)
    chosen = jnp.sum(scores[:, None, :] * chosen_mask, axis=2)
    return chosen / jnp.sum(chosen, axis=1, keepdims=True)


def slot_positions(route_rows, experts_count, capacity):
    flat_routes = route_rows.reshape(-1)
    onehot = (flat_routes[:, None] == jnp.arange(experts_count, dtype=jnp.int32)[None, :]).astype(
        jnp.int32
    )
    before = jnp.cumsum(onehot, axis=0) - onehot
    slot_index = jnp.sum(before * onehot, axis=1)
    return (flat_routes * capacity + slot_index).reshape(route_rows.shape)


def expert_layer(entering, route_rows, gain_row, router_weight, weights, capacity):
    gate_w, up_w, down_w = weights
    width = entering.shape[1]
    experts_count = router_weight.shape[1]
    local_experts, chunk, hidden_units = gate_w.shape
    fsdp_count = lax.axis_size("fsdp")
    expert_devices = lax.axis_size("expert")
    peers = fsdp_count * expert_devices
    normed = rms_scaled(entering, gain_row)
    mix_weights = gate_weights(normed, router_weight, route_rows)
    positions = slot_positions(route_rows, experts_count, capacity)
    slot_ids = jnp.arange(experts_count * capacity, dtype=jnp.int32)
    hits = positions[:, :, None] == slot_ids[None, None, :]
    placing = jnp.any(hits, axis=1).astype(jnp.bfloat16)
    buffer = jnp.einsum(
        "rs,rfd->fsd",
        placing,
        normed.reshape(normed.shape[0], fsdp_count, chunk),
        preferred_element_type=jnp.float32,
    ).astype(jnp.bfloat16)
    fsdp_index = lax.axis_index("fsdp")
    order = (fsdp_index - jnp.arange(fsdp_count, dtype=jnp.int32)) % fsdp_count
    combining = jnp.sum(jnp.where(hits, mix_weights[:, :, None], 0.0), axis=1).reshape(
        -1, expert_devices, local_experts, capacity
    )
    slots_in = buffer.reshape(peers, local_experts, capacity, chunk)
    group_size = local_experts // GROUPS
    group_slices = [slice(g * group_size, (g + 1) * group_size) for g in range(GROUPS)]

    def dispatch(outgoing):
        arrived = lax.all_to_all(outgoing, ("fsdp", "expert"), 0, 0, tiled=True)
        return arrived.reshape(peers, group_size, capacity, chunk)

    def partials(arrived, group_experts):
        gate_part = jnp.einsum(
            "sjcd,jdh->sjch", arrived, gate_w[group_experts], preferred_element_type=jnp.float32
        )
        up_part = jnp.einsum(
            "sjcd,jdh->sjch", arrived, up_w[group_experts], preferred_element_type=jnp.float32
        )
        block_shape = (fsdp_count, expert_devices, group_size, capacity, hidden_units)
        return gate_part.reshape(block_shape), up_part.reshape(block_shape)

    def exchange(gate_blocks, up_blocks):
        gate_sum = lax.dynamic_index_in_dim(gate_blocks, fsdp_index, 0, keepdims=False)
        up_sum = lax.dynamic_index_in_dim(up_blocks, fsdp_index, 0, keepdims=False)
        for shift in range(1, fsdp_count):
            target = (fsdp_index + shift) % fsdp_count
            outgoing_pair = jnp.stack(
                [
                    lax.dynamic_index_in_dim(gate_blocks, target, 0, keepdims=False),
                    lax.dynamic_index_in_dim(up_blocks, target, 0, keepdims=False),
                ]
            ).astype(jnp.bfloat16)
            got = lax.ppermute(outgoing_pair, "fsdp", ring_pairs(fsdp_count, shift))
            gate_sum = gate_sum + got[0].astype(jnp.float32)
            up_sum = up_sum + got[1].astype(jnp.float32)
        inner_act = (jax.nn.silu(gate_sum) * up_sum).astype(jnp.bfloat16)
        inner_pieces = [inner_act]
        for shift in range(1, fsdp_count):
            inner_pieces.append(lax.ppermute(inner_act, "fsdp", ring_pairs(fsdp_count, shift)))
        return jnp.take(jnp.stack(inner_pieces), order, axis=0).reshape(
            peers, group_size, capacity, hidden_units
        )

    def finish(inner_all, group_experts):
        produced = jnp.einsum(
            "sjch,jhd->sjcd", inner_all, down_w[group_experts], preferred_element_type=jnp.float32
        ).astype(jnp.bfloat16)
        returned = lax.all_to_all(
            produced.reshape(peers, group_size * capacity, chunk),
            ("fsdp", "expert"),
            0,
            0,
            tiled=True,
        )
        return jnp.einsum(
            "rejc,fejcd->rfd",
            combining[:, :, group_experts],
            returned.reshape(fsdp_count, expert_devices, group_size, capacity, chunk).astype(
                jnp.float32
            ),
            precision=lax.Precision.HIGHEST,
            preferred_element_type=jnp.float32,
        )

    outgoing = [slots_in[:, g].reshape(peers, group_size * capacity, chunk) for g in group_slices]
    blocks = partials(dispatch(outgoing[0]), group_slices[0])
    branch_sum = None
    for group in range(1, GROUPS):
        next_out, blocks = lax.optimization_barrier((outgoing[group], blocks))
        next_arrived = dispatch(next_out)
        inner_all = exchange(*blocks)
        blocks = partials(next_arrived, group_slices[group])
        inner_all, blocks = lax.optimization_barrier((inner_all, blocks))
        finished = finish(inner_all, group_slices[group - 1])
        branch_sum = finished if branch_sum is None else branch_sum + finished
    finished = finish(exchange(*blocks), group_slices[GROUPS - 1])
    branch_sum = finished if branch_sum is None else branch_sum + finished
    branch_sum = branch_sum.reshape(entering.shape[0], width)
    return (entering.astype(jnp.float32) + branch_sum).astype(jnp.bfloat16)


def body(tokens, norm_gain, router, w_gate, w_up, w_down, routes):
    section_index = lax.axis_index("section")
    sections = lax.axis_size("section")
    token_rows, width = tokens.shape
    piece = token_rows // sections
    experts_count = router.shape[2]
    block_capacity = (7 * BLOCK * TOP + 6 * experts_count - 1) // (6 * experts_count)
    capacity = block_capacity * (piece // BLOCK)
    layer_weights = tuple(
        lax.all_gather(w[0], "section", axis=0, tiled=False) for w in (w_gate, w_up, w_down)
    )
    own_small = (norm_gain[0], router[0], routes[0])
    other_small = tuple(other_section(v) for v in own_small)
    hidden = lax.dynamic_slice_in_dim(tokens, section_index * piece, piece, 0)
    squares = []
    for layer in range(sections):
        mine = section_index == layer
        gain_row, router_weight, route_all = [
            jnp.where(mine, a, b) for a, b in zip(own_small, other_small)
        ]
        weights = tuple(w[layer] for w in layer_weights)
        route_rows = lax.dynamic_slice_in_dim(route_all, section_index * piece, piece, 0)
        hidden = expert_layer(hidden, route_rows, gain_row, router_weight, weights, capacity)
        values = hidden.astype(jnp.float32)
        squares.append(jnp.sum(values * values))
    everyone = ("section", "fsdp", "expert")
    device_count = sections * lax.axis_size("fsdp") * lax.axis_size("expert")
    square_rows = jnp.broadcast_to(jnp.stack(squares)[None, :], (device_count, sections))
    totals = jnp.sum(lax.all_to_all(square_rows, everyone, 0, 0, tiled=True), axis=0)
    token_total = token_rows * lax.axis_size("fsdp") * lax.axis_size("expert")
    stats = jnp.sqrt(totals / (token_total * width))
    layer_stats = lax.dynamic_slice_in_dim(stats, section_index, 1, 0)
    half_width = width // 2
    keep = lax.dynamic_slice_in_dim(hidden, section_index * half_width, half_width, 1)
    send = lax.dynamic_slice_in_dim(hidden, (1 - section_index) * half_width, half_width, 1)
    arrived = other_section(send)
    final_out = jnp.where(
        section_index == 0,
        jnp.concatenate([keep, arrived], axis=0),
        jnp.concatenate([arrived, keep], axis=0),
    )
    return (final_out, layer_stats)


def solution(mesh):
    in_specs = (
        P(("fsdp", "expert"), None),
        P("section", None),
        P("section", None, None),
        P("section", "expert", "fsdp", None),
        P("section", "expert", "fsdp", None),
        P("section", "expert", None, "fsdp"),
        P("section", ("fsdp", "expert"), None),
    )
    out_specs = (P(("fsdp", "expert"), "section"), P("section"))
    return jax.shard_map(body, mesh=mesh, in_specs=in_specs, out_specs=out_specs, check_vma=False)
```

```python
import jax
import jax.numpy as jnp
from jax import lax
from jax.sharding import PartitionSpec as P

TOP = 6
BLOCK = 64


epsilon = 1e-06


def other_section(value):
    return lax.ppermute(value, "section", [(0, 1), (1, 0)])


def ring_pairs(count, shift):
    return [(source, (source + shift) % count) for source in range(count)]


def rms_scaled(hidden_rows, gain_row):
    values = hidden_rows.astype(jnp.float32)
    scale = lax.rsqrt(jnp.mean(values * values, axis=-1, keepdims=True) + epsilon)
    return (values * scale * gain_row).astype(jnp.bfloat16)


def gate_weights(normed, router_weight, route_rows):
    logits = jnp.dot(normed, router_weight, preferred_element_type=jnp.float32)
    scores = jax.nn.sigmoid(logits)
    expert_ids = jnp.arange(router_weight.shape[1], dtype=jnp.int32)
    chosen_mask = (route_rows[:, :, None] == expert_ids[None, None, :]).astype(jnp.float32)
    chosen = jnp.sum(scores[:, None, :] * chosen_mask, axis=2)
    return chosen / jnp.sum(chosen, axis=1, keepdims=True)


def slot_positions(route_rows, experts_count, capacity):
    flat_routes = route_rows.reshape(-1)
    onehot = (flat_routes[:, None] == jnp.arange(experts_count, dtype=jnp.int32)[None, :]).astype(
        jnp.int32
    )
    before = jnp.cumsum(onehot, axis=0) - onehot
    slot_index = jnp.sum(before * onehot, axis=1)
    return (flat_routes * capacity + slot_index).reshape(route_rows.shape)


def other_half(value):
    return lax.ppermute(value, "zhalf", [(0, 1), (1, 0)])


def half_buffer(positions, normed, slot_ids, fsdp_count, chunk):
    placing = jnp.any(positions[:, :, None] == slot_ids[None, None, :], axis=1).astype(jnp.bfloat16)
    return jnp.einsum(
        "rs,rfd->fsd",
        placing,
        normed.reshape(normed.shape[0], fsdp_count, chunk),
        preferred_element_type=jnp.float32,
    ).astype(jnp.bfloat16)


def expert_layer(entering, route_rows, gain_row, router_weight, weights, capacity):
    gate_w, up_w, down_w = weights
    rows, width = entering.shape
    experts_count = router_weight.shape[1]
    local_experts, chunk, hidden_units = gate_w.shape
    fsdp_count = lax.axis_size("fsdp")
    halves = lax.axis_size("zhalf")
    inner_devices = lax.axis_size("inner")
    half_index = lax.axis_index("zhalf")
    fsdp_index = lax.axis_index("fsdp")
    partner_entering = other_half(entering)
    partner_routes = other_half(route_rows)
    normed = rms_scaled(entering, gain_row)
    partner_normed = rms_scaled(partner_entering, gain_row)
    mix_weights = gate_weights(normed, router_weight, route_rows)
    positions = slot_positions(route_rows, experts_count, capacity)
    partner_positions = slot_positions(partner_routes, experts_count, capacity)
    half_slots = experts_count // halves * capacity
    local_ids = half_index * half_slots + jnp.arange(half_slots, dtype=jnp.int32)
    own_buffer = half_buffer(positions, normed, local_ids, fsdp_count, chunk)
    partner_buffer = half_buffer(partner_positions, partner_normed, local_ids, fsdp_count, chunk)
    group_slots = local_experts * capacity
    outgoing = jnp.stack(
        [
            own_buffer.reshape(fsdp_count, inner_devices, group_slots, chunk),
            partner_buffer.reshape(fsdp_count, inner_devices, group_slots, chunk),
        ],
        axis=2,
    ).reshape(fsdp_count * inner_devices, halves * group_slots, chunk)
    arrived = lax.all_to_all(outgoing, ("fsdp", "inner"), 0, 0, tiled=True)
    sources = fsdp_count * inner_devices * halves
    arrived = arrived.reshape(sources, local_experts, capacity, chunk)
    gate_part = jnp.einsum("sjcd,jdh->sjch", arrived, gate_w, preferred_element_type=jnp.float32)
    up_part = jnp.einsum("sjcd,jdh->sjch", arrived, up_w, preferred_element_type=jnp.float32)
    block_shape = (fsdp_count, sources // fsdp_count, local_experts, capacity, hidden_units)
    gate_blocks = gate_part.reshape(block_shape)
    up_blocks = up_part.reshape(block_shape)
    gate_sum = lax.dynamic_index_in_dim(gate_blocks, fsdp_index, 0, keepdims=False)
    up_sum = lax.dynamic_index_in_dim(up_blocks, fsdp_index, 0, keepdims=False)
    for shift in range(1, fsdp_count):
        target = (fsdp_index + shift) % fsdp_count
        outgoing_pair = jnp.stack(
            [
                lax.dynamic_index_in_dim(gate_blocks, target, 0, keepdims=False),
                lax.dynamic_index_in_dim(up_blocks, target, 0, keepdims=False),
            ]
        ).astype(jnp.bfloat16)
        got = lax.ppermute(outgoing_pair, "fsdp", ring_pairs(fsdp_count, shift))
        gate_sum = gate_sum + got[0].astype(jnp.float32)
        up_sum = up_sum + got[1].astype(jnp.float32)
    inner_act = (jax.nn.silu(gate_sum) * up_sum).astype(jnp.bfloat16)
    inner_pieces = [inner_act]
    for shift in range(1, fsdp_count):
        inner_pieces.append(lax.ppermute(inner_act, "fsdp", ring_pairs(fsdp_count, shift)))
    order = (fsdp_index - jnp.arange(fsdp_count, dtype=jnp.int32)) % fsdp_count
    inner_all = jnp.take(jnp.stack(inner_pieces), order, axis=0).reshape(
        sources, local_experts, capacity, hidden_units
    )
    produced = jnp.einsum(
        "sjch,jhd->sjcd", inner_all, down_w, preferred_element_type=jnp.float32
    ).astype(jnp.bfloat16)
    produced = produced.reshape(fsdp_count, inner_devices, halves, group_slots, chunk)
    piece_for_half = (jnp.arange(halves, dtype=jnp.int32) - half_index) % halves
    sending = jnp.take(produced, piece_for_half, axis=2).transpose(0, 2, 1, 3, 4)
    returned = lax.all_to_all(
        sending.reshape(sources, group_slots, chunk),
        ("fsdp", "zhalf", "inner"),
        0,
        0,
        tiled=True,
    )
    slot_ids = jnp.arange(experts_count * capacity, dtype=jnp.int32)
    hits = positions[:, :, None] == slot_ids[None, None, :]
    combining = jnp.sum(jnp.where(hits, mix_weights[:, :, None], 0.0), axis=1)
    branch_sum = jnp.einsum(
        "rs,fsd->rfd",
        combining,
        returned.reshape(fsdp_count, experts_count * capacity, chunk).astype(jnp.float32),
        precision=lax.Precision.HIGHEST,
        preferred_element_type=jnp.float32,
    ).reshape(rows, width)
    return (entering.astype(jnp.float32) + branch_sum).astype(jnp.bfloat16)


def body(tokens, norm_gain, router, w_gate, w_up, w_down, routes):
    section_index = lax.axis_index("section")
    sections = lax.axis_size("section")
    token_rows, width = tokens.shape
    piece = token_rows // sections
    experts_count = router.shape[2]
    block_capacity = (7 * BLOCK * TOP + 6 * experts_count - 1) // (6 * experts_count)
    capacity = block_capacity * (piece // BLOCK)
    own_weights = (w_gate[0], w_up[0], w_down[0])
    other_weights = tuple(other_section(w) for w in own_weights)
    own_small = (norm_gain[0], router[0], routes[0])
    other_small = tuple(other_section(v) for v in own_small)
    hidden = lax.dynamic_slice_in_dim(tokens, section_index * piece, piece, 0)
    squares = []
    for layer in range(sections):
        mine = section_index == layer
        gain_row, router_weight, route_all = [
            jnp.where(mine, a, b) for a, b in zip(own_small, other_small)
        ]
        weights = tuple(jnp.where(mine, a, b) for a, b in zip(own_weights, other_weights))
        route_rows = lax.dynamic_slice_in_dim(route_all, section_index * piece, piece, 0)
        hidden = expert_layer(hidden, route_rows, gain_row, router_weight, weights, capacity)
        values = hidden.astype(jnp.float32)
        squares.append(jnp.sum(values * values))
    everyone = ("section", "fsdp", "zhalf", "inner")
    expert_devices = lax.axis_size("zhalf") * lax.axis_size("inner")
    device_count = sections * lax.axis_size("fsdp") * expert_devices
    square_rows = jnp.broadcast_to(jnp.stack(squares)[None, :], (device_count, sections))
    totals = jnp.sum(lax.all_to_all(square_rows, everyone, 0, 0, tiled=True), axis=0)
    token_total = token_rows * lax.axis_size("fsdp") * expert_devices
    stats = jnp.sqrt(totals / (token_total * width))
    layer_stats = lax.dynamic_slice_in_dim(stats, section_index, 1, 0)
    half_width = width // 2
    keep = lax.dynamic_slice_in_dim(hidden, section_index * half_width, half_width, 1)
    send = lax.dynamic_slice_in_dim(hidden, (1 - section_index) * half_width, half_width, 1)
    arrived = other_section(send)
    final_out = jnp.where(
        section_index == 0,
        jnp.concatenate([keep, arrived], axis=0),
        jnp.concatenate([arrived, keep], axis=0),
    )
    return (final_out, layer_stats)


def solution(mesh):
    sizes = dict(zip(mesh.axis_names, mesh.devices.shape))
    devices = mesh.devices.reshape(
        sizes["section"], sizes["fsdp"], 2, sizes["expert"] // 2
    )
    split_mesh = jax.sharding.Mesh(devices, ("section", "fsdp", "zhalf", "inner"))
    tokens_axes = ("fsdp", "zhalf", "inner")
    experts_axes = ("zhalf", "inner")
    in_specs = (
        P(tokens_axes, None),
        P("section", None),
        P("section", None, None),
        P("section", experts_axes, "fsdp", None),
        P("section", experts_axes, "fsdp", None),
        P("section", experts_axes, None, "fsdp"),
        P("section", tokens_axes, None),
    )
    out_specs = (P(tokens_axes, "section"), P("section"))
    return jax.shard_map(
        body, mesh=split_mesh, in_specs=in_specs, out_specs=out_specs, check_vma=False
    )
```

```python
import jax
import jax.numpy as jnp
from jax import lax
from jax.sharding import PartitionSpec as P

TOP = 6
BLOCK = 64


epsilon = 1e-06


def other_section(value):
    return lax.ppermute(value, "section", [(0, 1), (1, 0)])


def ring_pairs(count, shift):
    return [(source, (source + shift) % count) for source in range(count)]


def rms_scaled(hidden_rows, gain_row):
    values = hidden_rows.astype(jnp.float32)
    scale = lax.rsqrt(jnp.mean(values * values, axis=-1, keepdims=True) + epsilon)
    return (values * scale * gain_row).astype(jnp.bfloat16)


def gate_weights(normed, router_weight, route_rows):
    logits = jnp.dot(normed, router_weight, preferred_element_type=jnp.float32)
    scores = jax.nn.sigmoid(logits)
    expert_ids = jnp.arange(router_weight.shape[1], dtype=jnp.int32)
    chosen_mask = (route_rows[:, :, None] == expert_ids[None, None, :]).astype(jnp.float32)
    chosen = jnp.sum(scores[:, None, :] * chosen_mask, axis=2)
    return chosen / jnp.sum(chosen, axis=1, keepdims=True)


def slot_positions(route_rows, experts_count, capacity):
    flat_routes = route_rows.reshape(-1)
    onehot = (flat_routes[:, None] == jnp.arange(experts_count, dtype=jnp.int32)[None, :]).astype(
        jnp.int32
    )
    before = jnp.cumsum(onehot, axis=0) - onehot
    slot_index = jnp.sum(before * onehot, axis=1)
    return (flat_routes * capacity + slot_index).reshape(route_rows.shape)


def other_half(value):
    return lax.ppermute(value, "zhalf", [(0, 1), (1, 0)])


def half_buffer(positions, normed, slot_ids, fsdp_count, chunk):
    placing = jnp.any(positions[:, :, None] == slot_ids[None, None, :], axis=1).astype(jnp.bfloat16)
    return jnp.einsum(
        "rs,rfd->fsd",
        placing,
        normed.reshape(normed.shape[0], fsdp_count, chunk),
        preferred_element_type=jnp.float32,
    ).astype(jnp.bfloat16)


def expert_layer(entering, route_rows, gain_row, router_weight, weights, capacity):
    gate_w, up_w, down_w = weights
    rows, width = entering.shape
    experts_count = router_weight.shape[1]
    local_experts, chunk, hidden_units = gate_w.shape
    fsdp_count = lax.axis_size("fsdp")
    halves = lax.axis_size("zhalf")
    inner_devices = lax.axis_size("inner")
    half_index = lax.axis_index("zhalf")
    fsdp_index = lax.axis_index("fsdp")
    partner_entering = other_half(entering)
    partner_routes = other_half(route_rows)
    normed = rms_scaled(entering, gain_row)
    partner_normed = rms_scaled(partner_entering, gain_row)
    mix_weights = gate_weights(normed, router_weight, route_rows)
    positions = slot_positions(route_rows, experts_count, capacity)
    partner_positions = slot_positions(partner_routes, experts_count, capacity)
    half_slots = experts_count // halves * capacity
    local_ids = half_index * half_slots + jnp.arange(half_slots, dtype=jnp.int32)
    first_half = half_index == 0
    lower_normed = jnp.where(first_half, normed, partner_normed)
    upper_normed = jnp.where(first_half, partner_normed, normed)
    lower_positions = jnp.where(first_half, positions, partner_positions)
    upper_positions = jnp.where(first_half, partner_positions, positions)
    lower_buffer = half_buffer(lower_positions, lower_normed, local_ids, fsdp_count, chunk)
    upper_buffer = half_buffer(upper_positions, upper_normed, local_ids, fsdp_count, chunk)
    group_slots = local_experts * capacity
    outgoing = jnp.stack(
        [
            lower_buffer.reshape(fsdp_count, inner_devices, group_slots, chunk),
            upper_buffer.reshape(fsdp_count, inner_devices, group_slots, chunk),
        ],
        axis=2,
    ).reshape(fsdp_count * inner_devices, halves * group_slots, chunk)
    arrived = lax.all_to_all(outgoing, ("fsdp", "inner"), 0, 0, tiled=True)
    sources = fsdp_count * inner_devices * halves
    arrived = arrived.reshape(sources, local_experts, capacity, chunk)
    gate_part = jnp.einsum("sjcd,jdh->sjch", arrived, gate_w, preferred_element_type=jnp.float32)
    up_part = jnp.einsum("sjcd,jdh->sjch", arrived, up_w, preferred_element_type=jnp.float32)
    block_shape = (fsdp_count, sources // fsdp_count, local_experts, capacity, hidden_units)
    gate_blocks = gate_part.reshape(block_shape)
    up_blocks = up_part.reshape(block_shape)
    gate_sum = lax.dynamic_index_in_dim(gate_blocks, fsdp_index, 0, keepdims=False)
    up_sum = lax.dynamic_index_in_dim(up_blocks, fsdp_index, 0, keepdims=False)
    for shift in range(1, fsdp_count):
        target = (fsdp_index + shift) % fsdp_count
        outgoing_pair = jnp.stack(
            [
                lax.dynamic_index_in_dim(gate_blocks, target, 0, keepdims=False),
                lax.dynamic_index_in_dim(up_blocks, target, 0, keepdims=False),
            ]
        ).astype(jnp.bfloat16)
        got = lax.ppermute(outgoing_pair, "fsdp", ring_pairs(fsdp_count, shift))
        gate_sum = gate_sum + got[0].astype(jnp.float32)
        up_sum = up_sum + got[1].astype(jnp.float32)
    inner_act = (jax.nn.silu(gate_sum) * up_sum).astype(jnp.bfloat16)
    inner_pieces = [inner_act]
    for shift in range(1, fsdp_count):
        inner_pieces.append(lax.ppermute(inner_act, "fsdp", ring_pairs(fsdp_count, shift)))
    order = (fsdp_index - jnp.arange(fsdp_count, dtype=jnp.int32)) % fsdp_count
    inner_all = jnp.take(jnp.stack(inner_pieces), order, axis=0).reshape(
        sources, local_experts, capacity, hidden_units
    )
    inner_all = inner_all.reshape(
        fsdp_count, inner_devices, halves, local_experts, capacity, hidden_units
    )
    sending = jnp.einsum(
        "fipjch,jhd->fpijcd", inner_all, down_w, preferred_element_type=jnp.float32
    ).astype(jnp.bfloat16)
    returned = lax.all_to_all(
        sending.reshape(sources, group_slots, chunk),
        ("fsdp", "zhalf", "inner"),
        0,
        0,
        tiled=True,
    )
    slot_ids = jnp.arange(experts_count * capacity, dtype=jnp.int32)
    hits = positions[:, :, None] == slot_ids[None, None, :]
    combining = jnp.sum(jnp.where(hits, mix_weights[:, :, None], 0.0), axis=1)
    branch_sum = jnp.einsum(
        "rs,fsd->rfd",
        combining,
        returned.reshape(fsdp_count, experts_count * capacity, chunk).astype(jnp.float32),
        precision=lax.Precision.HIGHEST,
        preferred_element_type=jnp.float32,
    ).reshape(rows, width)
    return (entering.astype(jnp.float32) + branch_sum).astype(jnp.bfloat16)


def body(tokens, norm_gain, router, w_gate, w_up, w_down, routes):
    section_index = lax.axis_index("section")
    sections = lax.axis_size("section")
    token_rows, width = tokens.shape
    piece = token_rows // sections
    experts_count = router.shape[2]
    block_capacity = (7 * BLOCK * TOP + 6 * experts_count - 1) // (6 * experts_count)
    capacity = block_capacity * (piece // BLOCK)
    own_weights = (w_gate[0], w_up[0], w_down[0])
    other_weights = tuple(other_section(w) for w in own_weights)
    own_small = (norm_gain[0], router[0], routes[0])
    other_small = tuple(other_section(v) for v in own_small)
    hidden = lax.dynamic_slice_in_dim(tokens, section_index * piece, piece, 0)
    squares = []
    for layer in range(sections):
        mine = section_index == layer
        gain_row, router_weight, route_all = [
            jnp.where(mine, a, b) for a, b in zip(own_small, other_small)
        ]
        weights = tuple(jnp.where(mine, a, b) for a, b in zip(own_weights, other_weights))
        route_rows = lax.dynamic_slice_in_dim(route_all, section_index * piece, piece, 0)
        hidden = expert_layer(hidden, route_rows, gain_row, router_weight, weights, capacity)
        values = hidden.astype(jnp.float32)
        squares.append(jnp.sum(values * values))
    everyone = ("section", "fsdp", "zhalf", "inner")
    expert_devices = lax.axis_size("zhalf") * lax.axis_size("inner")
    device_count = sections * lax.axis_size("fsdp") * expert_devices
    square_rows = jnp.broadcast_to(jnp.stack(squares)[None, :], (device_count, sections))
    totals = jnp.sum(lax.all_to_all(square_rows, everyone, 0, 0, tiled=True), axis=0)
    token_total = token_rows * lax.axis_size("fsdp") * expert_devices
    stats = jnp.sqrt(totals / (token_total * width))
    layer_stats = lax.dynamic_slice_in_dim(stats, section_index, 1, 0)
    half_width = width // 2
    keep = lax.dynamic_slice_in_dim(hidden, section_index * half_width, half_width, 1)
    send = lax.dynamic_slice_in_dim(hidden, (1 - section_index) * half_width, half_width, 1)
    arrived = other_section(send)
    final_out = jnp.where(
        section_index == 0,
        jnp.concatenate([keep, arrived], axis=0),
        jnp.concatenate([arrived, keep], axis=0),
    )
    return (final_out, layer_stats)


def solution(mesh):
    sizes = dict(zip(mesh.axis_names, mesh.devices.shape))
    devices = mesh.devices.reshape(
        sizes["section"], sizes["fsdp"], 2, sizes["expert"] // 2
    )
    split_mesh = jax.sharding.Mesh(devices, ("section", "fsdp", "zhalf", "inner"))
    tokens_axes = ("fsdp", "zhalf", "inner")
    experts_axes = ("zhalf", "inner")
    in_specs = (
        P(tokens_axes, None),
        P("section", None),
        P("section", None, None),
        P("section", experts_axes, "fsdp", None),
        P("section", experts_axes, "fsdp", None),
        P("section", experts_axes, None, "fsdp"),
        P("section", tokens_axes, None),
    )
    out_specs = (P(tokens_axes, "section"), P("section"))
    return jax.shard_map(
        body, mesh=split_mesh, in_specs=in_specs, out_specs=out_specs, check_vma=False
    )
```

```python
import jax
import jax.numpy as jnp
from jax import lax
from jax.sharding import PartitionSpec as P

TOP = 6
BLOCK = 64


epsilon = 1e-06


def other_section(value):
    return lax.ppermute(value, "section", [(0, 1), (1, 0)])


def ring_pairs(count, shift):
    return [(source, (source + shift) % count) for source in range(count)]


def rms_scaled(hidden_rows, gain_row):
    values = hidden_rows.astype(jnp.float32)
    scale = lax.rsqrt(jnp.mean(values * values, axis=-1, keepdims=True) + epsilon)
    return (values * scale * gain_row).astype(jnp.bfloat16)


def gate_weights(normed, router_weight, route_rows):
    logits = jnp.dot(normed, router_weight, preferred_element_type=jnp.float32)
    scores = jax.nn.sigmoid(logits)
    expert_ids = jnp.arange(router_weight.shape[1], dtype=jnp.int32)
    chosen_mask = (route_rows[:, :, None] == expert_ids[None, None, :]).astype(jnp.float32)
    chosen = jnp.sum(scores[:, None, :] * chosen_mask, axis=2)
    return chosen / jnp.sum(chosen, axis=1, keepdims=True)


def slot_positions(route_rows, experts_count, capacity):
    flat_routes = route_rows.reshape(-1)
    onehot = (flat_routes[:, None] == jnp.arange(experts_count, dtype=jnp.int32)[None, :]).astype(
        jnp.int32
    )
    before = jnp.cumsum(onehot, axis=0) - onehot
    slot_index = jnp.sum(before * onehot, axis=1)
    return (flat_routes * capacity + slot_index).reshape(route_rows.shape)


def other_half(value):
    return lax.ppermute(value, "zhalf", [(0, 1), (1, 0)])


def half_buffer(positions, normed, slot_ids, fsdp_count, chunk):
    placing = jnp.any(positions[:, :, None] == slot_ids[None, None, :], axis=1).astype(jnp.bfloat16)
    return jnp.einsum(
        "rs,rfd->fsd",
        placing,
        normed.reshape(normed.shape[0], fsdp_count, chunk),
        preferred_element_type=jnp.float32,
    ).astype(jnp.bfloat16)


def expert_layer(entering, route_rows, partner_routes, gain_row, router_weight, weights, capacity):
    gate_w, up_w, down_w = weights
    rows, width = entering.shape
    experts_count = router_weight.shape[1]
    local_experts, chunk, hidden_units = gate_w.shape
    fsdp_count = lax.axis_size("fsdp")
    halves = lax.axis_size("zhalf")
    inner_devices = lax.axis_size("inner")
    half_index = lax.axis_index("zhalf")
    fsdp_index = lax.axis_index("fsdp")
    partner_entering = other_half(entering)
    normed = rms_scaled(entering, gain_row)
    partner_normed = rms_scaled(partner_entering, gain_row)
    mix_weights = gate_weights(normed, router_weight, route_rows)
    positions = slot_positions(route_rows, experts_count, capacity)
    partner_positions = slot_positions(partner_routes, experts_count, capacity)
    half_slots = experts_count // halves * capacity
    local_ids = half_index * half_slots + jnp.arange(half_slots, dtype=jnp.int32)
    first_half = half_index == 0
    lower_normed = jnp.where(first_half, normed, partner_normed)
    upper_normed = jnp.where(first_half, partner_normed, normed)
    lower_positions = jnp.where(first_half, positions, partner_positions)
    upper_positions = jnp.where(first_half, partner_positions, positions)
    lower_buffer = half_buffer(lower_positions, lower_normed, local_ids, fsdp_count, chunk)
    upper_buffer = half_buffer(upper_positions, upper_normed, local_ids, fsdp_count, chunk)
    group_slots = local_experts * capacity
    outgoing = jnp.stack(
        [
            lower_buffer.reshape(fsdp_count, inner_devices, group_slots, chunk),
            upper_buffer.reshape(fsdp_count, inner_devices, group_slots, chunk),
        ],
        axis=2,
    ).reshape(fsdp_count * inner_devices, halves * group_slots, chunk)
    arrived = lax.all_to_all(outgoing, ("fsdp", "inner"), 0, 0, tiled=True)
    sources = fsdp_count * inner_devices * halves
    arrived = arrived.reshape(sources, local_experts, capacity, chunk)
    gate_part = jnp.einsum("sjcd,jdh->sjch", arrived, gate_w, preferred_element_type=jnp.float32)
    up_part = jnp.einsum("sjcd,jdh->sjch", arrived, up_w, preferred_element_type=jnp.float32)
    block_shape = (fsdp_count, sources // fsdp_count, local_experts, capacity, hidden_units)
    gate_blocks = gate_part.reshape(block_shape)
    up_blocks = up_part.reshape(block_shape)
    gate_sum = lax.dynamic_index_in_dim(gate_blocks, fsdp_index, 0, keepdims=False)
    up_sum = lax.dynamic_index_in_dim(up_blocks, fsdp_index, 0, keepdims=False)
    for shift in range(1, fsdp_count):
        target = (fsdp_index + shift) % fsdp_count
        outgoing_pair = jnp.stack(
            [
                lax.dynamic_index_in_dim(gate_blocks, target, 0, keepdims=False),
                lax.dynamic_index_in_dim(up_blocks, target, 0, keepdims=False),
            ]
        ).astype(jnp.bfloat16)
        got = lax.ppermute(outgoing_pair, "fsdp", ring_pairs(fsdp_count, shift))
        gate_sum = gate_sum + got[0].astype(jnp.float32)
        up_sum = up_sum + got[1].astype(jnp.float32)
    inner_act = (jax.nn.silu(gate_sum) * up_sum).astype(jnp.bfloat16)
    inner_pieces = [inner_act]
    for shift in range(1, fsdp_count):
        inner_pieces.append(lax.ppermute(inner_act, "fsdp", ring_pairs(fsdp_count, shift)))
    order = (fsdp_index - jnp.arange(fsdp_count, dtype=jnp.int32)) % fsdp_count
    inner_all = jnp.take(jnp.stack(inner_pieces), order, axis=0).reshape(
        sources, local_experts, capacity, hidden_units
    )
    inner_all = inner_all.reshape(
        fsdp_count, inner_devices, halves, local_experts, capacity, hidden_units
    )
    sending = jnp.einsum(
        "fipjch,jhd->fpijcd", inner_all, down_w, preferred_element_type=jnp.float32
    ).astype(jnp.bfloat16)
    returned = lax.all_to_all(
        sending.reshape(sources, group_slots, chunk),
        ("fsdp", "zhalf", "inner"),
        0,
        0,
        tiled=True,
    )
    slot_ids = jnp.arange(experts_count * capacity, dtype=jnp.int32)
    hits = positions[:, :, None] == slot_ids[None, None, :]
    combining = jnp.sum(jnp.where(hits, mix_weights[:, :, None], 0.0), axis=1)
    branch_sum = jnp.einsum(
        "rs,fsd->rfd",
        combining,
        returned.reshape(fsdp_count, experts_count * capacity, chunk).astype(jnp.float32),
        precision=lax.Precision.HIGHEST,
        preferred_element_type=jnp.float32,
    ).reshape(rows, width)
    return (entering.astype(jnp.float32) + branch_sum).astype(jnp.bfloat16)


def body(tokens, norm_gain, router, w_gate, w_up, w_down, routes):
    section_index = lax.axis_index("section")
    sections = lax.axis_size("section")
    token_rows, width = tokens.shape
    piece = token_rows // sections
    experts_count = router.shape[2]
    block_capacity = (7 * BLOCK * TOP + 6 * experts_count - 1) // (6 * experts_count)
    capacity = block_capacity * (piece // BLOCK)
    own_weights = (w_gate[0], w_up[0], w_down[0])
    other_weights = tuple(other_section(w) for w in own_weights)
    own_small = (norm_gain[0], router[0])
    other_small = tuple(other_section(v) for v in own_small)
    own_routes = routes[0]
    section_routes = other_section(own_routes)
    half_routes = other_half(own_routes)
    diagonal_routes = lax.ppermute(
        own_routes, ("section", "zhalf"), [(0, 3), (3, 0), (1, 2), (2, 1)]
    )
    hidden = lax.dynamic_slice_in_dim(tokens, section_index * piece, piece, 0)
    squares = []
    for layer in range(sections):
        mine = section_index == layer
        gain_row, router_weight = [jnp.where(mine, a, b) for a, b in zip(own_small, other_small)]
        weights = tuple(jnp.where(mine, a, b) for a, b in zip(own_weights, other_weights))
        route_all = jnp.where(mine, own_routes, section_routes)
        partner_all = jnp.where(mine, half_routes, diagonal_routes)
        route_rows = lax.dynamic_slice_in_dim(route_all, section_index * piece, piece, 0)
        partner_rows = lax.dynamic_slice_in_dim(partner_all, section_index * piece, piece, 0)
        hidden = expert_layer(
            hidden, route_rows, partner_rows, gain_row, router_weight, weights, capacity
        )
        values = hidden.astype(jnp.float32)
        squares.append(jnp.sum(values * values))
    everyone = ("section", "fsdp", "zhalf", "inner")
    expert_devices = lax.axis_size("zhalf") * lax.axis_size("inner")
    device_count = sections * lax.axis_size("fsdp") * expert_devices
    square_rows = jnp.broadcast_to(jnp.stack(squares)[None, :], (device_count, sections))
    totals = jnp.sum(lax.all_to_all(square_rows, everyone, 0, 0, tiled=True), axis=0)
    token_total = token_rows * lax.axis_size("fsdp") * expert_devices
    stats = jnp.sqrt(totals / (token_total * width))
    layer_stats = lax.dynamic_slice_in_dim(stats, section_index, 1, 0)
    half_width = width // 2
    keep = lax.dynamic_slice_in_dim(hidden, section_index * half_width, half_width, 1)
    send = lax.dynamic_slice_in_dim(hidden, (1 - section_index) * half_width, half_width, 1)
    arrived = other_section(send)
    final_out = jnp.where(
        section_index == 0,
        jnp.concatenate([keep, arrived], axis=0),
        jnp.concatenate([arrived, keep], axis=0),
    )
    return (final_out, layer_stats)


def solution(mesh):
    sizes = dict(zip(mesh.axis_names, mesh.devices.shape))
    devices = mesh.devices.reshape(
        sizes["section"], sizes["fsdp"], 2, sizes["expert"] // 2
    )
    split_mesh = jax.sharding.Mesh(devices, ("section", "fsdp", "zhalf", "inner"))
    tokens_axes = ("fsdp", "zhalf", "inner")
    experts_axes = ("zhalf", "inner")
    in_specs = (
        P(tokens_axes, None),
        P("section", None),
        P("section", None, None),
        P("section", experts_axes, "fsdp", None),
        P("section", experts_axes, "fsdp", None),
        P("section", experts_axes, None, "fsdp"),
        P("section", tokens_axes, None),
    )
    out_specs = (P(tokens_axes, "section"), P("section"))
    return jax.shard_map(
        body, mesh=split_mesh, in_specs=in_specs, out_specs=out_specs, check_vma=False
    )
```

```python
import jax
import jax.numpy as jnp
from jax import lax
from jax.sharding import PartitionSpec as P

TOP = 6
BLOCK = 64


epsilon = 1e-06


def other_section(value):
    return lax.ppermute(value, "section", [(0, 1), (1, 0)])


def ring_pairs(count, shift):
    return [(source, (source + shift) % count) for source in range(count)]


def rms_scaled(hidden_rows, gain_row):
    values = hidden_rows.astype(jnp.float32)
    scale = lax.rsqrt(jnp.mean(values * values, axis=-1, keepdims=True) + epsilon)
    return (values * scale * gain_row).astype(jnp.bfloat16)


def gate_weights(normed, router_weight, route_rows):
    logits = jnp.dot(normed, router_weight, preferred_element_type=jnp.float32)
    scores = jax.nn.sigmoid(logits)
    expert_ids = jnp.arange(router_weight.shape[1], dtype=jnp.int32)
    chosen_mask = (route_rows[:, :, None] == expert_ids[None, None, :]).astype(jnp.float32)
    chosen = jnp.sum(scores[:, None, :] * chosen_mask, axis=2)
    return chosen / jnp.sum(chosen, axis=1, keepdims=True)


def slot_positions(route_rows, experts_count, capacity):
    flat_routes = route_rows.reshape(-1)
    onehot = (flat_routes[:, None] == jnp.arange(experts_count, dtype=jnp.int32)[None, :]).astype(
        jnp.int32
    )
    before = jnp.cumsum(onehot, axis=0) - onehot
    slot_index = jnp.sum(before * onehot, axis=1)
    return (flat_routes * capacity + slot_index).reshape(route_rows.shape)


def other_half(value):
    return lax.ppermute(value, "zhalf", [(0, 1), (1, 0)])


def half_buffer(positions, normed, slot_ids, fsdp_count, chunk):
    placing = jnp.any(positions[:, :, None] == slot_ids[None, None, :], axis=1).astype(jnp.bfloat16)
    return jnp.einsum(
        "rs,rfd->fsd",
        placing,
        normed.reshape(normed.shape[0], fsdp_count, chunk),
        preferred_element_type=jnp.float32,
    ).astype(jnp.bfloat16)


def expert_layer(entering, route_rows, partner_routes, gain_row, router_weight, weights, capacity):
    gate_w, up_w, down_w = weights
    rows, width = entering.shape
    experts_count = router_weight.shape[1]
    local_experts, chunk, hidden_units = gate_w.shape
    fsdp_count = lax.axis_size("fsdp")
    halves = lax.axis_size("zhalf")
    inner_devices = lax.axis_size("inner")
    half_index = lax.axis_index("zhalf")
    fsdp_index = lax.axis_index("fsdp")
    partner_entering = other_half(entering)
    normed = rms_scaled(entering, gain_row)
    partner_normed = rms_scaled(partner_entering, gain_row)
    mix_weights = gate_weights(normed, router_weight, route_rows)
    positions = slot_positions(route_rows, experts_count, capacity)
    partner_positions = slot_positions(partner_routes, experts_count, capacity)
    half_slots = experts_count // halves * capacity
    local_ids = half_index * half_slots + jnp.arange(half_slots, dtype=jnp.int32)
    first_half = half_index == 0
    lower_normed = jnp.where(first_half, normed, partner_normed)
    upper_normed = jnp.where(first_half, partner_normed, normed)
    lower_positions = jnp.where(first_half, positions, partner_positions)
    upper_positions = jnp.where(first_half, partner_positions, positions)
    lower_buffer = half_buffer(lower_positions, lower_normed, local_ids, fsdp_count, chunk)
    upper_buffer = half_buffer(upper_positions, upper_normed, local_ids, fsdp_count, chunk)
    group_slots = local_experts * capacity
    outgoing = jnp.stack(
        [
            lower_buffer.reshape(fsdp_count, inner_devices, group_slots, chunk),
            upper_buffer.reshape(fsdp_count, inner_devices, group_slots, chunk),
        ],
        axis=2,
    ).reshape(fsdp_count * inner_devices, halves * group_slots, chunk)
    arrived = lax.all_to_all(outgoing, ("fsdp", "inner"), 0, 0, tiled=True)
    sources = fsdp_count * inner_devices * halves
    arrived = arrived.reshape(sources, local_experts, capacity, chunk)
    arrived_blocks = arrived.reshape(fsdp_count, sources // fsdp_count, local_experts, capacity, chunk)

    def gate_and_up(rows_in):
        gate_part = jnp.einsum(
            "sjcd,jdh->sjch", rows_in, gate_w, preferred_element_type=jnp.float32
        )
        up_part = jnp.einsum("sjcd,jdh->sjch", rows_in, up_w, preferred_element_type=jnp.float32)
        return gate_part, up_part

    received = []
    for shift in range(1, fsdp_count):
        target = (fsdp_index + shift) % fsdp_count
        outgoing_pair = jnp.stack(
            gate_and_up(lax.dynamic_index_in_dim(arrived_blocks, target, 0, keepdims=False))
        ).astype(jnp.bfloat16)
        received.append(lax.ppermute(outgoing_pair, "fsdp", ring_pairs(fsdp_count, shift)))
    gate_sum, up_sum = gate_and_up(
        lax.dynamic_index_in_dim(arrived_blocks, fsdp_index, 0, keepdims=False)
    )
    for got in received:
        gate_sum = gate_sum + got[0].astype(jnp.float32)
        up_sum = up_sum + got[1].astype(jnp.float32)
    inner_act = (jax.nn.silu(gate_sum) * up_sum).astype(jnp.bfloat16)
    inner_pieces = [inner_act]
    for shift in range(1, fsdp_count):
        inner_pieces.append(lax.ppermute(inner_act, "fsdp", ring_pairs(fsdp_count, shift)))
    order = (fsdp_index - jnp.arange(fsdp_count, dtype=jnp.int32)) % fsdp_count
    inner_all = jnp.take(jnp.stack(inner_pieces), order, axis=0).reshape(
        sources, local_experts, capacity, hidden_units
    )
    inner_all = inner_all.reshape(
        fsdp_count, inner_devices, halves, local_experts, capacity, hidden_units
    )
    sending = jnp.einsum(
        "fipjch,jhd->fpijcd", inner_all, down_w, preferred_element_type=jnp.float32
    ).astype(jnp.bfloat16)
    returned = lax.all_to_all(
        sending.reshape(sources, group_slots, chunk),
        ("fsdp", "zhalf", "inner"),
        0,
        0,
        tiled=True,
    )
    slot_ids = jnp.arange(experts_count * capacity, dtype=jnp.int32)
    hits = positions[:, :, None] == slot_ids[None, None, :]
    combining = jnp.sum(jnp.where(hits, mix_weights[:, :, None], 0.0), axis=1)
    branch_sum = jnp.einsum(
        "rs,fsd->rfd",
        combining,
        returned.reshape(fsdp_count, experts_count * capacity, chunk).astype(jnp.float32),
        precision=lax.Precision.HIGHEST,
        preferred_element_type=jnp.float32,
    ).reshape(rows, width)
    return (entering.astype(jnp.float32) + branch_sum).astype(jnp.bfloat16)


def body(tokens, norm_gain, router, w_gate, w_up, w_down, routes):
    section_index = lax.axis_index("section")
    sections = lax.axis_size("section")
    token_rows, width = tokens.shape
    piece = token_rows // sections
    experts_count = router.shape[2]
    block_capacity = (7 * BLOCK * TOP + 6 * experts_count - 1) // (6 * experts_count)
    capacity = block_capacity * (piece // BLOCK)
    own_weights = (w_gate[0], w_up[0], w_down[0])
    other_weights = tuple(other_section(w) for w in own_weights)
    own_small = (norm_gain[0], router[0])
    other_small = tuple(other_section(v) for v in own_small)
    own_routes = routes[0]
    section_routes = other_section(own_routes)
    half_routes = other_half(own_routes)
    diagonal_routes = lax.ppermute(
        own_routes, ("section", "zhalf"), [(0, 3), (3, 0), (1, 2), (2, 1)]
    )
    hidden = lax.dynamic_slice_in_dim(tokens, section_index * piece, piece, 0)
    squares = []
    for layer in range(sections):
        mine = section_index == layer
        gain_row, router_weight = [jnp.where(mine, a, b) for a, b in zip(own_small, other_small)]
        weights = tuple(jnp.where(mine, a, b) for a, b in zip(own_weights, other_weights))
        route_all = jnp.where(mine, own_routes, section_routes)
        partner_all = jnp.where(mine, half_routes, diagonal_routes)
        route_rows = lax.dynamic_slice_in_dim(route_all, section_index * piece, piece, 0)
        partner_rows = lax.dynamic_slice_in_dim(partner_all, section_index * piece, piece, 0)
        hidden = expert_layer(
            hidden, route_rows, partner_rows, gain_row, router_weight, weights, capacity
        )
        values = hidden.astype(jnp.float32)
        squares.append(jnp.sum(values * values))
    everyone = ("section", "fsdp", "zhalf", "inner")
    expert_devices = lax.axis_size("zhalf") * lax.axis_size("inner")
    device_count = sections * lax.axis_size("fsdp") * expert_devices
    square_rows = jnp.broadcast_to(jnp.stack(squares)[None, :], (device_count, sections))
    totals = jnp.sum(lax.all_to_all(square_rows, everyone, 0, 0, tiled=True), axis=0)
    token_total = token_rows * lax.axis_size("fsdp") * expert_devices
    stats = jnp.sqrt(totals / (token_total * width))
    layer_stats = lax.dynamic_slice_in_dim(stats, section_index, 1, 0)
    half_width = width // 2
    keep = lax.dynamic_slice_in_dim(hidden, section_index * half_width, half_width, 1)
    send = lax.dynamic_slice_in_dim(hidden, (1 - section_index) * half_width, half_width, 1)
    arrived = other_section(send)
    final_out = jnp.where(
        section_index == 0,
        jnp.concatenate([keep, arrived], axis=0),
        jnp.concatenate([arrived, keep], axis=0),
    )
    return (final_out, layer_stats)


def solution(mesh):
    sizes = dict(zip(mesh.axis_names, mesh.devices.shape))
    devices = mesh.devices.reshape(
        sizes["section"], sizes["fsdp"], 2, sizes["expert"] // 2
    )
    split_mesh = jax.sharding.Mesh(devices, ("section", "fsdp", "zhalf", "inner"))
    tokens_axes = ("fsdp", "zhalf", "inner")
    experts_axes = ("zhalf", "inner")
    in_specs = (
        P(tokens_axes, None),
        P("section", None),
        P("section", None, None),
        P("section", experts_axes, "fsdp", None),
        P("section", experts_axes, "fsdp", None),
        P("section", experts_axes, None, "fsdp"),
        P("section", tokens_axes, None),
    )
    out_specs = (P(tokens_axes, "section"), P("section"))
    return jax.shard_map(
        body, mesh=split_mesh, in_specs=in_specs, out_specs=out_specs, check_vma=False
    )
```

```python
import jax
import jax.numpy as jnp
from jax import lax
from jax.sharding import PartitionSpec as P

TOP = 6
BLOCK = 64


epsilon = 1e-06


def other_section(value):
    return lax.ppermute(value, "section", [(0, 1), (1, 0)])


def ring_pairs(count, shift):
    return [(source, (source + shift) % count) for source in range(count)]


def rms_scaled(hidden_rows, gain_row):
    values = hidden_rows.astype(jnp.float32)
    scale = lax.rsqrt(jnp.mean(values * values, axis=-1, keepdims=True) + epsilon)
    return (values * scale * gain_row).astype(jnp.bfloat16)


def gate_weights(normed, router_weight, route_rows):
    logits = jnp.dot(normed, router_weight, preferred_element_type=jnp.float32)
    scores = jax.nn.sigmoid(logits)
    expert_ids = jnp.arange(router_weight.shape[1], dtype=jnp.int32)
    chosen_mask = (route_rows[:, :, None] == expert_ids[None, None, :]).astype(jnp.float32)
    chosen = jnp.sum(scores[:, None, :] * chosen_mask, axis=2)
    return chosen / jnp.sum(chosen, axis=1, keepdims=True)


def slot_positions(route_rows, experts_count, capacity):
    flat_routes = route_rows.reshape(-1)
    onehot = (flat_routes[:, None] == jnp.arange(experts_count, dtype=jnp.int32)[None, :]).astype(
        jnp.int32
    )
    before = jnp.cumsum(onehot, axis=0) - onehot
    slot_index = jnp.sum(before * onehot, axis=1)
    return (flat_routes * capacity + slot_index).reshape(route_rows.shape)


def other_half(value):
    return lax.ppermute(value, "zhalf", [(0, 1), (1, 0)])


def half_buffer(positions, normed, slot_ids, fsdp_count, chunk):
    placing = jnp.any(positions[:, :, None] == slot_ids[None, None, :], axis=1).astype(jnp.bfloat16)
    return jnp.einsum(
        "rs,rfd->fsd",
        placing,
        normed.reshape(normed.shape[0], fsdp_count, chunk),
        preferred_element_type=jnp.float32,
    ).astype(jnp.bfloat16)


def expert_layer(entering, route_rows, partner_routes, gain_row, router_weight, weights, capacity):
    gate_up_w, down_w = weights
    rows, width = entering.shape
    experts_count = router_weight.shape[1]
    local_experts, hidden_units, chunk = down_w.shape
    fsdp_count = lax.axis_size("fsdp")
    halves = lax.axis_size("zhalf")
    inner_devices = lax.axis_size("inner")
    half_index = lax.axis_index("zhalf")
    fsdp_index = lax.axis_index("fsdp")
    partner_entering = other_half(entering)
    normed = rms_scaled(entering, gain_row)
    partner_normed = rms_scaled(partner_entering, gain_row)
    mix_weights = gate_weights(normed, router_weight, route_rows)
    positions = slot_positions(route_rows, experts_count, capacity)
    partner_positions = slot_positions(partner_routes, experts_count, capacity)
    half_slots = experts_count // halves * capacity
    local_ids = half_index * half_slots + jnp.arange(half_slots, dtype=jnp.int32)
    first_half = half_index == 0
    lower_normed = jnp.where(first_half, normed, partner_normed)
    upper_normed = jnp.where(first_half, partner_normed, normed)
    lower_positions = jnp.where(first_half, positions, partner_positions)
    upper_positions = jnp.where(first_half, partner_positions, positions)
    lower_buffer = half_buffer(lower_positions, lower_normed, local_ids, fsdp_count, chunk)
    upper_buffer = half_buffer(upper_positions, upper_normed, local_ids, fsdp_count, chunk)
    group_slots = local_experts * capacity
    outgoing = jnp.stack(
        [
            lower_buffer.reshape(fsdp_count, inner_devices, group_slots, chunk),
            upper_buffer.reshape(fsdp_count, inner_devices, group_slots, chunk),
        ],
        axis=2,
    ).reshape(fsdp_count * inner_devices, halves * group_slots, chunk)
    arrived = lax.all_to_all(outgoing, ("fsdp", "inner"), 0, 0, tiled=True)
    sources = fsdp_count * inner_devices * halves
    arrived = arrived.reshape(sources, local_experts, capacity, chunk)
    arrived_blocks = arrived.reshape(fsdp_count, sources // fsdp_count, local_experts, capacity, chunk)

    def gate_and_up(rows_in):
        return jnp.einsum("sjcd,jdh->sjch", rows_in, gate_up_w, preferred_element_type=jnp.float32)

    received = []
    for shift in range(1, fsdp_count):
        target = (fsdp_index + shift) % fsdp_count
        outgoing_part = gate_and_up(
            lax.dynamic_index_in_dim(arrived_blocks, target, 0, keepdims=False)
        ).astype(jnp.bfloat16)
        received.append(lax.ppermute(outgoing_part, "fsdp", ring_pairs(fsdp_count, shift)))
    both_sum = gate_and_up(lax.dynamic_index_in_dim(arrived_blocks, fsdp_index, 0, keepdims=False))
    for got in received:
        both_sum = both_sum + got.astype(jnp.float32)
    gate_sum = both_sum[..., :hidden_units]
    up_sum = both_sum[..., hidden_units:]
    inner_act = (jax.nn.silu(gate_sum) * up_sum).astype(jnp.bfloat16)
    inner_pieces = [inner_act]
    for shift in range(1, fsdp_count):
        inner_pieces.append(lax.ppermute(inner_act, "fsdp", ring_pairs(fsdp_count, shift)))
    order = (fsdp_index - jnp.arange(fsdp_count, dtype=jnp.int32)) % fsdp_count
    inner_all = jnp.take(jnp.stack(inner_pieces), order, axis=0).reshape(
        sources, local_experts, capacity, hidden_units
    )
    inner_all = inner_all.reshape(
        fsdp_count, inner_devices, halves, local_experts, capacity, hidden_units
    )
    sending = jnp.einsum(
        "fipjch,jhd->fpijcd", inner_all, down_w, preferred_element_type=jnp.float32
    ).astype(jnp.bfloat16)
    returned = lax.all_to_all(
        sending.reshape(sources, group_slots, chunk),
        ("fsdp", "zhalf", "inner"),
        0,
        0,
        tiled=True,
    )
    slot_ids = jnp.arange(experts_count * capacity, dtype=jnp.int32)
    hits = positions[:, :, None] == slot_ids[None, None, :]
    combining = jnp.sum(jnp.where(hits, mix_weights[:, :, None], 0.0), axis=1)
    branch_sum = jnp.einsum(
        "rs,fsd->rfd",
        combining,
        returned.reshape(fsdp_count, experts_count * capacity, chunk).astype(jnp.float32),
        precision=lax.Precision.HIGHEST,
        preferred_element_type=jnp.float32,
    ).reshape(rows, width)
    return (entering.astype(jnp.float32) + branch_sum).astype(jnp.bfloat16)


def body(tokens, norm_gain, router, w_gate, w_up, w_down, routes):
    section_index = lax.axis_index("section")
    sections = lax.axis_size("section")
    token_rows, width = tokens.shape
    piece = token_rows // sections
    experts_count = router.shape[2]
    block_capacity = (7 * BLOCK * TOP + 6 * experts_count - 1) // (6 * experts_count)
    capacity = block_capacity * (piece // BLOCK)
    own_weights = (w_gate[0], w_up[0], w_down[0])
    other_weights = tuple(other_section(w) for w in own_weights)
    own_small = (norm_gain[0], router[0])
    other_small = tuple(other_section(v) for v in own_small)
    own_routes = routes[0]
    section_routes = other_section(own_routes)
    half_routes = other_half(own_routes)
    diagonal_routes = lax.ppermute(
        own_routes, ("section", "zhalf"), [(0, 3), (3, 0), (1, 2), (2, 1)]
    )
    hidden = lax.dynamic_slice_in_dim(tokens, section_index * piece, piece, 0)
    squares = []
    for layer in range(sections):
        mine = section_index == layer
        gain_row, router_weight = [jnp.where(mine, a, b) for a, b in zip(own_small, other_small)]
        gate_sel, up_sel, down_sel = [jnp.where(mine, a, b) for a, b in zip(own_weights, other_weights)]
        weights = lax.optimization_barrier((jnp.concatenate([gate_sel, up_sel], axis=-1), down_sel))
        route_all = jnp.where(mine, own_routes, section_routes)
        partner_all = jnp.where(mine, half_routes, diagonal_routes)
        route_rows = lax.dynamic_slice_in_dim(route_all, section_index * piece, piece, 0)
        partner_rows = lax.dynamic_slice_in_dim(partner_all, section_index * piece, piece, 0)
        hidden = expert_layer(
            hidden, route_rows, partner_rows, gain_row, router_weight, weights, capacity
        )
        values = hidden.astype(jnp.float32)
        squares.append(jnp.sum(values * values))
    everyone = ("section", "fsdp", "zhalf", "inner")
    expert_devices = lax.axis_size("zhalf") * lax.axis_size("inner")
    device_count = sections * lax.axis_size("fsdp") * expert_devices
    square_rows = jnp.broadcast_to(jnp.stack(squares)[None, :], (device_count, sections))
    totals = jnp.sum(lax.all_to_all(square_rows, everyone, 0, 0, tiled=True), axis=0)
    token_total = token_rows * lax.axis_size("fsdp") * expert_devices
    stats = jnp.sqrt(totals / (token_total * width))
    layer_stats = lax.dynamic_slice_in_dim(stats, section_index, 1, 0)
    half_width = width // 2
    keep = lax.dynamic_slice_in_dim(hidden, section_index * half_width, half_width, 1)
    send = lax.dynamic_slice_in_dim(hidden, (1 - section_index) * half_width, half_width, 1)
    arrived = other_section(send)
    final_out = jnp.where(
        section_index == 0,
        jnp.concatenate([keep, arrived], axis=0),
        jnp.concatenate([arrived, keep], axis=0),
    )
    return (final_out, layer_stats)


def solution(mesh):
    sizes = dict(zip(mesh.axis_names, mesh.devices.shape))
    devices = mesh.devices.reshape(
        sizes["section"], sizes["fsdp"], 2, sizes["expert"] // 2
    )
    split_mesh = jax.sharding.Mesh(devices, ("section", "fsdp", "zhalf", "inner"))
    tokens_axes = ("fsdp", "zhalf", "inner")
    experts_axes = ("zhalf", "inner")
    in_specs = (
        P(tokens_axes, None),
        P("section", None),
        P("section", None, None),
        P("section", experts_axes, "fsdp", None),
        P("section", experts_axes, "fsdp", None),
        P("section", experts_axes, None, "fsdp"),
        P("section", tokens_axes, None),
    )
    out_specs = (P(tokens_axes, "section"), P("section"))
    return jax.shard_map(
        body, mesh=split_mesh, in_specs=in_specs, out_specs=out_specs, check_vma=False
    )
```

```python
import jax
import jax.numpy as jnp
from jax import lax
from jax.sharding import PartitionSpec as P

TOP = 6
BLOCK = 64


epsilon = 1e-06


def other_section(value):
    return lax.ppermute(value, "section", [(0, 1), (1, 0)])


def ring_pairs(count, shift):
    return [(source, (source + shift) % count) for source in range(count)]


def rms_scaled(hidden_rows, gain_row):
    values = hidden_rows.astype(jnp.float32)
    scale = lax.rsqrt(jnp.mean(values * values, axis=-1, keepdims=True) + epsilon)
    return (values * scale * gain_row).astype(jnp.bfloat16)


def gate_weights(normed, router_weight, route_rows):
    logits = jnp.dot(normed, router_weight, preferred_element_type=jnp.float32)
    scores = jax.nn.sigmoid(logits)
    expert_ids = jnp.arange(router_weight.shape[1], dtype=jnp.int32)
    chosen_mask = (route_rows[:, :, None] == expert_ids[None, None, :]).astype(jnp.float32)
    chosen = jnp.sum(scores[:, None, :] * chosen_mask, axis=2)
    return chosen / jnp.sum(chosen, axis=1, keepdims=True)


def slot_positions(route_rows, experts_count, capacity):
    flat_routes = route_rows.reshape(-1)
    onehot = (flat_routes[:, None] == jnp.arange(experts_count, dtype=jnp.int32)[None, :]).astype(
        jnp.int32
    )
    before = jnp.cumsum(onehot, axis=0) - onehot
    slot_index = jnp.sum(before * onehot, axis=1)
    return (flat_routes * capacity + slot_index).reshape(route_rows.shape)


def other_half(value):
    return lax.ppermute(value, "zhalf", [(0, 1), (1, 0)])


def half_buffer(positions, normed, slot_ids, fsdp_count, chunk):
    placing = jnp.any(positions[:, :, None] == slot_ids[None, None, :], axis=1).astype(jnp.bfloat16)
    return jnp.einsum(
        "rs,rfd->fsd",
        placing,
        normed.reshape(normed.shape[0], fsdp_count, chunk),
        preferred_element_type=jnp.float32,
    ).astype(jnp.bfloat16)


def expert_layer(entering, route_rows, partner_routes, gain_row, router_weight, weights, capacity):
    gate_w, up_w, down_w = weights
    rows, width = entering.shape
    experts_count = router_weight.shape[1]
    local_experts, chunk, hidden_units = gate_w.shape
    fsdp_count = lax.axis_size("fsdp")
    halves = lax.axis_size("zhalf")
    inner_devices = lax.axis_size("inner")
    half_index = lax.axis_index("zhalf")
    fsdp_index = lax.axis_index("fsdp")
    partner_entering = other_half(entering)
    normed = rms_scaled(entering, gain_row)
    partner_normed = rms_scaled(partner_entering, gain_row)
    mix_weights = gate_weights(normed, router_weight, route_rows)
    positions = slot_positions(route_rows, experts_count, capacity)
    partner_positions = slot_positions(partner_routes, experts_count, capacity)
    half_slots = experts_count // halves * capacity
    local_ids = half_index * half_slots + jnp.arange(half_slots, dtype=jnp.int32)
    first_half = half_index == 0
    group_slots = local_experts * capacity
    own_buffer = half_buffer(positions, normed, local_ids, fsdp_count, chunk)
    own_arrived = lax.all_to_all(
        own_buffer.reshape(fsdp_count * inner_devices, group_slots, chunk), ("fsdp", "inner"), 0, 0, tiled=True
    )
    partner_buffer = half_buffer(partner_positions, partner_normed, local_ids, fsdp_count, chunk)
    partner_arrived = lax.all_to_all(
        partner_buffer.reshape(fsdp_count * inner_devices, group_slots, chunk),
        ("fsdp", "inner"),
        0,
        0,
        tiled=True,
    )
    arrived = jnp.where(
        first_half,
        jnp.stack([own_arrived, partner_arrived], axis=1),
        jnp.stack([partner_arrived, own_arrived], axis=1),
    )
    sources = fsdp_count * inner_devices * halves
    arrived = arrived.reshape(sources, local_experts, capacity, chunk)
    arrived_blocks = arrived.reshape(fsdp_count, sources // fsdp_count, local_experts, capacity, chunk)

    def gate_and_up(rows_in):
        gate_part = jnp.einsum(
            "sjcd,jdh->sjch", rows_in, gate_w, preferred_element_type=jnp.float32
        )
        up_part = jnp.einsum("sjcd,jdh->sjch", rows_in, up_w, preferred_element_type=jnp.float32)
        return gate_part, up_part

    received = []
    for shift in range(1, fsdp_count):
        target = (fsdp_index + shift) % fsdp_count
        outgoing_pair = jnp.stack(
            gate_and_up(lax.dynamic_index_in_dim(arrived_blocks, target, 0, keepdims=False))
        ).astype(jnp.bfloat16)
        received.append(lax.ppermute(outgoing_pair, "fsdp", ring_pairs(fsdp_count, shift)))
    gate_sum, up_sum = gate_and_up(
        lax.dynamic_index_in_dim(arrived_blocks, fsdp_index, 0, keepdims=False)
    )
    for got in received:
        gate_sum = gate_sum + got[0].astype(jnp.float32)
        up_sum = up_sum + got[1].astype(jnp.float32)
    inner_act = (jax.nn.silu(gate_sum) * up_sum).astype(jnp.bfloat16)
    inner_pieces = [inner_act]
    for shift in range(1, fsdp_count):
        inner_pieces.append(lax.ppermute(inner_act, "fsdp", ring_pairs(fsdp_count, shift)))
    order = (fsdp_index - jnp.arange(fsdp_count, dtype=jnp.int32)) % fsdp_count
    inner_all = jnp.take(jnp.stack(inner_pieces), order, axis=0).reshape(
        sources, local_experts, capacity, hidden_units
    )
    inner_all = inner_all.reshape(
        fsdp_count, inner_devices, halves, local_experts, capacity, hidden_units
    )
    sending = jnp.einsum(
        "fipjch,jhd->fpijcd", inner_all, down_w, preferred_element_type=jnp.float32
    ).astype(jnp.bfloat16)
    returned = lax.all_to_all(
        sending.reshape(sources, group_slots, chunk),
        ("fsdp", "zhalf", "inner"),
        0,
        0,
        tiled=True,
    )
    slot_ids = jnp.arange(experts_count * capacity, dtype=jnp.int32)
    hits = positions[:, :, None] == slot_ids[None, None, :]
    combining = jnp.sum(jnp.where(hits, mix_weights[:, :, None], 0.0), axis=1)
    branch_sum = jnp.einsum(
        "rs,fsd->rfd",
        combining,
        returned.reshape(fsdp_count, experts_count * capacity, chunk).astype(jnp.float32),
        precision=lax.Precision.HIGHEST,
        preferred_element_type=jnp.float32,
    ).reshape(rows, width)
    return (entering.astype(jnp.float32) + branch_sum).astype(jnp.bfloat16)


def body(tokens, norm_gain, router, w_gate, w_up, w_down, routes):
    section_index = lax.axis_index("section")
    sections = lax.axis_size("section")
    token_rows, width = tokens.shape
    piece = token_rows // sections
    experts_count = router.shape[2]
    block_capacity = (7 * BLOCK * TOP + 6 * experts_count - 1) // (6 * experts_count)
    capacity = block_capacity * (piece // BLOCK)
    own_weights = (w_gate[0], w_up[0], w_down[0])
    other_weights = tuple(other_section(w) for w in own_weights)
    own_small = (norm_gain[0], router[0])
    other_small = tuple(other_section(v) for v in own_small)
    own_routes = routes[0]
    section_routes = other_section(own_routes)
    half_routes = other_half(own_routes)
    diagonal_routes = lax.ppermute(
        own_routes, ("section", "zhalf"), [(0, 3), (3, 0), (1, 2), (2, 1)]
    )
    hidden = lax.dynamic_slice_in_dim(tokens, section_index * piece, piece, 0)
    squares = []
    for layer in range(sections):
        mine = section_index == layer
        gain_row, router_weight = [jnp.where(mine, a, b) for a, b in zip(own_small, other_small)]
        weights = tuple(jnp.where(mine, a, b) for a, b in zip(own_weights, other_weights))
        route_all = jnp.where(mine, own_routes, section_routes)
        partner_all = jnp.where(mine, half_routes, diagonal_routes)
        route_rows = lax.dynamic_slice_in_dim(route_all, section_index * piece, piece, 0)
        partner_rows = lax.dynamic_slice_in_dim(partner_all, section_index * piece, piece, 0)
        hidden = expert_layer(
            hidden, route_rows, partner_rows, gain_row, router_weight, weights, capacity
        )
        values = hidden.astype(jnp.float32)
        squares.append(jnp.sum(values * values))
    everyone = ("section", "fsdp", "zhalf", "inner")
    expert_devices = lax.axis_size("zhalf") * lax.axis_size("inner")
    device_count = sections * lax.axis_size("fsdp") * expert_devices
    square_rows = jnp.broadcast_to(jnp.stack(squares)[None, :], (device_count, sections))
    totals = jnp.sum(lax.all_to_all(square_rows, everyone, 0, 0, tiled=True), axis=0)
    token_total = token_rows * lax.axis_size("fsdp") * expert_devices
    stats = jnp.sqrt(totals / (token_total * width))
    layer_stats = lax.dynamic_slice_in_dim(stats, section_index, 1, 0)
    half_width = width // 2
    keep = lax.dynamic_slice_in_dim(hidden, section_index * half_width, half_width, 1)
    send = lax.dynamic_slice_in_dim(hidden, (1 - section_index) * half_width, half_width, 1)
    arrived = other_section(send)
    final_out = jnp.where(
        section_index == 0,
        jnp.concatenate([keep, arrived], axis=0),
        jnp.concatenate([arrived, keep], axis=0),
    )
    return (final_out, layer_stats)


def solution(mesh):
    sizes = dict(zip(mesh.axis_names, mesh.devices.shape))
    devices = mesh.devices.reshape(
        sizes["section"], sizes["fsdp"], 2, sizes["expert"] // 2
    )
    split_mesh = jax.sharding.Mesh(devices, ("section", "fsdp", "zhalf", "inner"))
    tokens_axes = ("fsdp", "zhalf", "inner")
    experts_axes = ("zhalf", "inner")
    in_specs = (
        P(tokens_axes, None),
        P("section", None),
        P("section", None, None),
        P("section", experts_axes, "fsdp", None),
        P("section", experts_axes, "fsdp", None),
        P("section", experts_axes, None, "fsdp"),
        P("section", tokens_axes, None),
    )
    out_specs = (P(tokens_axes, "section"), P("section"))
    return jax.shard_map(
        body, mesh=split_mesh, in_specs=in_specs, out_specs=out_specs, check_vma=False
    )
```

```python
import jax
import jax.numpy as jnp
from jax import lax
from jax.sharding import PartitionSpec as P

TOP = 6
BLOCK = 64


epsilon = 1e-06


def other_section(value):
    return lax.ppermute(value, "section", [(0, 1), (1, 0)])


def ring_pairs(count, shift):
    return [(source, (source + shift) % count) for source in range(count)]


def rms_scaled(hidden_rows, gain_row):
    values = hidden_rows.astype(jnp.float32)
    scale = lax.rsqrt(jnp.mean(values * values, axis=-1, keepdims=True) + epsilon)
    return (values * scale * gain_row).astype(jnp.bfloat16)


def gate_weights(normed, router_weight, route_rows):
    logits = jnp.dot(normed, router_weight, preferred_element_type=jnp.float32)
    scores = jax.nn.sigmoid(logits)
    expert_ids = jnp.arange(router_weight.shape[1], dtype=jnp.int32)
    chosen_mask = (route_rows[:, :, None] == expert_ids[None, None, :]).astype(jnp.float32)
    chosen = jnp.sum(scores[:, None, :] * chosen_mask, axis=2)
    return chosen / jnp.sum(chosen, axis=1, keepdims=True)


def slot_positions(route_rows, experts_count, capacity):
    flat_routes = route_rows.reshape(-1)
    onehot = (flat_routes[:, None] == jnp.arange(experts_count, dtype=jnp.int32)[None, :]).astype(
        jnp.int32
    )
    before = jnp.cumsum(onehot, axis=0) - onehot
    slot_index = jnp.sum(before * onehot, axis=1)
    return (flat_routes * capacity + slot_index).reshape(route_rows.shape)


def other_half(value):
    return lax.ppermute(value, "zhalf", [(0, 1), (1, 0)])


def half_buffer(positions, normed, slot_ids, fsdp_count, chunk):
    placing = jnp.any(positions[:, :, None] == slot_ids[None, None, :], axis=1).astype(jnp.bfloat16)
    return jnp.einsum(
        "rs,rfd->fsd",
        placing,
        normed.reshape(normed.shape[0], fsdp_count, chunk),
        preferred_element_type=jnp.float32,
    ).astype(jnp.bfloat16)


def expert_layer(entering, route_rows, partner_routes, gain_row, router_weight, weights, capacity):
    down_w = weights[-1]
    rows, width = entering.shape
    experts_count = router_weight.shape[1]
    local_experts, hidden_units, chunk = down_w.shape
    fsdp_count = lax.axis_size("fsdp")
    halves = lax.axis_size("zhalf")
    inner_devices = lax.axis_size("inner")
    half_index = lax.axis_index("zhalf")
    fsdp_index = lax.axis_index("fsdp")
    partner_entering = other_half(entering)
    normed = rms_scaled(entering, gain_row)
    partner_normed = rms_scaled(partner_entering, gain_row)
    mix_weights = gate_weights(normed, router_weight, route_rows)
    positions = slot_positions(route_rows, experts_count, capacity)
    partner_positions = slot_positions(partner_routes, experts_count, capacity)
    half_slots = experts_count // halves * capacity
    local_ids = half_index * half_slots + jnp.arange(half_slots, dtype=jnp.int32)
    first_half = half_index == 0
    lower_normed = jnp.where(first_half, normed, partner_normed)
    upper_normed = jnp.where(first_half, partner_normed, normed)
    lower_positions = jnp.where(first_half, positions, partner_positions)
    upper_positions = jnp.where(first_half, partner_positions, positions)
    lower_buffer = half_buffer(lower_positions, lower_normed, local_ids, fsdp_count, chunk)
    upper_buffer = half_buffer(upper_positions, upper_normed, local_ids, fsdp_count, chunk)
    group_slots = local_experts * capacity
    outgoing = jnp.stack(
        [
            lower_buffer.reshape(fsdp_count, inner_devices, group_slots, chunk),
            upper_buffer.reshape(fsdp_count, inner_devices, group_slots, chunk),
        ],
        axis=2,
    ).reshape(fsdp_count * inner_devices, halves * group_slots, chunk)
    arrived = lax.all_to_all(outgoing, ("fsdp", "inner"), 0, 0, tiled=True)
    sources = fsdp_count * inner_devices * halves
    arrived = arrived.reshape(sources, local_experts, capacity, chunk)
    arrived_blocks = arrived.reshape(fsdp_count, sources // fsdp_count, local_experts, capacity, chunk)

    def gate_and_up(rows_in):
        parts = [
            jnp.einsum("sjcd,jdh->sjch", rows_in, w, preferred_element_type=jnp.float32)
            for w in weights[:-1]
        ]
        return parts[0] if len(parts) == 1 else jnp.concatenate(parts, axis=-1)

    received = []
    for shift in range(1, fsdp_count):
        target = (fsdp_index + shift) % fsdp_count
        outgoing_part = gate_and_up(
            lax.dynamic_index_in_dim(arrived_blocks, target, 0, keepdims=False)
        ).astype(jnp.bfloat16)
        received.append(lax.ppermute(outgoing_part, "fsdp", ring_pairs(fsdp_count, shift)))
    both_sum = gate_and_up(lax.dynamic_index_in_dim(arrived_blocks, fsdp_index, 0, keepdims=False))
    for got in received:
        both_sum = both_sum + got.astype(jnp.float32)
    gate_sum = both_sum[..., :hidden_units]
    up_sum = both_sum[..., hidden_units:]
    inner_act = (jax.nn.silu(gate_sum) * up_sum).astype(jnp.bfloat16)
    inner_pieces = [inner_act]
    for shift in range(1, fsdp_count):
        inner_pieces.append(lax.ppermute(inner_act, "fsdp", ring_pairs(fsdp_count, shift)))
    order = (fsdp_index - jnp.arange(fsdp_count, dtype=jnp.int32)) % fsdp_count
    inner_all = jnp.take(jnp.stack(inner_pieces), order, axis=0).reshape(
        sources, local_experts, capacity, hidden_units
    )
    inner_all = inner_all.reshape(
        fsdp_count, inner_devices, halves, local_experts, capacity, hidden_units
    )
    sending = jnp.einsum(
        "fipjch,jhd->fpijcd", inner_all, down_w, preferred_element_type=jnp.float32
    ).astype(jnp.bfloat16)
    returned = lax.all_to_all(
        sending.reshape(sources, group_slots, chunk),
        ("fsdp", "zhalf", "inner"),
        0,
        0,
        tiled=True,
    )
    slot_ids = jnp.arange(experts_count * capacity, dtype=jnp.int32)
    hits = positions[:, :, None] == slot_ids[None, None, :]
    combining = jnp.sum(jnp.where(hits, mix_weights[:, :, None], 0.0), axis=1)
    branch_sum = jnp.einsum(
        "rs,fsd->rfd",
        combining,
        returned.reshape(fsdp_count, experts_count * capacity, chunk).astype(jnp.float32),
        precision=lax.Precision.HIGHEST,
        preferred_element_type=jnp.float32,
    ).reshape(rows, width)
    return (entering.astype(jnp.float32) + branch_sum).astype(jnp.bfloat16)


def body(tokens, norm_gain, router, w_gate, w_up, w_down, routes):
    section_index = lax.axis_index("section")
    sections = lax.axis_size("section")
    token_rows, width = tokens.shape
    piece = token_rows // sections
    experts_count = router.shape[2]
    block_capacity = (7 * BLOCK * TOP + 6 * experts_count - 1) // (6 * experts_count)
    capacity = block_capacity * (piece // BLOCK)
    own_weights = (w_gate[0], w_up[0], w_down[0])
    other_weights = tuple(other_section(w) for w in own_weights)
    own_small = (norm_gain[0], router[0])
    other_small = tuple(other_section(v) for v in own_small)
    own_routes = routes[0]
    section_routes = other_section(own_routes)
    half_routes = other_half(own_routes)
    diagonal_routes = lax.ppermute(
        own_routes, ("section", "zhalf"), [(0, 3), (3, 0), (1, 2), (2, 1)]
    )
    hidden = lax.dynamic_slice_in_dim(tokens, section_index * piece, piece, 0)
    squares = []
    for layer in range(sections):
        mine = section_index == layer
        gain_row, router_weight = [jnp.where(mine, a, b) for a, b in zip(own_small, other_small)]
        if layer == 0:
            weights = tuple(jnp.where(mine, a, b) for a, b in zip(own_weights, other_weights))
        else:
            pairs = lax.optimization_barrier((own_weights, other_weights, hidden))[:2]
            gate_sel, up_sel, down_sel = [jnp.where(mine, a, b) for a, b in zip(*pairs)]
            weights = (jnp.concatenate([gate_sel, up_sel], axis=-1), down_sel)
        route_all = jnp.where(mine, own_routes, section_routes)
        partner_all = jnp.where(mine, half_routes, diagonal_routes)
        route_rows = lax.dynamic_slice_in_dim(route_all, section_index * piece, piece, 0)
        partner_rows = lax.dynamic_slice_in_dim(partner_all, section_index * piece, piece, 0)
        hidden = expert_layer(
            hidden, route_rows, partner_rows, gain_row, router_weight, weights, capacity
        )
        values = hidden.astype(jnp.float32)
        squares.append(jnp.sum(values * values))
    everyone = ("section", "fsdp", "zhalf", "inner")
    expert_devices = lax.axis_size("zhalf") * lax.axis_size("inner")
    device_count = sections * lax.axis_size("fsdp") * expert_devices
    square_rows = jnp.broadcast_to(jnp.stack(squares)[None, :], (device_count, sections))
    totals = jnp.sum(lax.all_to_all(square_rows, everyone, 0, 0, tiled=True), axis=0)
    token_total = token_rows * lax.axis_size("fsdp") * expert_devices
    stats = jnp.sqrt(totals / (token_total * width))
    layer_stats = lax.dynamic_slice_in_dim(stats, section_index, 1, 0)
    half_width = width // 2
    keep = lax.dynamic_slice_in_dim(hidden, section_index * half_width, half_width, 1)
    send = lax.dynamic_slice_in_dim(hidden, (1 - section_index) * half_width, half_width, 1)
    arrived = other_section(send)
    final_out = jnp.where(
        section_index == 0,
        jnp.concatenate([keep, arrived], axis=0),
        jnp.concatenate([arrived, keep], axis=0),
    )
    return (final_out, layer_stats)


def solution(mesh):
    sizes = dict(zip(mesh.axis_names, mesh.devices.shape))
    devices = mesh.devices.reshape(
        sizes["section"], sizes["fsdp"], 2, sizes["expert"] // 2
    )
    split_mesh = jax.sharding.Mesh(devices, ("section", "fsdp", "zhalf", "inner"))
    tokens_axes = ("fsdp", "zhalf", "inner")
    experts_axes = ("zhalf", "inner")
    in_specs = (
        P(tokens_axes, None),
        P("section", None),
        P("section", None, None),
        P("section", experts_axes, "fsdp", None),
        P("section", experts_axes, "fsdp", None),
        P("section", experts_axes, None, "fsdp"),
        P("section", tokens_axes, None),
    )
    out_specs = (P(tokens_axes, "section"), P("section"))
    return jax.shard_map(
        body, mesh=split_mesh, in_specs=in_specs, out_specs=out_specs, check_vma=False
    )
```

```python
import jax
import jax.numpy as jnp
from jax import lax
from jax.sharding import PartitionSpec as P

TOP = 6
BLOCK = 64


epsilon = 1e-06


def other_section(value):
    return lax.ppermute(value, "section", [(0, 1), (1, 0)])


def ring_pairs(count, shift):
    return [(source, (source + shift) % count) for source in range(count)]


def rms_scaled(hidden_rows, gain_row):
    values = hidden_rows.astype(jnp.float32)
    scale = lax.rsqrt(jnp.mean(values * values, axis=-1, keepdims=True) + epsilon)
    return (values * scale * gain_row).astype(jnp.bfloat16)


def gate_weights(normed, router_weight, route_rows):
    logits = jnp.dot(normed, router_weight, preferred_element_type=jnp.float32)
    scores = jax.nn.sigmoid(logits)
    expert_ids = jnp.arange(router_weight.shape[1], dtype=jnp.int32)
    chosen_mask = (route_rows[:, :, None] == expert_ids[None, None, :]).astype(jnp.float32)
    chosen = jnp.sum(scores[:, None, :] * chosen_mask, axis=2)
    return chosen / jnp.sum(chosen, axis=1, keepdims=True)


def slot_positions(route_rows, experts_count, capacity):
    flat_routes = route_rows.reshape(-1)
    onehot = (flat_routes[:, None] == jnp.arange(experts_count, dtype=jnp.int32)[None, :]).astype(
        jnp.int32
    )
    count = flat_routes.shape[0]
    earlier = (jnp.arange(count)[:, None] > jnp.arange(count)[None, :]).astype(jnp.bfloat16)
    before = jnp.dot(
        earlier, onehot.astype(jnp.bfloat16), preferred_element_type=jnp.float32
    ).astype(jnp.int32)
    slot_index = jnp.sum(before * onehot, axis=1)
    return (flat_routes * capacity + slot_index).reshape(route_rows.shape)


def other_half(value):
    return lax.ppermute(value, "zhalf", [(0, 1), (1, 0)])


def half_buffer(positions, normed, slot_ids, fsdp_count, chunk):
    placing = jnp.any(positions[:, :, None] == slot_ids[None, None, :], axis=1).astype(jnp.bfloat16)
    return jnp.einsum(
        "rs,rfd->fsd",
        placing,
        normed.reshape(normed.shape[0], fsdp_count, chunk),
        preferred_element_type=jnp.float32,
    ).astype(jnp.bfloat16)


def expert_layer(entering, route_rows, partner_routes, gain_row, router_weight, weights, capacity):
    gate_w, up_w, down_w = weights
    rows, width = entering.shape
    experts_count = router_weight.shape[1]
    local_experts, chunk, hidden_units = gate_w.shape
    fsdp_count = lax.axis_size("fsdp")
    halves = lax.axis_size("zhalf")
    inner_devices = lax.axis_size("inner")
    half_index = lax.axis_index("zhalf")
    fsdp_index = lax.axis_index("fsdp")
    partner_entering = other_half(entering)
    normed = rms_scaled(entering, gain_row)
    partner_normed = rms_scaled(partner_entering, gain_row)
    mix_weights = gate_weights(normed, router_weight, route_rows)
    positions = slot_positions(route_rows, experts_count, capacity)
    partner_positions = slot_positions(partner_routes, experts_count, capacity)
    half_slots = experts_count // halves * capacity
    local_ids = half_index * half_slots + jnp.arange(half_slots, dtype=jnp.int32)
    first_half = half_index == 0
    lower_normed = jnp.where(first_half, normed, partner_normed)
    upper_normed = jnp.where(first_half, partner_normed, normed)
    lower_positions = jnp.where(first_half, positions, partner_positions)
    upper_positions = jnp.where(first_half, partner_positions, positions)
    lower_buffer = half_buffer(lower_positions, lower_normed, local_ids, fsdp_count, chunk)
    upper_buffer = half_buffer(upper_positions, upper_normed, local_ids, fsdp_count, chunk)
    group_slots = local_experts * capacity
    outgoing = jnp.stack(
        [
            lower_buffer.reshape(fsdp_count, inner_devices, group_slots, chunk),
            upper_buffer.reshape(fsdp_count, inner_devices, group_slots, chunk),
        ],
        axis=2,
    ).reshape(fsdp_count * inner_devices, halves * group_slots, chunk)
    arrived = lax.all_to_all(outgoing, ("fsdp", "inner"), 0, 0, tiled=True)
    sources = fsdp_count * inner_devices * halves
    arrived = arrived.reshape(sources, local_experts, capacity, chunk)
    arrived_blocks = arrived.reshape(fsdp_count, sources // fsdp_count, local_experts, capacity, chunk)

    def gate_and_up(rows_in):
        gate_part = jnp.einsum(
            "sjcd,jdh->sjch", rows_in, gate_w, preferred_element_type=jnp.float32
        )
        up_part = jnp.einsum("sjcd,jdh->sjch", rows_in, up_w, preferred_element_type=jnp.float32)
        return gate_part, up_part

    received = []
    for shift in range(1, fsdp_count):
        target = (fsdp_index + shift) % fsdp_count
        outgoing_pair = jnp.stack(
            gate_and_up(lax.dynamic_index_in_dim(arrived_blocks, target, 0, keepdims=False))
        ).astype(jnp.bfloat16)
        received.append(lax.ppermute(outgoing_pair, "fsdp", ring_pairs(fsdp_count, shift)))
    gate_sum, up_sum = gate_and_up(
        lax.dynamic_index_in_dim(arrived_blocks, fsdp_index, 0, keepdims=False)
    )
    for got in received:
        gate_sum = gate_sum + got[0].astype(jnp.float32)
        up_sum = up_sum + got[1].astype(jnp.float32)
    inner_act = (jax.nn.silu(gate_sum) * up_sum).astype(jnp.bfloat16)
    inner_pieces = [inner_act]
    for shift in range(1, fsdp_count):
        inner_pieces.append(lax.ppermute(inner_act, "fsdp", ring_pairs(fsdp_count, shift)))
    order = (fsdp_index - jnp.arange(fsdp_count, dtype=jnp.int32)) % fsdp_count
    inner_all = jnp.take(jnp.stack(inner_pieces), order, axis=0).reshape(
        sources, local_experts, capacity, hidden_units
    )
    inner_all = inner_all.reshape(
        fsdp_count, inner_devices, halves, local_experts, capacity, hidden_units
    )
    sending = jnp.einsum(
        "fipjch,jhd->fpijcd", inner_all, down_w, preferred_element_type=jnp.float32
    ).astype(jnp.bfloat16)
    returned = lax.all_to_all(
        sending.reshape(sources, group_slots, chunk),
        ("fsdp", "zhalf", "inner"),
        0,
        0,
        tiled=True,
    )
    slot_ids = jnp.arange(experts_count * capacity, dtype=jnp.int32)
    hits = positions[:, :, None] == slot_ids[None, None, :]
    combining = jnp.sum(jnp.where(hits, mix_weights[:, :, None], 0.0), axis=1)
    branch_sum = jnp.einsum(
        "rs,fsd->rfd",
        combining,
        returned.reshape(fsdp_count, experts_count * capacity, chunk).astype(jnp.float32),
        precision=lax.Precision.HIGHEST,
        preferred_element_type=jnp.float32,
    ).reshape(rows, width)
    return (entering.astype(jnp.float32) + branch_sum).astype(jnp.bfloat16)


def body(tokens, norm_gain, router, w_gate, w_up, w_down, routes):
    section_index = lax.axis_index("section")
    sections = lax.axis_size("section")
    token_rows, width = tokens.shape
    piece = token_rows // sections
    experts_count = router.shape[2]
    block_capacity = (7 * BLOCK * TOP + 6 * experts_count - 1) // (6 * experts_count)
    capacity = block_capacity * (piece // BLOCK)
    own_weights = (w_gate[0], w_up[0], w_down[0])
    other_weights = tuple(other_section(w) for w in own_weights)
    own_small = (norm_gain[0], router[0])
    packed = jnp.concatenate([own_small[0][:, None], own_small[1].astype(jnp.float32)], axis=1)
    other_packed = other_section(packed)
    other_small = (other_packed[:, 0], other_packed[:, 1:].astype(router.dtype))
    own_routes = routes[0]
    section_routes = other_section(own_routes)
    half_routes = other_half(own_routes)
    diagonal_routes = lax.ppermute(
        own_routes, ("section", "zhalf"), [(0, 3), (3, 0), (1, 2), (2, 1)]
    )
    hidden = lax.dynamic_slice_in_dim(tokens, section_index * piece, piece, 0)
    squares = []
    for layer in range(sections):
        mine = section_index == layer
        gain_row, router_weight = [jnp.where(mine, a, b) for a, b in zip(own_small, other_small)]
        weights = tuple(jnp.where(mine, a, b) for a, b in zip(own_weights, other_weights))
        route_all = jnp.where(mine, own_routes, section_routes)
        partner_all = jnp.where(mine, half_routes, diagonal_routes)
        route_rows = lax.dynamic_slice_in_dim(route_all, section_index * piece, piece, 0)
        partner_rows = lax.dynamic_slice_in_dim(partner_all, section_index * piece, piece, 0)
        hidden = expert_layer(
            hidden, route_rows, partner_rows, gain_row, router_weight, weights, capacity
        )
        values = hidden.astype(jnp.float32)
        squares.append(jnp.sum(values * values))
    everyone = ("section", "fsdp", "zhalf", "inner")
    expert_devices = lax.axis_size("zhalf") * lax.axis_size("inner")
    device_count = sections * lax.axis_size("fsdp") * expert_devices
    square_rows = jnp.broadcast_to(jnp.stack(squares)[None, :], (device_count, sections))
    totals = jnp.sum(lax.all_to_all(square_rows, everyone, 0, 0, tiled=True), axis=0)
    token_total = token_rows * lax.axis_size("fsdp") * expert_devices
    stats = jnp.sqrt(totals / (token_total * width))
    layer_stats = lax.dynamic_slice_in_dim(stats, section_index, 1, 0)
    half_width = width // 2
    keep = lax.dynamic_slice_in_dim(hidden, section_index * half_width, half_width, 1)
    send = lax.dynamic_slice_in_dim(hidden, (1 - section_index) * half_width, half_width, 1)
    arrived = other_section(send)
    final_out = jnp.where(
        section_index == 0,
        jnp.concatenate([keep, arrived], axis=0),
        jnp.concatenate([arrived, keep], axis=0),
    )
    return (final_out, layer_stats)


def solution(mesh):
    sizes = dict(zip(mesh.axis_names, mesh.devices.shape))
    devices = mesh.devices.reshape(
        sizes["section"], sizes["fsdp"], 2, sizes["expert"] // 2
    )
    split_mesh = jax.sharding.Mesh(devices, ("section", "fsdp", "zhalf", "inner"))
    tokens_axes = ("fsdp", "zhalf", "inner")
    experts_axes = ("zhalf", "inner")
    in_specs = (
        P(tokens_axes, None),
        P("section", None),
        P("section", None, None),
        P("section", experts_axes, "fsdp", None),
        P("section", experts_axes, "fsdp", None),
        P("section", experts_axes, None, "fsdp"),
        P("section", tokens_axes, None),
    )
    out_specs = (P(tokens_axes, "section"), P("section"))
    return jax.shard_map(
        body, mesh=split_mesh, in_specs=in_specs, out_specs=out_specs, check_vma=False
    )
```

```python
import jax
import jax.numpy as jnp
from jax import lax
from jax.sharding import PartitionSpec as P

TOP = 6
BLOCK = 64


epsilon = 1e-06


def other_section(value):
    return lax.ppermute(value, "section", [(0, 1), (1, 0)])


def ring_pairs(count, shift):
    return [(source, (source + shift) % count) for source in range(count)]


def rms_scaled(hidden_rows, gain_row):
    values = hidden_rows.astype(jnp.float32)
    scale = lax.rsqrt(jnp.mean(values * values, axis=-1, keepdims=True) + epsilon)
    return (values * scale * gain_row).astype(jnp.bfloat16)


def gate_weights(normed, router_weight, route_rows):
    logits = jnp.dot(normed, router_weight, preferred_element_type=jnp.float32)
    scores = jax.nn.sigmoid(logits)
    expert_ids = jnp.arange(router_weight.shape[1], dtype=jnp.int32)
    chosen_mask = (route_rows[:, :, None] == expert_ids[None, None, :]).astype(jnp.float32)
    chosen = jnp.sum(scores[:, None, :] * chosen_mask, axis=2)
    return chosen / jnp.sum(chosen, axis=1, keepdims=True)


def slot_positions(route_rows, experts_count, capacity):
    flat_routes = route_rows.reshape(-1)
    onehot = (flat_routes[:, None] == jnp.arange(experts_count, dtype=jnp.int32)[None, :]).astype(
        jnp.int32
    )
    count = flat_routes.shape[0]
    earlier = (jnp.arange(count)[:, None] > jnp.arange(count)[None, :]).astype(jnp.bfloat16)
    before = jnp.dot(
        earlier, onehot.astype(jnp.bfloat16), preferred_element_type=jnp.float32
    ).astype(jnp.int32)
    slot_index = jnp.sum(before * onehot, axis=1)
    return (flat_routes * capacity + slot_index).reshape(route_rows.shape)


def other_half(value):
    return lax.ppermute(value, "zhalf", [(0, 1), (1, 0)])


def half_buffer(positions, normed, slot_ids, fsdp_count, chunk):
    placing = jnp.any(positions[:, :, None] == slot_ids[None, None, :], axis=1).astype(jnp.bfloat16)
    return jnp.einsum(
        "rs,rfd->fsd",
        placing,
        normed.reshape(normed.shape[0], fsdp_count, chunk),
        preferred_element_type=jnp.float32,
    ).astype(jnp.bfloat16)


def expert_layer(entering, route_rows, partner_routes, gain_row, router_weight, weights, capacity):
    gate_w, up_w, down_w = weights
    rows, width = entering.shape
    experts_count = router_weight.shape[1]
    local_experts, chunk, hidden_units = gate_w.shape
    fsdp_count = lax.axis_size("fsdp")
    halves = lax.axis_size("zhalf")
    inner_devices = lax.axis_size("inner")
    half_index = lax.axis_index("zhalf")
    fsdp_index = lax.axis_index("fsdp")
    partner_entering = other_half(entering)
    normed = rms_scaled(entering, gain_row)
    partner_normed = rms_scaled(partner_entering, gain_row)
    mix_weights = gate_weights(normed, router_weight, route_rows)
    positions = slot_positions(route_rows, experts_count, capacity)
    partner_positions = slot_positions(partner_routes, experts_count, capacity)
    half_slots = experts_count // halves * capacity
    local_ids = half_index * half_slots + jnp.arange(half_slots, dtype=jnp.int32)
    first_half = half_index == 0
    lower_normed = jnp.where(first_half, normed, partner_normed)
    upper_normed = jnp.where(first_half, partner_normed, normed)
    lower_positions = jnp.where(first_half, positions, partner_positions)
    upper_positions = jnp.where(first_half, partner_positions, positions)
    lower_buffer = half_buffer(lower_positions, lower_normed, local_ids, fsdp_count, chunk)
    upper_buffer = half_buffer(upper_positions, upper_normed, local_ids, fsdp_count, chunk)
    group_slots = local_experts * capacity
    outgoing = jnp.stack(
        [
            lower_buffer.reshape(fsdp_count, inner_devices, group_slots, chunk),
            upper_buffer.reshape(fsdp_count, inner_devices, group_slots, chunk),
        ],
        axis=2,
    ).reshape(fsdp_count * inner_devices, halves * group_slots, chunk)
    arrived = lax.all_to_all(outgoing, ("fsdp", "inner"), 0, 0, tiled=True)
    sources = fsdp_count * inner_devices * halves
    arrived = arrived.reshape(sources, local_experts, capacity, chunk)
    arrived_blocks = arrived.reshape(fsdp_count, sources // fsdp_count, local_experts, capacity, chunk)

    def gate_and_up(rows_in):
        gate_part = jnp.einsum(
            "sjcd,jdh->sjch", rows_in, gate_w, preferred_element_type=jnp.float32
        )
        up_part = jnp.einsum("sjcd,jdh->sjch", rows_in, up_w, preferred_element_type=jnp.float32)
        return gate_part, up_part

    received = []
    for shift in range(1, fsdp_count):
        target = (fsdp_index + shift) % fsdp_count
        outgoing_pair = jnp.stack(
            gate_and_up(lax.dynamic_index_in_dim(arrived_blocks, target, 0, keepdims=False))
        ).astype(jnp.bfloat16)
        received.append(lax.ppermute(outgoing_pair, "fsdp", ring_pairs(fsdp_count, shift)))
    gate_sum, up_sum = gate_and_up(
        lax.dynamic_index_in_dim(arrived_blocks, fsdp_index, 0, keepdims=False)
    )
    for got in received:
        gate_sum = gate_sum + got[0].astype(jnp.float32)
        up_sum = up_sum + got[1].astype(jnp.float32)
    inner_act = (jax.nn.silu(gate_sum) * up_sum).astype(jnp.bfloat16)
    inner_pieces = [inner_act]
    for shift in range(1, fsdp_count):
        inner_pieces.append(lax.ppermute(inner_act, "fsdp", ring_pairs(fsdp_count, shift)))
    order = (fsdp_index - jnp.arange(fsdp_count, dtype=jnp.int32)) % fsdp_count
    inner_all = jnp.take(jnp.stack(inner_pieces), order, axis=0).reshape(
        sources, local_experts, capacity, hidden_units
    )
    inner_all = inner_all.reshape(
        fsdp_count, inner_devices, halves, local_experts, capacity, hidden_units
    )
    sending = jnp.einsum(
        "fipjch,jhd->fpijcd", inner_all, down_w, preferred_element_type=jnp.float32
    ).astype(jnp.bfloat16)
    returned = lax.all_to_all(
        sending.reshape(sources, group_slots, chunk),
        ("fsdp", "zhalf", "inner"),
        0,
        0,
        tiled=True,
    )
    slot_ids = jnp.arange(experts_count * capacity, dtype=jnp.int32)
    hits = positions[:, :, None] == slot_ids[None, None, :]
    combining = jnp.sum(jnp.where(hits, mix_weights[:, :, None], 0.0), axis=1)
    branch_sum = jnp.einsum(
        "rs,fsd->rfd",
        combining,
        returned.reshape(fsdp_count, experts_count * capacity, chunk).astype(jnp.float32),
        precision=lax.Precision.HIGHEST,
        preferred_element_type=jnp.float32,
    ).reshape(rows, width)
    return (entering.astype(jnp.float32) + branch_sum).astype(jnp.bfloat16)


def body(tokens, norm_gain, router, w_gate, w_up, w_down, routes):
    section_index = lax.axis_index("section")
    sections = lax.axis_size("section")
    token_rows, width = tokens.shape
    piece = token_rows // sections
    experts_count = router.shape[2]
    block_capacity = (7 * BLOCK * TOP + 6 * experts_count - 1) // (6 * experts_count)
    capacity = block_capacity * (piece // BLOCK)
    own_weights = (w_gate[0], w_up[0], w_down[0])
    own_small = (norm_gain[0], router[0])
    packed = jnp.concatenate([own_small[0][:, None], own_small[1].astype(jnp.float32)], axis=1)
    other_packed = other_section(packed)
    other_small = (other_packed[:, 0], other_packed[:, 1:].astype(router.dtype))
    own_routes = routes[0]
    section_routes = other_section(own_routes)
    half_routes = other_half(own_routes)
    diagonal_routes = lax.ppermute(
        own_routes, ("section", "zhalf"), [(0, 3), (3, 0), (1, 2), (2, 1)]
    )
    held = lax.optimization_barrier((own_weights, section_routes, half_routes, diagonal_routes))
    other_weights = tuple(other_section(w) for w in held[0])
    hidden = lax.dynamic_slice_in_dim(tokens, section_index * piece, piece, 0)
    squares = []
    for layer in range(sections):
        mine = section_index == layer
        gain_row, router_weight = [jnp.where(mine, a, b) for a, b in zip(own_small, other_small)]
        weights = tuple(jnp.where(mine, a, b) for a, b in zip(own_weights, other_weights))
        route_all = jnp.where(mine, own_routes, section_routes)
        partner_all = jnp.where(mine, half_routes, diagonal_routes)
        route_rows = lax.dynamic_slice_in_dim(route_all, section_index * piece, piece, 0)
        partner_rows = lax.dynamic_slice_in_dim(partner_all, section_index * piece, piece, 0)
        hidden = expert_layer(
            hidden, route_rows, partner_rows, gain_row, router_weight, weights, capacity
        )
        values = hidden.astype(jnp.float32)
        squares.append(jnp.sum(values * values))
    everyone = ("section", "fsdp", "zhalf", "inner")
    expert_devices = lax.axis_size("zhalf") * lax.axis_size("inner")
    device_count = sections * lax.axis_size("fsdp") * expert_devices
    square_rows = jnp.broadcast_to(jnp.stack(squares)[None, :], (device_count, sections))
    totals = jnp.sum(lax.all_to_all(square_rows, everyone, 0, 0, tiled=True), axis=0)
    token_total = token_rows * lax.axis_size("fsdp") * expert_devices
    stats = jnp.sqrt(totals / (token_total * width))
    layer_stats = lax.dynamic_slice_in_dim(stats, section_index, 1, 0)
    half_width = width // 2
    keep = lax.dynamic_slice_in_dim(hidden, section_index * half_width, half_width, 1)
    send = lax.dynamic_slice_in_dim(hidden, (1 - section_index) * half_width, half_width, 1)
    arrived = other_section(send)
    final_out = jnp.where(
        section_index == 0,
        jnp.concatenate([keep, arrived], axis=0),
        jnp.concatenate([arrived, keep], axis=0),
    )
    return (final_out, layer_stats)


def solution(mesh):
    sizes = dict(zip(mesh.axis_names, mesh.devices.shape))
    devices = mesh.devices.reshape(
        sizes["section"], sizes["fsdp"], 2, sizes["expert"] // 2
    )
    split_mesh = jax.sharding.Mesh(devices, ("section", "fsdp", "zhalf", "inner"))
    tokens_axes = ("fsdp", "zhalf", "inner")
    experts_axes = ("zhalf", "inner")
    in_specs = (
        P(tokens_axes, None),
        P("section", None),
        P("section", None, None),
        P("section", experts_axes, "fsdp", None),
        P("section", experts_axes, "fsdp", None),
        P("section", experts_axes, None, "fsdp"),
        P("section", tokens_axes, None),
    )
    out_specs = (P(tokens_axes, "section"), P("section"))
    return jax.shard_map(
        body, mesh=split_mesh, in_specs=in_specs, out_specs=out_specs, check_vma=False
    )
```

```python
import jax
import jax.numpy as jnp
from jax import lax
from jax.sharding import PartitionSpec as P

TOP = 6
BLOCK = 64


epsilon = 1e-06


def other_section(value):
    return lax.ppermute(value, "section", [(0, 1), (1, 0)])


def ring_pairs(count, shift):
    return [(source, (source + shift) % count) for source in range(count)]


def rms_scaled(hidden_rows, gain_row):
    values = hidden_rows.astype(jnp.float32)
    scale = lax.rsqrt(jnp.mean(values * values, axis=-1, keepdims=True) + epsilon)
    return (values * scale * gain_row).astype(jnp.bfloat16)


def gate_weights(normed, router_weight, route_rows):
    logits = jnp.dot(normed, router_weight, preferred_element_type=jnp.float32)
    scores = jax.nn.sigmoid(logits)
    expert_ids = jnp.arange(router_weight.shape[1], dtype=jnp.int32)
    chosen_mask = (route_rows[:, :, None] == expert_ids[None, None, :]).astype(jnp.float32)
    chosen = jnp.sum(scores[:, None, :] * chosen_mask, axis=2)
    return chosen / jnp.sum(chosen, axis=1, keepdims=True)


def slot_positions(route_rows, experts_count, capacity):
    flat_routes = route_rows.reshape(-1)
    onehot = (flat_routes[:, None] == jnp.arange(experts_count, dtype=jnp.int32)[None, :]).astype(
        jnp.int32
    )
    count = flat_routes.shape[0]
    earlier = (jnp.arange(count)[:, None] > jnp.arange(count)[None, :]).astype(jnp.bfloat16)
    before = jnp.dot(
        earlier, onehot.astype(jnp.bfloat16), preferred_element_type=jnp.float32
    ).astype(jnp.int32)
    slot_index = jnp.sum(before * onehot, axis=1)
    return (flat_routes * capacity + slot_index).reshape(route_rows.shape)


def other_half(value):
    return lax.ppermute(value, "zhalf", [(0, 1), (1, 0)])


def half_buffer(positions, normed, slot_ids, fsdp_count, chunk):
    placing = jnp.any(positions[:, :, None] == slot_ids[None, None, :], axis=1).astype(jnp.bfloat16)
    return jnp.einsum(
        "rs,rfd->fsd",
        placing,
        normed.reshape(normed.shape[0], fsdp_count, chunk),
        preferred_element_type=jnp.float32,
    ).astype(jnp.bfloat16)


def expert_layer(entering, route_rows, partner_routes, gain_row, router_weight, weights, capacity):
    gate_w, up_w, down_w = weights
    rows, width = entering.shape
    experts_count = router_weight.shape[1]
    local_experts, chunk, hidden_units = gate_w.shape
    fsdp_count = lax.axis_size("fsdp")
    halves = lax.axis_size("zhalf")
    inner_devices = lax.axis_size("inner")
    half_index = lax.axis_index("zhalf")
    fsdp_index = lax.axis_index("fsdp")
    partner_entering = other_half(entering)
    normed = rms_scaled(entering, gain_row)
    partner_normed = rms_scaled(partner_entering, gain_row)
    mix_weights = gate_weights(normed, router_weight, route_rows)
    positions = slot_positions(route_rows, experts_count, capacity)
    partner_positions = slot_positions(partner_routes, experts_count, capacity)
    half_slots = experts_count // halves * capacity
    local_ids = half_index * half_slots + jnp.arange(half_slots, dtype=jnp.int32)
    first_half = half_index == 0
    lower_normed = jnp.where(first_half, normed, partner_normed)
    upper_normed = jnp.where(first_half, partner_normed, normed)
    lower_positions = jnp.where(first_half, positions, partner_positions)
    upper_positions = jnp.where(first_half, partner_positions, positions)
    lower_buffer = half_buffer(lower_positions, lower_normed, local_ids, fsdp_count, chunk)
    upper_buffer = half_buffer(upper_positions, upper_normed, local_ids, fsdp_count, chunk)
    group_slots = local_experts * capacity
    outgoing = jnp.stack(
        [
            lower_buffer.reshape(fsdp_count, inner_devices, group_slots, chunk),
            upper_buffer.reshape(fsdp_count, inner_devices, group_slots, chunk),
        ],
        axis=2,
    ).reshape(fsdp_count * inner_devices, halves * group_slots, chunk)
    arrived = lax.all_to_all(outgoing, ("fsdp", "inner"), 0, 0, tiled=True)
    sources = fsdp_count * inner_devices * halves
    arrived = arrived.reshape(sources, local_experts, capacity, chunk)
    arrived_blocks = arrived.reshape(fsdp_count, sources // fsdp_count, local_experts, capacity, chunk)

    def gate_and_up(rows_in):
        gate_part = jnp.einsum(
            "sjcd,jdh->sjch", rows_in, gate_w, preferred_element_type=jnp.float32
        )
        up_part = jnp.einsum("sjcd,jdh->sjch", rows_in, up_w, preferred_element_type=jnp.float32)
        return gate_part, up_part

    received = []
    for shift in range(1, fsdp_count):
        target = (fsdp_index + shift) % fsdp_count
        outgoing_pair = jnp.stack(
            gate_and_up(lax.dynamic_index_in_dim(arrived_blocks, target, 0, keepdims=False))
        ).astype(jnp.bfloat16)
        received.append(lax.ppermute(outgoing_pair, "fsdp", ring_pairs(fsdp_count, shift)))
    gate_sum, up_sum = gate_and_up(
        lax.dynamic_index_in_dim(arrived_blocks, fsdp_index, 0, keepdims=False)
    )
    for got in received:
        gate_sum = gate_sum + got[0].astype(jnp.float32)
        up_sum = up_sum + got[1].astype(jnp.float32)
    inner_act = (jax.nn.silu(gate_sum) * up_sum).astype(jnp.bfloat16)
    inner_pieces = [inner_act]
    for shift in range(1, fsdp_count):
        inner_pieces.append(lax.ppermute(inner_act, "fsdp", ring_pairs(fsdp_count, shift)))
    order = (fsdp_index - jnp.arange(fsdp_count, dtype=jnp.int32)) % fsdp_count
    inner_all = jnp.take(jnp.stack(inner_pieces), order, axis=0).reshape(
        sources, local_experts, capacity, hidden_units
    )
    inner_all = inner_all.reshape(
        fsdp_count, inner_devices, halves, local_experts, capacity, hidden_units
    )
    sending = jnp.einsum(
        "fipjch,jhd->fpijcd", inner_all, down_w, preferred_element_type=jnp.float32
    ).astype(jnp.bfloat16)
    returned = lax.all_to_all(
        sending.reshape(sources, group_slots, chunk),
        ("fsdp", "zhalf", "inner"),
        0,
        0,
        tiled=True,
    )
    slot_ids = jnp.arange(experts_count * capacity, dtype=jnp.int32)
    hits = positions[:, :, None] == slot_ids[None, None, :]
    combining = jnp.sum(jnp.where(hits, mix_weights[:, :, None], 0.0), axis=1)
    branch_sum = jnp.einsum(
        "rs,fsd->rfd",
        combining,
        returned.reshape(fsdp_count, experts_count * capacity, chunk).astype(jnp.float32),
        precision=lax.Precision.HIGHEST,
        preferred_element_type=jnp.float32,
    ).reshape(rows, width)
    return (entering.astype(jnp.float32) + branch_sum).astype(jnp.bfloat16)


def body(tokens, norm_gain, router, w_gate, w_up, w_down, routes):
    section_index = lax.axis_index("section")
    sections = lax.axis_size("section")
    token_rows, width = tokens.shape
    piece = token_rows // sections
    experts_count = router.shape[2]
    block_capacity = (7 * BLOCK * TOP + 6 * experts_count - 1) // (6 * experts_count)
    capacity = block_capacity * (piece // BLOCK)
    own_weights = (w_gate[0], w_up[0], w_down[0])
    other_weights = tuple(other_section(w) for w in own_weights)
    own_small = (norm_gain[0], router[0])
    packed = jnp.concatenate([own_small[0][:, None], own_small[1].astype(jnp.float32)], axis=1)
    other_packed = other_section(packed)
    other_small = (other_packed[:, 0], other_packed[:, 1:].astype(router.dtype))
    own_routes = routes[0]
    section_routes = other_section(own_routes)
    half_routes = other_half(own_routes)
    diagonal_routes = lax.ppermute(
        own_routes, ("section", "zhalf"), [(0, 3), (3, 0), (1, 2), (2, 1)]
    )
    hidden = lax.dynamic_slice_in_dim(tokens, section_index * piece, piece, 0)
    squares = []
    for layer in range(sections):
        mine = section_index == layer
        gain_row, router_weight = [jnp.where(mine, a, b) for a, b in zip(own_small, other_small)]
        pairs = (own_weights, other_weights)
        if layer > 0:
            pairs = lax.optimization_barrier((own_weights, other_weights, hidden))[:2]
        weights = tuple(jnp.where(mine, a, b) for a, b in zip(*pairs))
        if layer > 0:
            weights = lax.optimization_barrier(weights)
        route_all = jnp.where(mine, own_routes, section_routes)
        partner_all = jnp.where(mine, half_routes, diagonal_routes)
        route_rows = lax.dynamic_slice_in_dim(route_all, section_index * piece, piece, 0)
        partner_rows = lax.dynamic_slice_in_dim(partner_all, section_index * piece, piece, 0)
        hidden = expert_layer(
            hidden, route_rows, partner_rows, gain_row, router_weight, weights, capacity
        )
        values = hidden.astype(jnp.float32)
        squares.append(jnp.sum(values * values))
    everyone = ("section", "fsdp", "zhalf", "inner")
    expert_devices = lax.axis_size("zhalf") * lax.axis_size("inner")
    device_count = sections * lax.axis_size("fsdp") * expert_devices
    square_rows = jnp.broadcast_to(jnp.stack(squares)[None, :], (device_count, sections))
    totals = jnp.sum(lax.all_to_all(square_rows, everyone, 0, 0, tiled=True), axis=0)
    token_total = token_rows * lax.axis_size("fsdp") * expert_devices
    stats = jnp.sqrt(totals / (token_total * width))
    layer_stats = lax.dynamic_slice_in_dim(stats, section_index, 1, 0)
    half_width = width // 2
    keep = lax.dynamic_slice_in_dim(hidden, section_index * half_width, half_width, 1)
    send = lax.dynamic_slice_in_dim(hidden, (1 - section_index) * half_width, half_width, 1)
    arrived = other_section(send)
    final_out = jnp.where(
        section_index == 0,
        jnp.concatenate([keep, arrived], axis=0),
        jnp.concatenate([arrived, keep], axis=0),
    )
    return (final_out, layer_stats)


def solution(mesh):
    sizes = dict(zip(mesh.axis_names, mesh.devices.shape))
    devices = mesh.devices.reshape(
        sizes["section"], sizes["fsdp"], 2, sizes["expert"] // 2
    )
    split_mesh = jax.sharding.Mesh(devices, ("section", "fsdp", "zhalf", "inner"))
    tokens_axes = ("fsdp", "zhalf", "inner")
    experts_axes = ("zhalf", "inner")
    in_specs = (
        P(tokens_axes, None),
        P("section", None),
        P("section", None, None),
        P("section", experts_axes, "fsdp", None),
        P("section", experts_axes, "fsdp", None),
        P("section", experts_axes, None, "fsdp"),
        P("section", tokens_axes, None),
    )
    out_specs = (P(tokens_axes, "section"), P("section"))
    return jax.shard_map(
        body, mesh=split_mesh, in_specs=in_specs, out_specs=out_specs, check_vma=False
    )
```

```python
import jax
import jax.numpy as jnp
from jax import lax
from jax.sharding import PartitionSpec as P

TOP = 6
BLOCK = 64


epsilon = 1e-06


def other_section(value):
    return lax.ppermute(value, "section", [(0, 1), (1, 0)])


def ring_pairs(count, shift):
    return [(source, (source + shift) % count) for source in range(count)]


def rms_scaled(hidden_rows, gain_row):
    values = hidden_rows.astype(jnp.float32)
    scale = lax.rsqrt(jnp.mean(values * values, axis=-1, keepdims=True) + epsilon)
    return (values * scale * gain_row).astype(jnp.bfloat16)


def gate_weights(normed, router_weight, route_rows):
    logits = jnp.dot(normed, router_weight, preferred_element_type=jnp.float32)
    scores = jax.nn.sigmoid(logits)
    expert_ids = jnp.arange(router_weight.shape[1], dtype=jnp.int32)
    chosen_mask = (route_rows[:, :, None] == expert_ids[None, None, :]).astype(jnp.float32)
    chosen = jnp.sum(scores[:, None, :] * chosen_mask, axis=2)
    return chosen / jnp.sum(chosen, axis=1, keepdims=True)


def slot_positions(route_rows, experts_count, capacity):
    flat_routes = route_rows.reshape(-1)
    onehot = (flat_routes[:, None] == jnp.arange(experts_count, dtype=jnp.int32)[None, :]).astype(
        jnp.int32
    )
    count = flat_routes.shape[0]
    earlier = (jnp.arange(count)[:, None] > jnp.arange(count)[None, :]).astype(jnp.bfloat16)
    before = jnp.dot(
        earlier, onehot.astype(jnp.bfloat16), preferred_element_type=jnp.float32
    ).astype(jnp.int32)
    slot_index = jnp.sum(before * onehot, axis=1)
    return (flat_routes * capacity + slot_index).reshape(route_rows.shape)


def other_half(value):
    return lax.ppermute(value, "zhalf", [(0, 1), (1, 0)])


def half_buffer(positions, normed, slot_ids, fsdp_count, chunk):
    placing = jnp.any(positions[:, :, None] == slot_ids[None, None, :], axis=1).astype(jnp.bfloat16)
    return jnp.einsum(
        "rs,rfd->fsd",
        placing,
        normed.reshape(normed.shape[0], fsdp_count, chunk),
        preferred_element_type=jnp.float32,
    ).astype(jnp.bfloat16)


def expert_layer(entering, route_rows, partner_routes, gain_row, router_weight, weights, capacity):
    gate_w, up_w, down_w = weights
    rows, width = entering.shape
    experts_count = router_weight.shape[1]
    local_experts, chunk, hidden_units = gate_w.shape
    fsdp_count = lax.axis_size("fsdp")
    halves = lax.axis_size("zhalf")
    inner_devices = lax.axis_size("inner")
    half_index = lax.axis_index("zhalf")
    fsdp_index = lax.axis_index("fsdp")
    partner_entering = other_half(entering)
    normed = rms_scaled(entering, gain_row)
    partner_normed = rms_scaled(partner_entering, gain_row)
    mix_weights = gate_weights(normed, router_weight, route_rows)
    positions = slot_positions(route_rows, experts_count, capacity)
    partner_positions = slot_positions(partner_routes, experts_count, capacity)
    half_slots = experts_count // halves * capacity
    local_ids = half_index * half_slots + jnp.arange(half_slots, dtype=jnp.int32)
    first_half = half_index == 0
    lower_normed = jnp.where(first_half, normed, partner_normed)
    upper_normed = jnp.where(first_half, partner_normed, normed)
    lower_positions = jnp.where(first_half, positions, partner_positions)
    upper_positions = jnp.where(first_half, partner_positions, positions)
    lower_buffer = half_buffer(lower_positions, lower_normed, local_ids, fsdp_count, chunk)
    upper_buffer = half_buffer(upper_positions, upper_normed, local_ids, fsdp_count, chunk)
    group_slots = local_experts * capacity
    outgoing = jnp.stack(
        [
            lower_buffer.reshape(fsdp_count, inner_devices, group_slots, chunk),
            upper_buffer.reshape(fsdp_count, inner_devices, group_slots, chunk),
        ],
        axis=2,
    ).reshape(fsdp_count * inner_devices, halves * group_slots, chunk)
    arrived = lax.all_to_all(outgoing, ("fsdp", "inner"), 0, 0, tiled=True)
    sources = fsdp_count * inner_devices * halves
    arrived = arrived.reshape(sources, local_experts, capacity, chunk)
    arrived_blocks = arrived.reshape(fsdp_count, sources // fsdp_count, local_experts, capacity, chunk)

    def gate_and_up(rows_in):
        gate_part = jnp.einsum(
            "sjcd,jdh->sjch", rows_in, gate_w, preferred_element_type=jnp.float32
        )
        up_part = jnp.einsum("sjcd,jdh->sjch", rows_in, up_w, preferred_element_type=jnp.float32)
        return gate_part, up_part

    received = []
    for shift in range(1, fsdp_count):
        target = (fsdp_index + shift) % fsdp_count
        outgoing_pair = jnp.stack(
            gate_and_up(lax.dynamic_index_in_dim(arrived_blocks, target, 0, keepdims=False))
        ).astype(jnp.bfloat16)
        received.append(lax.ppermute(outgoing_pair, "fsdp", ring_pairs(fsdp_count, shift)))
    gate_sum, up_sum = gate_and_up(
        lax.dynamic_index_in_dim(arrived_blocks, fsdp_index, 0, keepdims=False)
    )
    for got in received:
        gate_sum = gate_sum + got[0].astype(jnp.float32)
        up_sum = up_sum + got[1].astype(jnp.float32)
    inner_act = (jax.nn.silu(gate_sum) * up_sum).astype(jnp.bfloat16)
    inner_pieces = [inner_act]
    for shift in range(1, fsdp_count):
        inner_pieces.append(lax.ppermute(inner_act, "fsdp", ring_pairs(fsdp_count, shift)))
    order = (fsdp_index - jnp.arange(fsdp_count, dtype=jnp.int32)) % fsdp_count
    inner_all = jnp.take(jnp.stack(inner_pieces), order, axis=0).reshape(
        sources, local_experts, capacity, hidden_units
    )
    inner_all = inner_all.reshape(
        fsdp_count, inner_devices, halves, local_experts, capacity, hidden_units
    )
    sending = jnp.einsum(
        "fipjch,jhd->fpijcd", inner_all, down_w, preferred_element_type=jnp.float32
    ).astype(jnp.bfloat16)
    returned = lax.all_to_all(
        sending.reshape(sources, group_slots, chunk),
        ("fsdp", "zhalf", "inner"),
        0,
        0,
        tiled=True,
    )
    slot_ids = jnp.arange(experts_count * capacity, dtype=jnp.int32)
    hits = positions[:, :, None] == slot_ids[None, None, :]
    combining = jnp.sum(jnp.where(hits, mix_weights[:, :, None], 0.0), axis=1)
    outputs_in = returned.reshape(fsdp_count, experts_count * capacity, chunk)
    branch_sum = jnp.zeros((rows, fsdp_count, chunk), jnp.float32)
    remainder = combining
    for _ in range(3):
        term = remainder.astype(jnp.bfloat16)
        remainder = remainder - term.astype(jnp.float32)
        branch_sum = branch_sum + jnp.einsum(
            "rs,fsd->rfd", term, outputs_in, preferred_element_type=jnp.float32
        )
    branch_sum = branch_sum.reshape(rows, width)
    return (entering.astype(jnp.float32) + branch_sum).astype(jnp.bfloat16)


def body(tokens, norm_gain, router, w_gate, w_up, w_down, routes):
    section_index = lax.axis_index("section")
    sections = lax.axis_size("section")
    token_rows, width = tokens.shape
    piece = token_rows // sections
    experts_count = router.shape[2]
    block_capacity = (7 * BLOCK * TOP + 6 * experts_count - 1) // (6 * experts_count)
    capacity = block_capacity * (piece // BLOCK)
    own_weights = (w_gate[0], w_up[0], w_down[0])
    other_weights = tuple(other_section(w) for w in own_weights)
    own_small = (norm_gain[0], router[0])
    packed = jnp.concatenate([own_small[0][:, None], own_small[1].astype(jnp.float32)], axis=1)
    other_packed = other_section(packed)
    other_small = (other_packed[:, 0], other_packed[:, 1:].astype(router.dtype))
    own_routes = routes[0]
    section_routes = other_section(own_routes)
    half_routes = other_half(own_routes)
    diagonal_routes = lax.ppermute(
        own_routes, ("section", "zhalf"), [(0, 3), (3, 0), (1, 2), (2, 1)]
    )
    hidden = lax.dynamic_slice_in_dim(tokens, section_index * piece, piece, 0)
    squares = []
    for layer in range(sections):
        mine = section_index == layer
        gain_row, router_weight = [jnp.where(mine, a, b) for a, b in zip(own_small, other_small)]
        weights = tuple(jnp.where(mine, a, b) for a, b in zip(own_weights, other_weights))
        route_all = jnp.where(mine, own_routes, section_routes)
        partner_all = jnp.where(mine, half_routes, diagonal_routes)
        route_rows = lax.dynamic_slice_in_dim(route_all, section_index * piece, piece, 0)
        partner_rows = lax.dynamic_slice_in_dim(partner_all, section_index * piece, piece, 0)
        hidden = expert_layer(
            hidden, route_rows, partner_rows, gain_row, router_weight, weights, capacity
        )
        values = hidden.astype(jnp.float32)
        squares.append(jnp.sum(values * values))
    everyone = ("section", "fsdp", "zhalf", "inner")
    expert_devices = lax.axis_size("zhalf") * lax.axis_size("inner")
    device_count = sections * lax.axis_size("fsdp") * expert_devices
    square_rows = jnp.broadcast_to(jnp.stack(squares)[None, :], (device_count, sections))
    totals = jnp.sum(lax.all_to_all(square_rows, everyone, 0, 0, tiled=True), axis=0)
    token_total = token_rows * lax.axis_size("fsdp") * expert_devices
    stats = jnp.sqrt(totals / (token_total * width))
    layer_stats = lax.dynamic_slice_in_dim(stats, section_index, 1, 0)
    half_width = width // 2
    keep = lax.dynamic_slice_in_dim(hidden, section_index * half_width, half_width, 1)
    send = lax.dynamic_slice_in_dim(hidden, (1 - section_index) * half_width, half_width, 1)
    arrived = other_section(send)
    final_out = jnp.where(
        section_index == 0,
        jnp.concatenate([keep, arrived], axis=0),
        jnp.concatenate([arrived, keep], axis=0),
    )
    return (final_out, layer_stats)


def solution(mesh):
    sizes = dict(zip(mesh.axis_names, mesh.devices.shape))
    devices = mesh.devices.reshape(
        sizes["section"], sizes["fsdp"], 2, sizes["expert"] // 2
    )
    split_mesh = jax.sharding.Mesh(devices, ("section", "fsdp", "zhalf", "inner"))
    tokens_axes = ("fsdp", "zhalf", "inner")
    experts_axes = ("zhalf", "inner")
    in_specs = (
        P(tokens_axes, None),
        P("section", None),
        P("section", None, None),
        P("section", experts_axes, "fsdp", None),
        P("section", experts_axes, "fsdp", None),
        P("section", experts_axes, None, "fsdp"),
        P("section", tokens_axes, None),
    )
    out_specs = (P(tokens_axes, "section"), P("section"))
    return jax.shard_map(
        body, mesh=split_mesh, in_specs=in_specs, out_specs=out_specs, check_vma=False
    )
```

```python
import jax
import jax.numpy as jnp
from jax import lax
from jax.sharding import PartitionSpec as P

TOP = 6
BLOCK = 64


epsilon = 1e-06


def other_section(value):
    return lax.ppermute(value, "section", [(0, 1), (1, 0)])


def ring_pairs(count, shift):
    return [(source, (source + shift) % count) for source in range(count)]


def rms_scaled(hidden_rows, gain_row):
    values = hidden_rows.astype(jnp.float32)
    scale = lax.rsqrt(jnp.mean(values * values, axis=-1, keepdims=True) + epsilon)
    return (values * scale * gain_row).astype(jnp.bfloat16)


def gate_weights(normed, router_weight, route_rows):
    logits = jnp.dot(normed, router_weight, preferred_element_type=jnp.float32)
    scores = jax.nn.sigmoid(logits)
    expert_ids = jnp.arange(router_weight.shape[1], dtype=jnp.int32)
    chosen_mask = (route_rows[:, :, None] == expert_ids[None, None, :]).astype(jnp.float32)
    chosen = jnp.sum(scores[:, None, :] * chosen_mask, axis=2)
    return chosen / jnp.sum(chosen, axis=1, keepdims=True)


def slot_positions(route_rows, experts_count, capacity):
    flat_routes = route_rows.reshape(-1)
    onehot = (flat_routes[:, None] == jnp.arange(experts_count, dtype=jnp.int32)[None, :]).astype(
        jnp.int32
    )
    count = flat_routes.shape[0]
    earlier = (jnp.arange(count)[:, None] > jnp.arange(count)[None, :]).astype(jnp.bfloat16)
    before = jnp.dot(
        earlier, onehot.astype(jnp.bfloat16), preferred_element_type=jnp.float32
    ).astype(jnp.int32)
    slot_index = jnp.sum(before * onehot, axis=1)
    return (flat_routes * capacity + slot_index).reshape(route_rows.shape)


def other_half(value):
    return lax.ppermute(value, "zhalf", [(0, 1), (1, 0)])


def half_buffer(positions, normed, slot_ids, fsdp_count, chunk):
    placing = jnp.any(positions[:, :, None] == slot_ids[None, None, :], axis=1).astype(jnp.bfloat16)
    return jnp.einsum(
        "rs,rfd->fsd",
        placing,
        normed.reshape(normed.shape[0], fsdp_count, chunk),
        preferred_element_type=jnp.float32,
    ).astype(jnp.bfloat16)


def expert_layer(entering, route_rows, partner_routes, gain_row, router_weight, weights, capacity):
    gate_w, up_w, down_w = weights
    rows, width = entering.shape
    experts_count = router_weight.shape[1]
    local_experts, chunk, hidden_units = gate_w.shape
    fsdp_count = lax.axis_size("fsdp")
    halves = lax.axis_size("zhalf")
    inner_devices = lax.axis_size("inner")
    half_index = lax.axis_index("zhalf")
    fsdp_index = lax.axis_index("fsdp")
    partner_entering = other_half(entering)
    normed = rms_scaled(entering, gain_row)
    partner_normed = rms_scaled(partner_entering, gain_row)
    mix_weights = gate_weights(normed, router_weight, route_rows)
    positions = slot_positions(route_rows, experts_count, capacity)
    partner_positions = slot_positions(partner_routes, experts_count, capacity)
    half_slots = experts_count // halves * capacity
    local_ids = half_index * half_slots + jnp.arange(half_slots, dtype=jnp.int32)
    first_half = half_index == 0
    lower_normed = jnp.where(first_half, normed, partner_normed)
    upper_normed = jnp.where(first_half, partner_normed, normed)
    lower_positions = jnp.where(first_half, positions, partner_positions)
    upper_positions = jnp.where(first_half, partner_positions, positions)
    lower_buffer = half_buffer(lower_positions, lower_normed, local_ids, fsdp_count, chunk)
    upper_buffer = half_buffer(upper_positions, upper_normed, local_ids, fsdp_count, chunk)
    group_slots = local_experts * capacity
    piece_shape = (fsdp_count, inner_devices, local_experts, capacity, chunk)
    outgoing = jnp.stack(
        [lower_buffer.reshape(piece_shape), upper_buffer.reshape(piece_shape)], axis=3
    ).reshape(fsdp_count * inner_devices, local_experts, halves * capacity, chunk)
    arrived = lax.all_to_all(outgoing, ("fsdp", "inner"), 0, 2, tiled=True)
    sources = fsdp_count * inner_devices * halves
    arrived_blocks = arrived.reshape(local_experts, fsdp_count, -1, chunk)

    def gate_and_up(rows_in):
        gate_part = jnp.einsum("jrd,jdh->jrh", rows_in, gate_w, preferred_element_type=jnp.float32)
        up_part = jnp.einsum("jrd,jdh->jrh", rows_in, up_w, preferred_element_type=jnp.float32)
        return gate_part, up_part

    received = []
    for shift in range(1, fsdp_count):
        target = (fsdp_index + shift) % fsdp_count
        outgoing_pair = jnp.stack(
            gate_and_up(lax.dynamic_index_in_dim(arrived_blocks, target, 1, keepdims=False))
        ).astype(jnp.bfloat16)
        received.append(lax.ppermute(outgoing_pair, "fsdp", ring_pairs(fsdp_count, shift)))
    gate_sum, up_sum = gate_and_up(
        lax.dynamic_index_in_dim(arrived_blocks, fsdp_index, 1, keepdims=False)
    )
    for got in received:
        gate_sum = gate_sum + got[0].astype(jnp.float32)
        up_sum = up_sum + got[1].astype(jnp.float32)
    inner_act = (jax.nn.silu(gate_sum) * up_sum).astype(jnp.bfloat16)
    inner_pieces = [inner_act]
    for shift in range(1, fsdp_count):
        inner_pieces.append(lax.ppermute(inner_act, "fsdp", ring_pairs(fsdp_count, shift)))
    order = (fsdp_index - jnp.arange(fsdp_count, dtype=jnp.int32)) % fsdp_count
    inner_all = jnp.take(jnp.stack(inner_pieces), order, axis=0).reshape(
        fsdp_count, local_experts, inner_devices, halves, capacity, hidden_units
    )
    sending = jnp.einsum(
        "fjipch,jhd->fpijcd", inner_all, down_w, preferred_element_type=jnp.float32
    ).astype(jnp.bfloat16)
    returned = lax.all_to_all(
        sending.reshape(sources, group_slots, chunk),
        ("fsdp", "zhalf", "inner"),
        0,
        0,
        tiled=True,
    )
    slot_ids = jnp.arange(experts_count * capacity, dtype=jnp.int32)
    hits = positions[:, :, None] == slot_ids[None, None, :]
    combining = jnp.sum(jnp.where(hits, mix_weights[:, :, None], 0.0), axis=1)
    branch_sum = jnp.einsum(
        "rs,fsd->rfd",
        combining,
        returned.reshape(fsdp_count, experts_count * capacity, chunk).astype(jnp.float32),
        precision=lax.Precision.HIGHEST,
        preferred_element_type=jnp.float32,
    ).reshape(rows, width)
    return (entering.astype(jnp.float32) + branch_sum).astype(jnp.bfloat16)


def body(tokens, norm_gain, router, w_gate, w_up, w_down, routes):
    section_index = lax.axis_index("section")
    sections = lax.axis_size("section")
    token_rows, width = tokens.shape
    piece = token_rows // sections
    experts_count = router.shape[2]
    block_capacity = (7 * BLOCK * TOP + 6 * experts_count - 1) // (6 * experts_count)
    capacity = block_capacity * (piece // BLOCK)
    own_weights = (w_gate[0], w_up[0], w_down[0])
    other_weights = tuple(other_section(w) for w in own_weights)
    own_small = (norm_gain[0], router[0])
    packed = jnp.concatenate([own_small[0][:, None], own_small[1].astype(jnp.float32)], axis=1)
    other_packed = other_section(packed)
    other_small = (other_packed[:, 0], other_packed[:, 1:].astype(router.dtype))
    own_routes = routes[0]
    section_routes = other_section(own_routes)
    half_routes = other_half(own_routes)
    diagonal_routes = lax.ppermute(
        own_routes, ("section", "zhalf"), [(0, 3), (3, 0), (1, 2), (2, 1)]
    )
    hidden = lax.dynamic_slice_in_dim(tokens, section_index * piece, piece, 0)
    squares = []
    for layer in range(sections):
        mine = section_index == layer
        gain_row, router_weight = [jnp.where(mine, a, b) for a, b in zip(own_small, other_small)]
        weights = tuple(jnp.where(mine, a, b) for a, b in zip(own_weights, other_weights))
        route_all = jnp.where(mine, own_routes, section_routes)
        partner_all = jnp.where(mine, half_routes, diagonal_routes)
        route_rows = lax.dynamic_slice_in_dim(route_all, section_index * piece, piece, 0)
        partner_rows = lax.dynamic_slice_in_dim(partner_all, section_index * piece, piece, 0)
        hidden = expert_layer(
            hidden, route_rows, partner_rows, gain_row, router_weight, weights, capacity
        )
        values = hidden.astype(jnp.float32)
        squares.append(jnp.sum(values * values))
    everyone = ("section", "fsdp", "zhalf", "inner")
    expert_devices = lax.axis_size("zhalf") * lax.axis_size("inner")
    device_count = sections * lax.axis_size("fsdp") * expert_devices
    square_rows = jnp.broadcast_to(jnp.stack(squares)[None, :], (device_count, sections))
    totals = jnp.sum(lax.all_to_all(square_rows, everyone, 0, 0, tiled=True), axis=0)
    token_total = token_rows * lax.axis_size("fsdp") * expert_devices
    stats = jnp.sqrt(totals / (token_total * width))
    layer_stats = lax.dynamic_slice_in_dim(stats, section_index, 1, 0)
    half_width = width // 2
    keep = lax.dynamic_slice_in_dim(hidden, section_index * half_width, half_width, 1)
    send = lax.dynamic_slice_in_dim(hidden, (1 - section_index) * half_width, half_width, 1)
    arrived = other_section(send)
    final_out = jnp.where(
        section_index == 0,
        jnp.concatenate([keep, arrived], axis=0),
        jnp.concatenate([arrived, keep], axis=0),
    )
    return (final_out, layer_stats)


def solution(mesh):
    sizes = dict(zip(mesh.axis_names, mesh.devices.shape))
    devices = mesh.devices.reshape(
        sizes["section"], sizes["fsdp"], 2, sizes["expert"] // 2
    )
    split_mesh = jax.sharding.Mesh(devices, ("section", "fsdp", "zhalf", "inner"))
    tokens_axes = ("fsdp", "zhalf", "inner")
    experts_axes = ("zhalf", "inner")
    in_specs = (
        P(tokens_axes, None),
        P("section", None),
        P("section", None, None),
        P("section", experts_axes, "fsdp", None),
        P("section", experts_axes, "fsdp", None),
        P("section", experts_axes, None, "fsdp"),
        P("section", tokens_axes, None),
    )
    out_specs = (P(tokens_axes, "section"), P("section"))
    return jax.shard_map(
        body, mesh=split_mesh, in_specs=in_specs, out_specs=out_specs, check_vma=False
    )
```

```python
import jax
import jax.numpy as jnp
from jax import lax
from jax.sharding import PartitionSpec as P

TOP = 6
BLOCK = 64


epsilon = 1e-06


def other_section(value):
    return lax.ppermute(value, "section", [(0, 1), (1, 0)])


def ring_pairs(count, shift):
    return [(source, (source + shift) % count) for source in range(count)]


def rms_scaled(hidden_rows, gain_row):
    values = hidden_rows.astype(jnp.float32)
    scale = lax.rsqrt(jnp.mean(values * values, axis=-1, keepdims=True) + epsilon)
    return (values * scale * gain_row).astype(jnp.bfloat16)


def gate_weights(normed, router_weight, route_rows):
    logits = jnp.dot(normed, router_weight, preferred_element_type=jnp.float32)
    scores = jax.nn.sigmoid(logits)
    expert_ids = jnp.arange(router_weight.shape[1], dtype=jnp.int32)
    chosen_mask = (route_rows[:, :, None] == expert_ids[None, None, :]).astype(jnp.float32)
    chosen = jnp.sum(scores[:, None, :] * chosen_mask, axis=2)
    return chosen / jnp.sum(chosen, axis=1, keepdims=True)


def slot_positions(route_rows, experts_count, capacity):
    flat_routes = route_rows.reshape(-1)
    onehot = (flat_routes[:, None] == jnp.arange(experts_count, dtype=jnp.int32)[None, :]).astype(
        jnp.int32
    )
    count = flat_routes.shape[0]
    earlier = (jnp.arange(count)[:, None] > jnp.arange(count)[None, :]).astype(jnp.bfloat16)
    before = jnp.dot(
        earlier, onehot.astype(jnp.bfloat16), preferred_element_type=jnp.float32
    ).astype(jnp.int32)
    slot_index = jnp.sum(before * onehot, axis=1)
    return (flat_routes * capacity + slot_index).reshape(route_rows.shape)


def other_half(value):
    return lax.ppermute(value, "zhalf", [(0, 1), (1, 0)])


def half_buffer(positions, normed, slot_ids, fsdp_count, chunk):
    placing = jnp.any(positions[:, :, None] == slot_ids[None, None, :], axis=1).astype(jnp.bfloat16)
    return jnp.einsum(
        "rs,rfd->fsd",
        placing,
        normed.reshape(normed.shape[0], fsdp_count, chunk),
        preferred_element_type=jnp.float32,
    ).astype(jnp.bfloat16)


def expert_layer(entering, route_rows, partner_routes, gain_row, router_weight, weights, capacity):
    gate_w, up_w, down_w = weights
    rows, width = entering.shape
    experts_count = router_weight.shape[1]
    local_experts, chunk, hidden_units = gate_w.shape
    fsdp_count = lax.axis_size("fsdp")
    halves = lax.axis_size("zhalf")
    inner_devices = lax.axis_size("inner")
    half_index = lax.axis_index("zhalf")
    fsdp_index = lax.axis_index("fsdp")
    partner_entering = other_half(entering)
    normed = rms_scaled(entering, gain_row)
    partner_normed = rms_scaled(partner_entering, gain_row)
    mix_weights = gate_weights(normed, router_weight, route_rows)
    positions = slot_positions(route_rows, experts_count, capacity)
    partner_positions = slot_positions(partner_routes, experts_count, capacity)
    half_slots = experts_count // halves * capacity
    local_ids = half_index * half_slots + jnp.arange(half_slots, dtype=jnp.int32)
    first_half = half_index == 0
    lower_normed = jnp.where(first_half, normed, partner_normed)
    upper_normed = jnp.where(first_half, partner_normed, normed)
    lower_positions = jnp.where(first_half, positions, partner_positions)
    upper_positions = jnp.where(first_half, partner_positions, positions)
    lower_buffer = half_buffer(lower_positions, lower_normed, local_ids, fsdp_count, chunk)
    upper_buffer = half_buffer(upper_positions, upper_normed, local_ids, fsdp_count, chunk)
    group_slots = local_experts * capacity
    piece_shape = (fsdp_count, inner_devices, local_experts, capacity, chunk)
    outgoing = jnp.stack(
        [lower_buffer.reshape(piece_shape), upper_buffer.reshape(piece_shape)], axis=3
    ).reshape(fsdp_count * inner_devices, local_experts, halves * capacity, chunk)
    arrived = lax.all_to_all(outgoing, ("fsdp", "inner"), 0, 2, tiled=True)
    sources = fsdp_count * inner_devices * halves
    arrived_blocks = arrived.reshape(local_experts, fsdp_count, -1, chunk)

    def gate_and_up(rows_in):
        gate_part = jnp.einsum("jrd,jdh->jrh", rows_in, gate_w, preferred_element_type=jnp.float32)
        up_part = jnp.einsum("jrd,jdh->jrh", rows_in, up_w, preferred_element_type=jnp.float32)
        return gate_part, up_part

    received = []
    for shift in range(1, fsdp_count):
        target = (fsdp_index + shift) % fsdp_count
        outgoing_pair = jnp.stack(
            gate_and_up(lax.dynamic_index_in_dim(arrived_blocks, target, 1, keepdims=False))
        ).astype(jnp.bfloat16)
        received.append(lax.ppermute(outgoing_pair, "fsdp", ring_pairs(fsdp_count, shift)))
    gate_sum, up_sum = gate_and_up(
        lax.dynamic_index_in_dim(arrived_blocks, fsdp_index, 1, keepdims=False)
    )
    for got in received:
        gate_sum = gate_sum + got[0].astype(jnp.float32)
        up_sum = up_sum + got[1].astype(jnp.float32)
    inner_act = (jax.nn.silu(gate_sum) * up_sum).astype(jnp.bfloat16)
    inner_pieces = [inner_act]
    for shift in range(1, fsdp_count):
        inner_pieces.append(lax.ppermute(inner_act, "fsdp", ring_pairs(fsdp_count, shift)))
    order = (fsdp_index - jnp.arange(fsdp_count, dtype=jnp.int32)) % fsdp_count
    inner_all = jnp.take(jnp.stack(inner_pieces), order, axis=0).reshape(
        fsdp_count, local_experts, inner_devices, halves, capacity, hidden_units
    )
    sending = jnp.einsum(
        "fjipch,jhd->fpijcd", inner_all, down_w, preferred_element_type=jnp.float32
    ).astype(jnp.bfloat16)
    returned = lax.all_to_all(
        sending.reshape(sources, group_slots, chunk),
        ("fsdp", "zhalf", "inner"),
        0,
        0,
        tiled=True,
    )
    slot_ids = jnp.arange(experts_count * capacity, dtype=jnp.int32)
    hits = positions[:, :, None] == slot_ids[None, None, :]
    combining = jnp.sum(jnp.where(hits, mix_weights[:, :, None], 0.0), axis=1)
    branch_sum = jnp.einsum(
        "rs,fsd->rfd",
        combining,
        returned.reshape(fsdp_count, experts_count * capacity, chunk).astype(jnp.float32),
        precision=lax.Precision.HIGHEST,
        preferred_element_type=jnp.float32,
    ).reshape(rows, width)
    return (entering.astype(jnp.float32) + branch_sum).astype(jnp.bfloat16)


def body(tokens, norm_gain, router, w_gate, w_up, w_down, routes):
    section_index = lax.axis_index("section")
    sections = lax.axis_size("section")
    token_rows, width = tokens.shape
    piece = token_rows // sections
    experts_count = router.shape[2]
    block_capacity = (7 * BLOCK * TOP + 6 * experts_count - 1) // (6 * experts_count)
    capacity = block_capacity * (piece // BLOCK)
    own_weights = (w_gate[0], w_up[0], w_down[0])
    other_weights = tuple(other_section(w) for w in own_weights)
    own_small = (norm_gain[0], router[0])
    packed = jnp.concatenate([own_small[0][:, None], own_small[1].astype(jnp.float32)], axis=1)
    other_packed = other_section(packed)
    other_small = (other_packed[:, 0], other_packed[:, 1:].astype(router.dtype))
    own_routes = routes[0]
    section_routes = other_section(own_routes)
    half_routes = other_half(own_routes)
    diagonal_routes = lax.ppermute(
        own_routes, ("section", "zhalf"), [(0, 3), (3, 0), (1, 2), (2, 1)]
    )
    hidden = lax.dynamic_slice_in_dim(tokens, section_index * piece, piece, 0)
    def one_layer(layer, carried):
        hidden, squares = carried
        mine = section_index == layer
        gain_row, router_weight = [jnp.where(mine, a, b) for a, b in zip(own_small, other_small)]
        weights = tuple(jnp.where(mine, a, b) for a, b in zip(own_weights, other_weights))
        route_all = jnp.where(mine, own_routes, section_routes)
        partner_all = jnp.where(mine, half_routes, diagonal_routes)
        route_rows = lax.dynamic_slice_in_dim(route_all, section_index * piece, piece, 0)
        partner_rows = lax.dynamic_slice_in_dim(partner_all, section_index * piece, piece, 0)
        hidden = expert_layer(
            hidden, route_rows, partner_rows, gain_row, router_weight, weights, capacity
        )
        values = hidden.astype(jnp.float32)
        return hidden, squares.at[layer].set(jnp.sum(values * values))

    hidden, square_sums = lax.fori_loop(
        0, sections, one_layer, (hidden, jnp.zeros((sections,), jnp.float32))
    )
    everyone = ("section", "fsdp", "zhalf", "inner")
    expert_devices = lax.axis_size("zhalf") * lax.axis_size("inner")
    device_count = sections * lax.axis_size("fsdp") * expert_devices
    square_rows = jnp.broadcast_to(square_sums[None, :], (device_count, sections))
    totals = jnp.sum(lax.all_to_all(square_rows, everyone, 0, 0, tiled=True), axis=0)
    token_total = token_rows * lax.axis_size("fsdp") * expert_devices
    stats = jnp.sqrt(totals / (token_total * width))
    layer_stats = lax.dynamic_slice_in_dim(stats, section_index, 1, 0)
    half_width = width // 2
    keep = lax.dynamic_slice_in_dim(hidden, section_index * half_width, half_width, 1)
    send = lax.dynamic_slice_in_dim(hidden, (1 - section_index) * half_width, half_width, 1)
    arrived = other_section(send)
    final_out = jnp.where(
        section_index == 0,
        jnp.concatenate([keep, arrived], axis=0),
        jnp.concatenate([arrived, keep], axis=0),
    )
    return (final_out, layer_stats)


def solution(mesh):
    sizes = dict(zip(mesh.axis_names, mesh.devices.shape))
    devices = mesh.devices.reshape(
        sizes["section"], sizes["fsdp"], 2, sizes["expert"] // 2
    )
    split_mesh = jax.sharding.Mesh(devices, ("section", "fsdp", "zhalf", "inner"))
    tokens_axes = ("fsdp", "zhalf", "inner")
    experts_axes = ("zhalf", "inner")
    in_specs = (
        P(tokens_axes, None),
        P("section", None),
        P("section", None, None),
        P("section", experts_axes, "fsdp", None),
        P("section", experts_axes, "fsdp", None),
        P("section", experts_axes, None, "fsdp"),
        P("section", tokens_axes, None),
    )
    out_specs = (P(tokens_axes, "section"), P("section"))
    return jax.shard_map(
        body, mesh=split_mesh, in_specs=in_specs, out_specs=out_specs, check_vma=False
    )
```

```python
import jax
import jax.numpy as jnp
from jax import lax
from jax.sharding import PartitionSpec as P

TOP = 6
BLOCK = 64


epsilon = 1e-06


def other_section(value):
    return lax.ppermute(value, "section", [(0, 1), (1, 0)])


def ring_pairs(count, shift):
    return [(source, (source + shift) % count) for source in range(count)]


def rms_scaled(hidden_rows, gain_row):
    values = hidden_rows.astype(jnp.float32)
    scale = lax.rsqrt(jnp.mean(values * values, axis=-1, keepdims=True) + epsilon)
    return (values * scale * gain_row).astype(jnp.bfloat16)


def gate_weights(normed, router_weight, route_rows):
    logits = jnp.dot(normed, router_weight, preferred_element_type=jnp.float32)
    scores = jax.nn.sigmoid(logits)
    expert_ids = jnp.arange(router_weight.shape[1], dtype=jnp.int32)
    chosen_mask = (route_rows[:, :, None] == expert_ids[None, None, :]).astype(jnp.float32)
    chosen = jnp.sum(scores[:, None, :] * chosen_mask, axis=2)
    return chosen / jnp.sum(chosen, axis=1, keepdims=True)


def slot_positions(route_rows, experts_count, capacity):
    flat_routes = route_rows.reshape(-1)
    onehot = (flat_routes[:, None] == jnp.arange(experts_count, dtype=jnp.int32)[None, :]).astype(
        jnp.int32
    )
    count = flat_routes.shape[0]
    earlier = (jnp.arange(count)[:, None] > jnp.arange(count)[None, :]).astype(jnp.bfloat16)
    before = jnp.dot(
        earlier, onehot.astype(jnp.bfloat16), preferred_element_type=jnp.float32
    ).astype(jnp.int32)
    slot_index = jnp.sum(before * onehot, axis=1)
    return (flat_routes * capacity + slot_index).reshape(route_rows.shape)


def other_half(value):
    return lax.ppermute(value, "zhalf", [(0, 1), (1, 0)])


def half_buffer(positions, normed, slot_ids, fsdp_count, chunk):
    placing = jnp.any(positions[:, :, None] == slot_ids[None, None, :], axis=1).astype(jnp.bfloat16)
    return jnp.einsum(
        "rs,rfd->fsd",
        placing,
        normed.reshape(normed.shape[0], fsdp_count, chunk),
        preferred_element_type=jnp.float32,
    ).astype(jnp.bfloat16)


def expert_layer(entering, route_rows, partner_routes, gain_row, router_weight, weights, capacity):
    gate_w, up_w, down_w = weights
    rows, width = entering.shape
    experts_count = router_weight.shape[1]
    local_experts, chunk, hidden_units = gate_w.shape
    fsdp_count = lax.axis_size("fsdp")
    halves = lax.axis_size("zhalf")
    inner_devices = lax.axis_size("inner")
    half_index = lax.axis_index("zhalf")
    fsdp_index = lax.axis_index("fsdp")
    partner_entering = other_half(entering)
    normed = rms_scaled(entering, gain_row)
    partner_normed = rms_scaled(partner_entering, gain_row)
    mix_weights = gate_weights(normed, router_weight, route_rows)
    positions = slot_positions(route_rows, experts_count, capacity)
    partner_positions = slot_positions(partner_routes, experts_count, capacity)
    half_slots = experts_count // halves * capacity
    local_ids = half_index * half_slots + jnp.arange(half_slots, dtype=jnp.int32)
    first_half = half_index == 0
    lower_normed = jnp.where(first_half, normed, partner_normed)
    upper_normed = jnp.where(first_half, partner_normed, normed)
    lower_positions = jnp.where(first_half, positions, partner_positions)
    upper_positions = jnp.where(first_half, partner_positions, positions)
    group_slots = local_experts * capacity
    both_positions = jnp.stack([lower_positions, upper_positions])
    placing = jnp.any(
        both_positions[:, :, :, None] == local_ids[None, None, None, :], axis=2
    ).astype(jnp.bfloat16)
    placing = placing.reshape(halves, rows, inner_devices, local_experts, capacity)
    both_normed = jnp.stack([lower_normed, upper_normed]).reshape(halves, rows, fsdp_count, chunk)
    outgoing = jnp.einsum(
        "prijc,prfd->fijpcd", placing, both_normed, preferred_element_type=jnp.float32
    ).astype(jnp.bfloat16).reshape(fsdp_count * inner_devices, local_experts, halves * capacity, chunk)
    arrived = lax.all_to_all(outgoing, ("fsdp", "inner"), 0, 2, tiled=True)
    sources = fsdp_count * inner_devices * halves
    arrived_blocks = arrived.reshape(local_experts, fsdp_count, -1, chunk)

    def gate_and_up(rows_in):
        gate_part = jnp.einsum("jrd,jdh->jrh", rows_in, gate_w, preferred_element_type=jnp.float32)
        up_part = jnp.einsum("jrd,jdh->jrh", rows_in, up_w, preferred_element_type=jnp.float32)
        return gate_part, up_part

    received = []
    for shift in range(1, fsdp_count):
        target = (fsdp_index + shift) % fsdp_count
        outgoing_pair = jnp.stack(
            gate_and_up(lax.dynamic_index_in_dim(arrived_blocks, target, 1, keepdims=False))
        ).astype(jnp.bfloat16)
        received.append(lax.ppermute(outgoing_pair, "fsdp", ring_pairs(fsdp_count, shift)))
    gate_sum, up_sum = gate_and_up(
        lax.dynamic_index_in_dim(arrived_blocks, fsdp_index, 1, keepdims=False)
    )
    for got in received:
        gate_sum = gate_sum + got[0].astype(jnp.float32)
        up_sum = up_sum + got[1].astype(jnp.float32)
    inner_act = (jax.nn.silu(gate_sum) * up_sum).astype(jnp.bfloat16)
    inner_pieces = [inner_act]
    for shift in range(1, fsdp_count):
        inner_pieces.append(lax.ppermute(inner_act, "fsdp", ring_pairs(fsdp_count, shift)))
    order = (fsdp_index - jnp.arange(fsdp_count, dtype=jnp.int32)) % fsdp_count
    inner_all = jnp.take(jnp.stack(inner_pieces), order, axis=0).reshape(
        fsdp_count, local_experts, inner_devices, halves, capacity, hidden_units
    )
    sending = jnp.einsum(
        "fjipch,jhd->fpijcd", inner_all, down_w, preferred_element_type=jnp.float32
    ).astype(jnp.bfloat16)
    returned = lax.all_to_all(
        sending.reshape(sources, group_slots, chunk),
        ("fsdp", "zhalf", "inner"),
        0,
        0,
        tiled=True,
    )
    slot_ids = jnp.arange(experts_count * capacity, dtype=jnp.int32)
    hits = positions[:, :, None] == slot_ids[None, None, :]
    combining = jnp.sum(jnp.where(hits, mix_weights[:, :, None], 0.0), axis=1)
    branch_sum = jnp.einsum(
        "rs,fsd->rfd",
        combining,
        returned.reshape(fsdp_count, experts_count * capacity, chunk).astype(jnp.float32),
        precision=lax.Precision.HIGHEST,
        preferred_element_type=jnp.float32,
    ).reshape(rows, width)
    return (entering.astype(jnp.float32) + branch_sum).astype(jnp.bfloat16)


def body(tokens, norm_gain, router, w_gate, w_up, w_down, routes):
    section_index = lax.axis_index("section")
    sections = lax.axis_size("section")
    token_rows, width = tokens.shape
    piece = token_rows // sections
    experts_count = router.shape[2]
    block_capacity = (7 * BLOCK * TOP + 6 * experts_count - 1) // (6 * experts_count)
    capacity = block_capacity * (piece // BLOCK)
    own_weights = (w_gate[0], w_up[0], w_down[0])
    other_weights = tuple(other_section(w) for w in own_weights)
    own_small = (norm_gain[0], router[0])
    packed = jnp.concatenate([own_small[0][:, None], own_small[1].astype(jnp.float32)], axis=1)
    other_packed = other_section(packed)
    other_small = (other_packed[:, 0], other_packed[:, 1:].astype(router.dtype))
    own_routes = routes[0]
    section_routes = other_section(own_routes)
    half_routes = other_half(own_routes)
    diagonal_routes = lax.ppermute(
        own_routes, ("section", "zhalf"), [(0, 3), (3, 0), (1, 2), (2, 1)]
    )
    hidden = lax.dynamic_slice_in_dim(tokens, section_index * piece, piece, 0)
    squares = []
    for layer in range(sections):
        mine = section_index == layer
        gain_row, router_weight = [jnp.where(mine, a, b) for a, b in zip(own_small, other_small)]
        weights = tuple(jnp.where(mine, a, b) for a, b in zip(own_weights, other_weights))
        route_all = jnp.where(mine, own_routes, section_routes)
        partner_all = jnp.where(mine, half_routes, diagonal_routes)
        route_rows = lax.dynamic_slice_in_dim(route_all, section_index * piece, piece, 0)
        partner_rows = lax.dynamic_slice_in_dim(partner_all, section_index * piece, piece, 0)
        hidden = expert_layer(
            hidden, route_rows, partner_rows, gain_row, router_weight, weights, capacity
        )
        values = hidden.astype(jnp.float32)
        squares.append(jnp.sum(values * values))
    everyone = ("section", "fsdp", "zhalf", "inner")
    expert_devices = lax.axis_size("zhalf") * lax.axis_size("inner")
    device_count = sections * lax.axis_size("fsdp") * expert_devices
    square_rows = jnp.broadcast_to(jnp.stack(squares)[None, :], (device_count, sections))
    totals = jnp.sum(lax.all_to_all(square_rows, everyone, 0, 0, tiled=True), axis=0)
    token_total = token_rows * lax.axis_size("fsdp") * expert_devices
    stats = jnp.sqrt(totals / (token_total * width))
    layer_stats = lax.dynamic_slice_in_dim(stats, section_index, 1, 0)
    half_width = width // 2
    keep = lax.dynamic_slice_in_dim(hidden, section_index * half_width, half_width, 1)
    send = lax.dynamic_slice_in_dim(hidden, (1 - section_index) * half_width, half_width, 1)
    arrived = other_section(send)
    final_out = jnp.where(
        section_index == 0,
        jnp.concatenate([keep, arrived], axis=0),
        jnp.concatenate([arrived, keep], axis=0),
    )
    return (final_out, layer_stats)


def solution(mesh):
    sizes = dict(zip(mesh.axis_names, mesh.devices.shape))
    devices = mesh.devices.reshape(
        sizes["section"], sizes["fsdp"], 2, sizes["expert"] // 2
    )
    split_mesh = jax.sharding.Mesh(devices, ("section", "fsdp", "zhalf", "inner"))
    tokens_axes = ("fsdp", "zhalf", "inner")
    experts_axes = ("zhalf", "inner")
    in_specs = (
        P(tokens_axes, None),
        P("section", None),
        P("section", None, None),
        P("section", experts_axes, "fsdp", None),
        P("section", experts_axes, "fsdp", None),
        P("section", experts_axes, None, "fsdp"),
        P("section", tokens_axes, None),
    )
    out_specs = (P(tokens_axes, "section"), P("section"))
    return jax.shard_map(
        body, mesh=split_mesh, in_specs=in_specs, out_specs=out_specs, check_vma=False
    )
```
